32 devices in a mesh: groups: 2 (over y), sec: 4 (over z), tile: 2 (over x), sub: 2 (over core).
Axes of the slice: x: 2, y: 2, z: 4, core: 2. Of those that a mesh axis runs over, the one named last changes fastest.
Arguments:
- images: bfloat16 [8, 2048, 2048], P(('groups', 'sec'), 'sub', 'tile'), parts along dimension 0, may hold values from -8 to 8
- skipped: int32 [8, 16, 16], P(('groups', 'sec'), 'sub', 'tile'), parts along dimension 0, may hold values from 0 to 1, as said below
- patch_mask: int32 [8, 16, 16], P(('groups', 'sec'), 'sub', 'tile'), parts along dimension 0, may hold values 0 or 1
Outputs:
- flow_field: float32 [2, 8, 16, 16], P(None, ('groups', 'sec'), 'sub', 'tile'), parts along dimension 1
- positions: float32 [2, 8, 16, 16], P(None, ('groups', 'sec'), 'sub', 'tile'), parts along dimension 1
The draws below stay inside these ranges and needn't reach their ends.
There are 2 independent parts, one for each index of `groups`. The reference program is written for one: setup_inputs(seed, part) draws one part's arguments, and reference() takes and returns one part's arrays. A program takes and returns all parts, laid end to end along the dimension named above; each array names one. Nothing has to cross between parts.
Inputs may be any that keep to these rules, and one draw needn't show every extreme that they name: `skipped`: of patch columns 2k and 2k + 1 of a section and patch row, exactly one is 1.
All inputs are finite; a program needn't handle non-finite values. No bound on the sum of `patch_mask` on one device may be relied on, other than what follows from the above.
Results may differ from the reference program's by a relative error of at most 0.012.
The reference program's roundings to bfloat16 on the way count: a program that leaves them out, or rounds other values in their place, can miss the bound.
Values may be sent and summed in bfloat16 or wider, within the bound.
No kernel may reach another device: no remote copies, remote signals or barrier semaphores. Data moves between devices by JAX's collectives and lax.ppermute only.
A program may use at most 128 MiB of HBM per device.

```python
import math
import jax
import jax.numpy as jnp
from jax import lax

H = 2048
W = 2048
PATCH = 160
STRIDE = 128
RELAX = 6
RIM = 16
SECTIONS = 4
PR = 16
PC = 16


def roll_base(base, offset):
    return jnp.roll(base, (offset[0], offset[1]), axis=(0, 1))


def draw_images(key, part):
    base_key, shift_key, strength_key, noise_key = jax.random.split(jax.random.fold_in(key, 11), 4)
    base = jax.random.normal(base_key, (H, W), jnp.float32)
    shifts = jax.random.randint(shift_key, (SECTIONS, 2), -RIM, RIM + 1)
    strength = jnp.exp(jax.random.uniform(strength_key, (SECTIONS,), jnp.float32, math.log(0.35), math.log(0.6)))
    noise = jax.random.normal(noise_key, (SECTIONS, H, W), jnp.float32)
    moved = jax.vmap(roll_base, in_axes=(None, 0))(base, shifts)
    mixed = strength[:, None, None] * moved + jnp.sqrt(1.0 - strength * strength)[:, None, None] * noise
    return jnp.clip(mixed, -8.0, 8.0).astype(jnp.bfloat16)


def draw_skipped(key, part):
    first = jax.random.randint(jax.random.fold_in(key, 23), (SECTIONS, PR, PC // 2, 1), 0, 2).astype(jnp.int32)
    paired = jnp.concatenate([first, 1 - first], axis=3)
    return paired.reshape(SECTIONS, PR, PC).astype(jnp.int32)


def with_ends(entries, own_key, low, largest):
    spot = [jax.random.randint(jax.random.fold_in(own_key, axis), (), 0, length) for axis, length in enumerate(entries.shape)]
    longest = entries.shape.index(max(entries.shape))
    beside = spot[:longest] + [(spot[longest] + 1) % entries.shape[longest]] + spot[longest + 1:]
    return entries.at[tuple(spot)].set(low).at[tuple(beside)].set(largest)


def setup_inputs(seed: int = 0, part: int = 0) -> dict:
    key_of = jax.random.split(jax.random.key(seed), 4)
    own_keys = jax.random.split(jax.random.fold_in(key_of[3], part), 4)
    images = draw_images(jax.random.fold_in(jax.random.fold_in(key_of[3], part), 71), part)
    skipped = draw_skipped(jax.random.fold_in(jax.random.fold_in(key_of[3], part), 71), part)
    patch_mask = with_ends((jax.random.randint(own_keys[2], (SECTIONS, PR, PC), 0, 4) < 3).astype(jnp.int32), jax.random.fold_in(own_keys[2], 1), 0, 1)
    return dict(images=images, skipped=skipped, patch_mask=patch_mask)


SHARPNESS = 48.0
STIFFNESS = 0.25
RELAXATION = 0.8
EPSILON = 1e-05

def cut_patches(padded, stride, patch):
    count, tall, broad = padded.shape
    margin = patch - stride
    rows_count = (tall - margin) // stride
    cols_count = (broad - margin) // stride
    filled = jnp.pad(padded, ((0, 0), (0, stride - margin), (0, stride - margin)))
    upper = filled[:, :rows_count * stride].reshape(count, rows_count, stride, -1)
    lower = filled[:, stride:(rows_count + 1) * stride].reshape(count, rows_count, stride, -1)[:, :, :margin]
    banded = jnp.concatenate([upper, lower], axis=2)
    left_part = banded[..., :cols_count * stride].reshape(count, rows_count, patch, cols_count, stride)
    right_part = banded[..., stride:(cols_count + 1) * stride].reshape(count, rows_count, patch, cols_count, stride)[..., :margin]
    tiled = jnp.concatenate([left_part, right_part], axis=4)
    return jnp.transpose(tiled, (0, 1, 3, 2, 4))

def dft_tables(patch):
    index = jnp.arange(patch, dtype=jnp.int32)
    product = index[:, None] * index[None, :] % patch
    angle = product.astype(jnp.float32) * (2.0 * math.pi / patch)
    return (jnp.cos(angle).astype(jnp.bfloat16), (-jnp.sin(angle)).astype(jnp.bfloat16))

def normalize(blocks):
    values = blocks.astype(jnp.float32)
    centered = values - lax.optimization_barrier(jnp.mean(values, axis=(-2, -1), keepdims=True))
    spread = lax.optimization_barrier(jnp.mean(centered * centered, axis=(-2, -1), keepdims=True))
    return (centered * lax.rsqrt(spread + EPSILON)).astype(jnp.bfloat16)

def left_mul(table, blocks):
    return jnp.einsum('kx,nxy->nky', table.astype(jnp.float32), blocks.astype(jnp.float32), precision=lax.Precision.HIGHEST)

def right_mul(blocks, table):
    return jnp.einsum('nky,yl->nkl', blocks.astype(jnp.float32), table.astype(jnp.float32), precision=lax.Precision.HIGHEST)

def spectrum(blocks, cos_table, sin_table):
    normed = normalize(blocks)
    half_real = left_mul(cos_table, normed).astype(jnp.bfloat16)
    half_imag = left_mul(sin_table, normed).astype(jnp.bfloat16)
    real_part = right_mul(half_real, cos_table) - right_mul(half_imag, sin_table)
    imag_part = right_mul(half_real, sin_table) + right_mul(half_imag, cos_table)
    return (real_part, imag_part)

def patch_flow(own_blocks, other_blocks, rim):
    patch = own_blocks.shape[-1]
    cos_table, sin_table = dft_tables(patch)
    own_real, own_imag = spectrum(own_blocks, cos_table, sin_table)
    other_real, other_imag = spectrum(other_blocks, cos_table, sin_table)
    cross_real = (own_real * other_real + own_imag * other_imag).astype(jnp.bfloat16)
    cross_imag = (own_real * other_imag - own_imag * other_real).astype(jnp.bfloat16)
    back_real = (left_mul(cos_table, cross_real) + left_mul(sin_table, cross_imag)).astype(jnp.bfloat16)
    back_imag = (left_mul(cos_table, cross_imag) - left_mul(sin_table, cross_real)).astype(jnp.bfloat16)
    corr = (right_mul(back_real, cos_table) + right_mul(back_imag, sin_table)) / float(patch) ** 4
    weights = jnp.exp(SHARPNESS * corr)
    total = lax.optimization_barrier(jnp.sum(weights, axis=(1, 2)))
    offsets = ((jnp.arange(patch, dtype=jnp.int32) + patch // 2) % patch - patch // 2).astype(jnp.float32)
    along_rows = lax.optimization_barrier(jnp.sum(lax.optimization_barrier(jnp.sum(weights, axis=2)) * offsets, axis=1))
    along_cols = lax.optimization_barrier(jnp.sum(lax.optimization_barrier(jnp.sum(weights, axis=1)) * offsets, axis=1))
    return jnp.stack([along_rows / total, along_cols / total]) / float(rim)

def earlier(values, steps, axis):
    width = values.shape[axis]
    widths = [(0, 0)] * values.ndim
    widths[axis] = (steps, 0)
    return lax.slice_in_dim(jnp.pad(values, widths), 0, width, axis=axis)

def later(values, steps, axis):
    width = values.shape[axis]
    widths = [(0, 0)] * values.ndim
    widths[axis] = (0, steps)
    return lax.slice_in_dim(jnp.pad(values, widths), steps, steps + width, axis=axis)

def relax(flow_field, weight, distance):
    near = (distance == 1).astype(jnp.float32)
    far = 1.0 - near
    diag = STIFFNESS + weight + later(weight * near, 1, 0) + later(weight * far, 2, 0)
    positions = jnp.zeros_like(flow_field)
    for sweep in range(RELAX):
        partner = near * earlier(positions, 1, 1) + far * earlier(positions, 2, 1)
        error = weight * (positions - partner - flow_field)
        gradient = STIFFNESS * positions + error - later(error * near, 1, 1) - later(error * far, 2, 1)
        positions = positions - RELAXATION * gradient / diag
    return positions

def reference(images, skipped, patch_mask):
    sections = images.shape[0]
    order = jnp.arange(sections, dtype=jnp.int32)
    distance = jnp.where((order >= 2)[:, None, None], 1 + skipped, 1).astype(jnp.int32)
    near_src = jnp.maximum(order - 1, 0).astype(jnp.int32)
    far_src = jnp.maximum(order - 2, 0).astype(jnp.int32)
    nears = jnp.where((order >= 1)[:, None, None], images[near_src], jnp.zeros_like(images))
    fars = jnp.where((order >= 2)[:, None, None], images[far_src], jnp.zeros_like(images))

    def one_section(group):
        own, near_img, far_img, dist = group
        stacked = jnp.stack([own, near_img, far_img])
        padded = jnp.pad(stacked, ((0, 0), (RIM, RIM), (RIM, RIM)))
        blocks = cut_patches(padded, STRIDE, PATCH)
        rows_count, cols_count = (blocks.shape[1], blocks.shape[2])
        flat = blocks.reshape(3, rows_count * cols_count, PATCH, PATCH)
        choose = (dist == 1).reshape(rows_count * cols_count)
        other = jnp.where(choose[:, None, None], flat[1], flat[2])
        return patch_flow(flat[0], other, RIM).reshape(2, rows_count, cols_count)
    raw = lax.map(one_section, (images, nears, fars, distance))
    raw = jnp.transpose(raw, (1, 0, 2, 3))
    weight = patch_mask.astype(jnp.float32) * (order >= 1).astype(jnp.float32)[:, None, None]
    flow_field = raw * weight
    positions = relax(flow_field, weight, distance)
    return (flow_field, positions)
```

```python
import functools
import math

import jax
import jax.numpy as jnp
from jax import lax
from jax.experimental import pallas as pl
from jax.experimental.pallas import tpu as pltpu
from jax.sharding import PartitionSpec as P

PATCH = 160
STRIDE = 128
RELAX = 6
RIM = 16


SHARPNESS = 48.0
STIFFNESS = 0.25
RELAXATION = 0.8
EPSILON = 1e-05


def shifted(value, axis, steps):
    count = lax.axis_size(axis)
    first, last = (max(0, -steps), min(count, count - steps))
    return lax.ppermute(value, axis, [(source, source + steps) for source in range(first, last)])


def extended(block, sides, width):
    for axis, dim in sides:
        count = lax.axis_size(axis)
        forward = [(i, i + 1) for i in range(count - 1)]
        backward = [(target, source) for source, target in forward]
        low = lax.ppermute(
            lax.slice_in_dim(block, block.shape[dim] - width, None, axis=dim), axis, forward
        )
        high = lax.ppermute(lax.slice_in_dim(block, 0, width, axis=dim), axis, backward)
        block = jnp.concatenate([low, block, high], axis=dim)
    return block


def dft_tables(patch):
    index = jnp.arange(patch, dtype=jnp.int32)
    product = index[:, None] * index[None, :] % patch
    angle = product.astype(jnp.float32) * (2.0 * math.pi / patch)
    return (jnp.cos(angle).astype(jnp.bfloat16), (-jnp.sin(angle)).astype(jnp.bfloat16))


def _sum_all(x):
    return jnp.sum(jnp.sum(x, axis=1, keepdims=True), axis=0, keepdims=True)


def _flow_kernel(
    skip_ref, skip_next_ref, flag_ref, own_ref, prev_ref, next_ref, cs_ref, c_ref, s_ref, out_ref,
    *, cols,
):
    f32, bf16 = jnp.float32, jnp.bfloat16
    p = PATCH
    i = pl.program_id(0)
    cos_t = c_ref[...]
    sin_t = s_ref[...]
    both_t = cs_ref[...]
    size = float(p * p)

    def spectrum(blk):
        x = blk.astype(f32)
        centered = x - _sum_all(x) / size
        spread = _sum_all(centered * centered) / size
        normed = (centered * lax.rsqrt(spread + EPSILON)).astype(bf16)
        half = jnp.dot(both_t, normed, preferred_element_type=f32).astype(bf16)
        h_re, h_im = half[:p], half[p:]
        re = jnp.dot(h_re, cos_t, preferred_element_type=f32) - jnp.dot(
            h_im, sin_t, preferred_element_type=f32
        )
        im = jnp.dot(h_re, sin_t, preferred_element_type=f32) + jnp.dot(
            h_im, cos_t, preferred_element_type=f32
        )
        return re, im

    u_col = lax.broadcasted_iota(jnp.int32, (p, 1), 0)
    off_col = jnp.where(u_col < p // 2, u_col, u_col - p).astype(f32)
    u_row = lax.broadcasted_iota(jnp.int32, (1, p), 1)
    off_row = jnp.where(u_row < p // 2, u_row, u_row - p).astype(f32)

    def moments(own_blk, other_blk):
        o_re, o_im = spectrum(own_blk)
        t_re, t_im = spectrum(other_blk)
        c_re = (o_re * t_re + o_im * t_im).astype(bf16)
        c_im = (o_re * t_im - o_im * t_re).astype(bf16)
        a = jnp.dot(both_t, c_re, preferred_element_type=f32)
        b = jnp.dot(both_t, c_im, preferred_element_type=f32)
        b_re = (a[:p] + b[p:]).astype(bf16)
        b_im = (b[:p] - a[p:]).astype(bf16)
        corr = (
            jnp.dot(b_re, cos_t, preferred_element_type=f32)
            + jnp.dot(b_im, sin_t, preferred_element_type=f32)
        ) / float(p) ** 4
        w = jnp.exp(SHARPNESS * corr)
        total = _sum_all(w)
        rows_sum = jnp.sum(w, axis=1, keepdims=True)
        cols_sum = jnp.sum(w, axis=0, keepdims=True)
        along_rows = jnp.sum(rows_sum * off_col, axis=0, keepdims=True)
        along_cols = jnp.sum(cols_sum * off_row, axis=1, keepdims=True)
        return along_rows / total / float(RIM), along_cols / total / float(RIM)

    def window(ref, j):
        return ref[:, j * STRIDE : j * STRIDE + p]

    lane = lax.broadcasted_iota(jnp.int32, (1, 128), 1)
    acc = [jnp.zeros((1, 128), f32) for _ in range(4)]
    use_own = flag_ref[0] == 1
    for k in range(cols // 2):
        left, right = 2 * k, 2 * k + 1
        first_near = skip_ref[i * cols + left] == 0
        own_a = jnp.where(first_near, window(own_ref, left), window(own_ref, right))
        oth_a = jnp.where(first_near, window(prev_ref, left), window(prev_ref, right))
        ra, ca = moments(own_a, oth_a)
        second_far = skip_next_ref[i * cols + right] == 1
        own_b = jnp.where(second_far, window(next_ref, right), window(next_ref, left))
        col_b_prev = jnp.where(second_far, window(prev_ref, right), window(prev_ref, left))
        col_b_own = jnp.where(second_far, window(own_ref, right), window(own_ref, left))
        oth_b = jnp.where(use_own, col_b_own, col_b_prev)
        rb, cb = moments(own_b, oth_b)
        sel = lane == k
        acc = [jnp.where(sel, v, a) for v, a in zip((ra, ca, rb, cb), acc)]
    out_ref[0] = jnp.concatenate(acc + [jnp.zeros((4, 128), f32)], axis=0)


def pair_flows(own_pad, prev_pad, next_pad, skip, skip_next, use_own):
    tall, broad = own_pad.shape
    rows = (tall - (PATCH - STRIDE)) // STRIDE
    cols = (broad - (PATCH - STRIDE)) // STRIDE
    assert cols % 2 == 0 and cols // 2 <= 128
    cos_t, sin_t = dft_tables(PATCH)
    both_t = jnp.concatenate([cos_t, sin_t], axis=0)
    band = pl.BlockSpec((pl.Element(PATCH), pl.Element(broad)), lambda i, *_: (i * STRIDE, 0))
    table = pl.BlockSpec((PATCH, PATCH), lambda i, *_: (0, 0))
    grid_spec = pltpu.PrefetchScalarGridSpec(
        num_scalar_prefetch=3,
        grid=(rows,),
        in_specs=[band, band, band, pl.BlockSpec((2 * PATCH, PATCH), lambda i, *_: (0, 0)), table, table],
        out_specs=pl.BlockSpec((1, 8, 128), lambda i, *_: (i, 0, 0)),
    )
    out = pl.pallas_call(
        functools.partial(_flow_kernel, cols=cols),
        grid_spec=grid_spec,
        out_shape=jax.ShapeDtypeStruct((rows, 8, 128), jnp.float32),
        compiler_params=pltpu.CompilerParams(dimension_semantics=("arbitrary",)),
    )(
        skip.reshape(-1),
        skip_next.reshape(-1),
        use_own.reshape(1),
        own_pad,
        prev_pad,
        next_pad,
        both_t,
        cos_t,
        sin_t,
    )
    half = cols // 2
    first = jnp.repeat(jnp.transpose(out[:, 0:2, :half], (1, 0, 2)), 2, axis=2)
    second = jnp.repeat(jnp.transpose(out[:, 2:4, :half], (1, 0, 2)), 2, axis=2)
    return first, second


def gather_sections(value, axis):
    count = lax.axis_size(axis)
    spread = jnp.broadcast_to(value[None], (count,) + value.shape)
    return lax.all_to_all(spread, axis, 0, 0, tiled=True)


def earlier(values, steps, axis):
    width = values.shape[axis]
    widths = [(0, 0)] * values.ndim
    widths[axis] = (steps, 0)
    return lax.slice_in_dim(jnp.pad(values, widths), 0, width, axis=axis)


def later(values, steps, axis):
    width = values.shape[axis]
    widths = [(0, 0)] * values.ndim
    widths[axis] = (0, steps)
    return lax.slice_in_dim(jnp.pad(values, widths), steps, steps + width, axis=axis)


def relax(flow_field, weight, distance):
    near = (distance == 1).astype(jnp.float32)
    far = 1.0 - near
    diag = STIFFNESS + weight + later(weight * near, 1, 0) + later(weight * far, 2, 0)
    positions = jnp.zeros_like(flow_field)
    for sweep in range(RELAX):
        partner = near * earlier(positions, 1, 1) + far * earlier(positions, 2, 1)
        error = weight * (positions - partner - flow_field)
        gradient = (
            STIFFNESS * positions + error - later(error * near, 1, 1) - later(error * far, 2, 1)
        )
        positions = positions - RELAXATION * gradient / diag
    return positions


def body(images, skipped, patch_mask):
    index = lax.axis_index("sec")
    own_distance = jnp.where(index >= 2, 1 + skipped, 1)
    own_pad = extended(images, (("sub", 1), ("tile", 2)), RIM)
    prev_pad = shifted(own_pad, "sec", 1)
    next_pad = shifted(own_pad, "sec", -1)
    skip_next = shifted(skipped, "sec", -1)
    use_own = (index == 0).astype(jnp.int32)
    first, second = pair_flows(
        own_pad[0], prev_pad[0], next_pad[0], skipped[0], skip_next[0], use_own
    )
    first = jnp.where(skipped[0] == 0, first, 0.0)
    second = jnp.where(skip_next[0] == 1, second, 0.0)
    weight = patch_mask.astype(jnp.float32) * (index >= 1).astype(jnp.float32)
    stacked = jnp.concatenate(
        [first, second, weight, own_distance.astype(jnp.float32)], axis=0
    )
    every = jnp.moveaxis(gather_sections(stacked, "sec"), 0, 1)
    raw_all = every[0:2] + earlier(every[2:4], 1, 1)
    flow_all = raw_all * every[4]
    positions_all = relax(flow_all, every[4], every[5])
    flow_field = lax.dynamic_slice_in_dim(flow_all, index, 1, 1)
    positions = lax.dynamic_slice_in_dim(positions_all, index, 1, 1)
    return (flow_field, positions)


def solution(mesh):
    placed = (
        P(("groups", "sec"), "sub", "tile"),
        P(("groups", "sec"), "sub", "tile"),
        P(("groups", "sec"), "sub", "tile"),
    )
    return jax.shard_map(
        body,
        mesh=mesh,
        in_specs=placed,
        out_specs=(
            P(None, ("groups", "sec"), "sub", "tile"),
            P(None, ("groups", "sec"), "sub", "tile"),
        ),
        check_vma=False,
    )
```

```python
import functools
import math

import jax
import jax.numpy as jnp
from jax import lax
from jax.experimental import pallas as pl
from jax.experimental.pallas import tpu as pltpu
from jax.sharding import PartitionSpec as P

PATCH = 160
STRIDE = 128
RELAX = 6
RIM = 16


SHARPNESS = 48.0
STIFFNESS = 0.25
RELAXATION = 0.8
EPSILON = 1e-05


def shifted(value, axis, steps):
    count = lax.axis_size(axis)
    first, last = (max(0, -steps), min(count, count - steps))
    return lax.ppermute(value, axis, [(source, source + steps) for source in range(first, last)])


def extended(block, sides, width):
    for axis, dim in sides:
        count = lax.axis_size(axis)
        forward = [(i, i + 1) for i in range(count - 1)]
        backward = [(target, source) for source, target in forward]
        low = lax.ppermute(
            lax.slice_in_dim(block, block.shape[dim] - width, None, axis=dim), axis, forward
        )
        high = lax.ppermute(lax.slice_in_dim(block, 0, width, axis=dim), axis, backward)
        block = jnp.concatenate([low, block, high], axis=dim)
    return block


def dft_tables(patch):
    index = jnp.arange(patch, dtype=jnp.int32)
    product = index[:, None] * index[None, :] % patch
    angle = product.astype(jnp.float32) * (2.0 * math.pi / patch)
    return (jnp.cos(angle).astype(jnp.bfloat16), (-jnp.sin(angle)).astype(jnp.bfloat16))


def _sum_all(x):
    return jnp.sum(jnp.sum(x, axis=1, keepdims=True), axis=0, keepdims=True)


def _flow_kernel(
    skip_ref, skip_next_ref, flag_ref, own_ref, prev_ref, next_ref, cs_ref, c_ref, s_ref, out_ref,
    *, cols,
):
    f32, bf16 = jnp.float32, jnp.bfloat16
    p = PATCH
    i = pl.program_id(0)
    cos_t = c_ref[...]
    sin_t = s_ref[...]
    both_t = cs_ref[...]
    size = float(p * p)

    def spectrum(blk):
        x = blk.astype(f32)
        centered = x - _sum_all(x) / size
        spread = _sum_all(centered * centered) / size
        normed = (centered * lax.rsqrt(spread + EPSILON)).astype(bf16)
        half = jnp.dot(both_t, normed, preferred_element_type=f32).astype(bf16)
        h_re, h_im = half[:p], half[p:]
        re = jnp.dot(h_re, cos_t, preferred_element_type=f32) - jnp.dot(
            h_im, sin_t, preferred_element_type=f32
        )
        im = jnp.dot(h_re, sin_t, preferred_element_type=f32) + jnp.dot(
            h_im, cos_t, preferred_element_type=f32
        )
        return re, im

    u_col = lax.broadcasted_iota(jnp.int32, (p, 1), 0)
    off_col = jnp.where(u_col < p // 2, u_col, u_col - p).astype(f32)
    u_row = lax.broadcasted_iota(jnp.int32, (1, p), 1)
    off_row = jnp.where(u_row < p // 2, u_row, u_row - p).astype(f32)

    def moments(own_blk, other_blk):
        o_re, o_im = spectrum(own_blk)
        t_re, t_im = spectrum(other_blk)
        c_re = (o_re * t_re + o_im * t_im).astype(bf16)
        c_im = (o_re * t_im - o_im * t_re).astype(bf16)
        a = jnp.dot(both_t, c_re, preferred_element_type=f32)
        b = jnp.dot(both_t, c_im, preferred_element_type=f32)
        b_re = (a[:p] + b[p:]).astype(bf16)
        b_im = (b[:p] - a[p:]).astype(bf16)
        corr = (
            jnp.dot(b_re, cos_t, preferred_element_type=f32)
            + jnp.dot(b_im, sin_t, preferred_element_type=f32)
        ) / float(p) ** 4
        w = jnp.exp(SHARPNESS * corr)
        total = _sum_all(w)
        rows_sum = jnp.sum(w, axis=1, keepdims=True)
        cols_sum = jnp.sum(w, axis=0, keepdims=True)
        along_rows = jnp.sum(rows_sum * off_col, axis=0, keepdims=True)
        along_cols = jnp.sum(cols_sum * off_row, axis=1, keepdims=True)
        return along_rows / total / float(RIM), along_cols / total / float(RIM)

    def window(ref, j):
        return ref[:, j * STRIDE : j * STRIDE + p]

    lane = lax.broadcasted_iota(jnp.int32, (1, 128), 1)
    acc = [jnp.zeros((1, 128), f32) for _ in range(4)]
    use_own = flag_ref[0] == 1
    for k in range(cols // 2):
        left, right = 2 * k, 2 * k + 1
        first_near = skip_ref[i * cols + left] == 0
        own_a = jnp.where(first_near, window(own_ref, left), window(own_ref, right))
        oth_a = jnp.where(first_near, window(prev_ref, left), window(prev_ref, right))
        ra, ca = moments(own_a, oth_a)
        second_far = skip_next_ref[i * cols + right] == 1
        own_b = jnp.where(second_far, window(next_ref, right), window(next_ref, left))
        col_b_prev = jnp.where(second_far, window(prev_ref, right), window(prev_ref, left))
        col_b_own = jnp.where(second_far, window(own_ref, right), window(own_ref, left))
        oth_b = jnp.where(use_own, col_b_own, col_b_prev)
        rb, cb = moments(own_b, oth_b)
        sel = lane == k
        acc = [jnp.where(sel, v, a) for v, a in zip((ra, ca, rb, cb), acc)]
    out_ref[0] = jnp.concatenate(acc + [jnp.zeros((4, 128), f32)], axis=0)


def pair_flows(own_pad, prev_pad, next_pad, skip, skip_next, use_own):
    tall, broad = own_pad.shape
    rows = (tall - (PATCH - STRIDE)) // STRIDE
    cols = (broad - (PATCH - STRIDE)) // STRIDE
    assert cols % 2 == 0 and cols // 2 <= 128
    cos_t, sin_t = dft_tables(PATCH)
    both_t = jnp.concatenate([cos_t, sin_t], axis=0)
    band = pl.BlockSpec((pl.Element(PATCH), pl.Element(broad)), lambda i, *_: (i * STRIDE, 0))
    table = pl.BlockSpec((PATCH, PATCH), lambda i, *_: (0, 0))
    grid_spec = pltpu.PrefetchScalarGridSpec(
        num_scalar_prefetch=3,
        grid=(rows,),
        in_specs=[band, band, band, pl.BlockSpec((2 * PATCH, PATCH), lambda i, *_: (0, 0)), table, table],
        out_specs=pl.BlockSpec((1, 8, 128), lambda i, *_: (i, 0, 0)),
    )
    out = pl.pallas_call(
        functools.partial(_flow_kernel, cols=cols),
        grid_spec=grid_spec,
        out_shape=jax.ShapeDtypeStruct((rows, 8, 128), jnp.float32),
        compiler_params=pltpu.CompilerParams(dimension_semantics=("arbitrary",)),
    )(
        skip.reshape(-1),
        skip_next.reshape(-1),
        use_own.reshape(1),
        own_pad,
        prev_pad,
        next_pad,
        both_t,
        cos_t,
        sin_t,
    )
    half = cols // 2
    first = jnp.repeat(jnp.transpose(out[:, 0:2, :half], (1, 0, 2)), 2, axis=2)
    second = jnp.repeat(jnp.transpose(out[:, 2:4, :half], (1, 0, 2)), 2, axis=2)
    return first, second


def gather_sections(value, axis):
    count = lax.axis_size(axis)
    spread = jnp.broadcast_to(value[None], (count,) + value.shape)
    return lax.all_to_all(spread, axis, 0, 0, tiled=True)


def earlier(values, steps, axis):
    width = values.shape[axis]
    widths = [(0, 0)] * values.ndim
    widths[axis] = (steps, 0)
    return lax.slice_in_dim(jnp.pad(values, widths), 0, width, axis=axis)


def later(values, steps, axis):
    width = values.shape[axis]
    widths = [(0, 0)] * values.ndim
    widths[axis] = (0, steps)
    return lax.slice_in_dim(jnp.pad(values, widths), steps, steps + width, axis=axis)


def relax(flow_field, weight, distance):
    near = (distance == 1).astype(jnp.float32)
    far = 1.0 - near
    diag = STIFFNESS + weight + later(weight * near, 1, 0) + later(weight * far, 2, 0)
    positions = jnp.zeros_like(flow_field)
    for sweep in range(RELAX):
        partner = near * earlier(positions, 1, 1) + far * earlier(positions, 2, 1)
        error = weight * (positions - partner - flow_field)
        gradient = (
            STIFFNESS * positions + error - later(error * near, 1, 1) - later(error * far, 2, 1)
        )
        positions = positions - RELAXATION * gradient / diag
    return positions


def body(images, skipped, patch_mask):
    index = lax.axis_index("sec")
    own_distance = jnp.where(index >= 2, 1 + skipped, 1)
    own_pad = extended(images, (("sub", 1), ("tile", 2)), RIM)[0]
    skip_next = shifted(skipped, "sec", -1)
    use_own = (index == 0).astype(jnp.int32)
    rows_count = (own_pad.shape[0] - (PATCH - STRIDE)) // STRIDE
    chunks = max(n for n in (1, 2, 4) if rows_count % n == 0)
    per = rows_count // chunks
    firsts, seconds = [], []
    for c in range(chunks):
        start = c * per * STRIDE
        own_c = own_pad[start : start + per * STRIDE + PATCH - STRIDE]
        prev_c = shifted(own_c, "sec", 1)
        next_c = shifted(own_c, "sec", -1)
        part = slice(c * per, (c + 1) * per)
        first_c, second_c = pair_flows(
            own_c, prev_c, next_c, skipped[0, part], skip_next[0, part], use_own
        )
        firsts.append(first_c)
        seconds.append(second_c)
    first = jnp.concatenate(firsts, axis=1)
    second = jnp.concatenate(seconds, axis=1)
    first = jnp.where(skipped[0] == 0, first, 0.0)
    second = jnp.where(skip_next[0] == 1, second, 0.0)
    weight = patch_mask.astype(jnp.float32) * (index >= 1).astype(jnp.float32)
    stacked = jnp.concatenate(
        [first, second, weight, own_distance.astype(jnp.float32)], axis=0
    )
    every = jnp.moveaxis(gather_sections(stacked, "sec"), 0, 1)
    raw_all = every[0:2] + earlier(every[2:4], 1, 1)
    flow_all = raw_all * every[4]
    positions_all = relax(flow_all, every[4], every[5])
    flow_field = lax.dynamic_slice_in_dim(flow_all, index, 1, 1)
    positions = lax.dynamic_slice_in_dim(positions_all, index, 1, 1)
    return (flow_field, positions)


def solution(mesh):
    placed = (
        P(("groups", "sec"), "sub", "tile"),
        P(("groups", "sec"), "sub", "tile"),
        P(("groups", "sec"), "sub", "tile"),
    )
    return jax.shard_map(
        body,
        mesh=mesh,
        in_specs=placed,
        out_specs=(
            P(None, ("groups", "sec"), "sub", "tile"),
            P(None, ("groups", "sec"), "sub", "tile"),
        ),
        check_vma=False,
    )
```

```python
import functools
import math

import jax
import jax.numpy as jnp
from jax import lax
from jax.experimental import pallas as pl
from jax.experimental.pallas import tpu as pltpu
from jax.sharding import PartitionSpec as P

PATCH = 160
STRIDE = 128
RELAX = 6
RIM = 16


SHARPNESS = 48.0
STIFFNESS = 0.25
RELAXATION = 0.8
EPSILON = 1e-05


def shifted(value, axis, steps):
    count = lax.axis_size(axis)
    first, last = (max(0, -steps), min(count, count - steps))
    return lax.ppermute(value, axis, [(source, source + steps) for source in range(first, last)])


def extended(block, sides, width):
    for axis, dim in sides:
        count = lax.axis_size(axis)
        forward = [(i, i + 1) for i in range(count - 1)]
        backward = [(target, source) for source, target in forward]
        low = lax.ppermute(
            lax.slice_in_dim(block, block.shape[dim] - width, None, axis=dim), axis, forward
        )
        high = lax.ppermute(lax.slice_in_dim(block, 0, width, axis=dim), axis, backward)
        block = jnp.concatenate([low, block, high], axis=dim)
    return block


def dft_tables(patch):
    index = jnp.arange(patch, dtype=jnp.int32)
    product = index[:, None] * index[None, :] % patch
    angle = product.astype(jnp.float32) * (2.0 * math.pi / patch)
    return (jnp.cos(angle).astype(jnp.bfloat16), (-jnp.sin(angle)).astype(jnp.bfloat16))


def _sum_all(x):
    return jnp.sum(jnp.sum(x, axis=1, keepdims=True), axis=0, keepdims=True)


def _flow_kernel(
    skip_ref, skip_next_ref, flag_ref, own_ref, prev_ref, next_ref, cs_ref, c_ref, s_ref, out_ref,
    half_ref, x_ref, y_ref, br_ref, bi_ref,
    *, cols, row0,
):
    f32, bf16 = jnp.float32, jnp.bfloat16
    p = PATCH
    pairs = cols // 2
    i = pl.program_id(0) + row0
    cos_t = c_ref[...]
    sin_t = s_ref[...]
    both_t = cs_ref[...]
    size = float(p * p)

    def window(ref, j):
        return ref[:, j * STRIDE : j * STRIDE + p]

    use_own = flag_ref[0] == 1
    blocks = []
    for k in range(pairs):
        left, right = 2 * k, 2 * k + 1
        first_near = skip_ref[i * cols + left] == 0
        blocks.append(jnp.where(first_near, window(own_ref, left), window(own_ref, right)))
        blocks.append(jnp.where(first_near, window(prev_ref, left), window(prev_ref, right)))
    for k in range(pairs):
        left, right = 2 * k, 2 * k + 1
        second_far = skip_next_ref[i * cols + right] == 1
        blocks.append(jnp.where(second_far, window(next_ref, right), window(next_ref, left)))
        col_prev = jnp.where(second_far, window(prev_ref, right), window(prev_ref, left))
        col_own = jnp.where(second_far, window(own_ref, right), window(own_ref, left))
        blocks.append(jnp.where(use_own, col_own, col_prev))

    for t, blk in enumerate(blocks):
        x = blk.astype(f32)
        centered = x - _sum_all(x) / size
        spread = _sum_all(centered * centered) / size
        normed = (centered * lax.rsqrt(spread + EPSILON)).astype(bf16)
        half_ref[2 * p * t : 2 * p * (t + 1), :] = jnp.dot(
            both_t, normed, preferred_element_type=f32
        ).astype(bf16)
    halves = half_ref[...]
    x_ref[...] = jnp.dot(halves, cos_t, preferred_element_type=f32)
    y_ref[...] = jnp.dot(halves, sin_t, preferred_element_type=f32)

    def spectrum(t):
        base = 2 * p * t
        re = x_ref[base : base + p, :] - y_ref[base + p : base + 2 * p, :]
        im = y_ref[base : base + p, :] + x_ref[base + p : base + 2 * p, :]
        return re, im

    for c in range(cols):
        o_re, o_im = spectrum(2 * c)
        t_re, t_im = spectrum(2 * c + 1)
        c_re = (o_re * t_re + o_im * t_im).astype(bf16)
        c_im = (o_re * t_im - o_im * t_re).astype(bf16)
        a = jnp.dot(both_t, c_re, preferred_element_type=f32)
        b = jnp.dot(both_t, c_im, preferred_element_type=f32)
        br_ref[p * c : p * (c + 1), :] = (a[:p] + b[p:]).astype(bf16)
        bi_ref[p * c : p * (c + 1), :] = (b[:p] - a[p:]).astype(bf16)

    corr = (
        jnp.dot(br_ref[...], cos_t, preferred_element_type=f32)
        + jnp.dot(bi_ref[...], sin_t, preferred_element_type=f32)
    ) / float(p) ** 4
    w = jnp.exp(SHARPNESS * corr)
    u_col = lax.broadcasted_iota(jnp.int32, (cols * p, 1), 0) % p
    off_col = jnp.where(u_col < p // 2, u_col, u_col - p).astype(f32)
    u_row = lax.broadcasted_iota(jnp.int32, (1, p), 1)
    off_row = jnp.where(u_row < p // 2, u_row, u_row - p).astype(f32)
    rows_sum = jnp.sum(w, axis=1, keepdims=True)
    total = jnp.sum(rows_sum.reshape(cols, p, 1), axis=1)
    along_rows = jnp.sum((rows_sum * off_col).reshape(cols, p, 1), axis=1)
    cols_sum = jnp.sum(w.reshape(cols, p, p), axis=1)
    along_cols = jnp.sum(cols_sum * off_row, axis=1, keepdims=True)
    ar = along_rows / total / float(RIM)
    ac = along_cols / total / float(RIM)
    lane = lax.broadcasted_iota(jnp.int32, (cols, 128), 1)
    res = jnp.where(lane == 0, ar, jnp.where(lane == 1, ac, 0.0))
    height = out_ref.shape[1]
    if height > cols:
        res = jnp.concatenate([res, jnp.zeros((height - cols, 128), f32)], axis=0)
    out_ref[0] = res


def pair_flows(own_pad, prev_pad, next_pad, skip_flat, skip_next_flat, use_own, row0, tables):
    tall, broad = own_pad.shape
    rows = (tall - (PATCH - STRIDE)) // STRIDE
    cols = (broad - (PATCH - STRIDE)) // STRIDE
    assert cols % 2 == 0
    height = max(8, -(-cols // 8) * 8)
    both_t, cos_t, sin_t = tables
    band = pl.BlockSpec((pl.Element(PATCH), pl.Element(broad)), lambda i, *_: (i * STRIDE, 0))
    table = pl.BlockSpec((PATCH, PATCH), lambda i, *_: (0, 0))
    grid_spec = pltpu.PrefetchScalarGridSpec(
        num_scalar_prefetch=3,
        grid=(rows,),
        in_specs=[band, band, band, pl.BlockSpec((2 * PATCH, PATCH), lambda i, *_: (0, 0)), table, table],
        out_specs=pl.BlockSpec((1, height, 128), lambda i, *_: (i, 0, 0)),
        scratch_shapes=[
            pltpu.VMEM((4 * cols * PATCH, PATCH), jnp.bfloat16),
            pltpu.VMEM((4 * cols * PATCH, PATCH), jnp.float32),
            pltpu.VMEM((4 * cols * PATCH, PATCH), jnp.float32),
            pltpu.VMEM((cols * PATCH, PATCH), jnp.bfloat16),
            pltpu.VMEM((cols * PATCH, PATCH), jnp.bfloat16),
        ],
    )
    out = pl.pallas_call(
        functools.partial(_flow_kernel, cols=cols, row0=row0),
        grid_spec=grid_spec,
        out_shape=jax.ShapeDtypeStruct((rows, height, 128), jnp.float32),
        compiler_params=pltpu.CompilerParams(
            dimension_semantics=("arbitrary",), vmem_limit_bytes=48 * 1024 * 1024
        ),
    )(skip_flat, skip_next_flat, use_own.reshape(1), own_pad, prev_pad, next_pad, both_t, cos_t, sin_t)
    half = cols // 2
    first = jnp.repeat(jnp.transpose(out[:, :half, 0:2], (2, 0, 1)), 2, axis=2)
    second = jnp.repeat(jnp.transpose(out[:, half:cols, 0:2], (2, 0, 1)), 2, axis=2)
    return first, second


def gather_sections(value, axis):
    count = lax.axis_size(axis)
    spread = jnp.broadcast_to(value[None], (count,) + value.shape)
    return lax.all_to_all(spread, axis, 0, 0, tiled=True)


def earlier(values, steps, axis):
    width = values.shape[axis]
    widths = [(0, 0)] * values.ndim
    widths[axis] = (steps, 0)
    return lax.slice_in_dim(jnp.pad(values, widths), 0, width, axis=axis)


def later(values, steps, axis):
    width = values.shape[axis]
    widths = [(0, 0)] * values.ndim
    widths[axis] = (0, steps)
    return lax.slice_in_dim(jnp.pad(values, widths), steps, steps + width, axis=axis)


def relax(flow_field, weight, distance):
    near = (distance == 1).astype(jnp.float32)
    far = 1.0 - near
    diag = STIFFNESS + weight + later(weight * near, 1, 0) + later(weight * far, 2, 0)
    positions = jnp.zeros_like(flow_field)
    for sweep in range(RELAX):
        partner = near * earlier(positions, 1, 1) + far * earlier(positions, 2, 1)
        error = weight * (positions - partner - flow_field)
        gradient = (
            STIFFNESS * positions + error - later(error * near, 1, 1) - later(error * far, 2, 1)
        )
        positions = positions - RELAXATION * gradient / diag
    return positions


def body(images, skipped, patch_mask):
    index = lax.axis_index("sec")
    own_distance = jnp.where(index >= 2, 1 + skipped, 1)
    own_pad = extended(images, (("sub", 1), ("tile", 2)), RIM)[0]
    skip_next = shifted(skipped, "sec", -1)
    use_own = (index == 0).astype(jnp.int32)
    rows_count = (own_pad.shape[0] - (PATCH - STRIDE)) // STRIDE
    chunks = max(n for n in (1, 2, 4) if rows_count % n == 0)
    per = rows_count // chunks
    cos_t, sin_t = dft_tables(PATCH)
    tables = (jnp.concatenate([cos_t, sin_t], axis=0), cos_t, sin_t)
    skip_flat = skipped.reshape(-1)
    skip_next_flat = skip_next.reshape(-1)
    firsts, seconds = [], []
    for c in range(chunks):
        start = c * per * STRIDE
        own_c = own_pad[start : start + per * STRIDE + PATCH - STRIDE]
        prev_c = shifted(own_c, "sec", 1)
        next_c = shifted(own_c, "sec", -1)
        first_c, second_c = pair_flows(
            own_c, prev_c, next_c, skip_flat, skip_next_flat, use_own, c * per, tables
        )
        firsts.append(first_c)
        seconds.append(second_c)
    first = jnp.concatenate(firsts, axis=1)
    second = jnp.concatenate(seconds, axis=1)
    first = jnp.where(skipped[0] == 0, first, 0.0)
    second = jnp.where(skip_next[0] == 1, second, 0.0)
    weight = patch_mask.astype(jnp.float32) * (index >= 1).astype(jnp.float32)
    stacked = jnp.concatenate(
        [first, second, weight, own_distance.astype(jnp.float32)], axis=0
    )
    every = jnp.moveaxis(gather_sections(stacked, "sec"), 0, 1)
    raw_all = every[0:2] + earlier(every[2:4], 1, 1)
    flow_all = raw_all * every[4]
    positions_all = relax(flow_all, every[4], every[5])
    flow_field = lax.dynamic_slice_in_dim(flow_all, index, 1, 1)
    positions = lax.dynamic_slice_in_dim(positions_all, index, 1, 1)
    return (flow_field, positions)


def solution(mesh):
    placed = (
        P(("groups", "sec"), "sub", "tile"),
        P(("groups", "sec"), "sub", "tile"),
        P(("groups", "sec"), "sub", "tile"),
    )
    return jax.shard_map(
        body,
        mesh=mesh,
        in_specs=placed,
        out_specs=(
            P(None, ("groups", "sec"), "sub", "tile"),
            P(None, ("groups", "sec"), "sub", "tile"),
        ),
        check_vma=False,
    )
```

```python
import functools
import math

import jax
import jax.numpy as jnp
from jax import lax
from jax.experimental import pallas as pl
from jax.experimental.pallas import tpu as pltpu
from jax.sharding import PartitionSpec as P

PATCH = 160
STRIDE = 128
RELAX = 6
RIM = 16


SHARPNESS = 48.0
STIFFNESS = 0.25
RELAXATION = 0.8
EPSILON = 1e-05


def shifted(value, axis, steps):
    count = lax.axis_size(axis)
    first, last = (max(0, -steps), min(count, count - steps))
    return lax.ppermute(value, axis, [(source, source + steps) for source in range(first, last)])


def _strip_send(strip, dim):
    return jnp.swapaxes(strip, 1, 2) if dim == 2 else strip


def _strip_recv(strip, dim):
    return jnp.swapaxes(strip, 1, 2) if dim == 2 else strip


def extended(block, sides, width):
    for axis, dim in sides:
        count = lax.axis_size(axis)
        top = lax.slice_in_dim(block, 0, width, axis=dim)
        bottom = lax.slice_in_dim(block, block.shape[dim] - width, None, axis=dim)
        if count == 2:
            index = lax.axis_index(axis)
            send = _strip_send(jnp.where(index == 0, bottom, top), dim)
            got = _strip_recv(lax.ppermute(send, axis, [(0, 1), (1, 0)]), dim)
            low = jnp.where(index == 1, got, jnp.zeros_like(got))
            high = jnp.where(index == 0, got, jnp.zeros_like(got))
        else:
            forward = [(i, i + 1) for i in range(count - 1)]
            backward = [(target, source) for source, target in forward]
            low = _strip_recv(lax.ppermute(_strip_send(bottom, dim), axis, forward), dim)
            high = _strip_recv(lax.ppermute(_strip_send(top, dim), axis, backward), dim)
        block = jnp.concatenate([low, block, high], axis=dim)
    return block


def dft_tables(patch):
    index = jnp.arange(patch, dtype=jnp.int32)
    product = index[:, None] * index[None, :] % patch
    angle = product.astype(jnp.float32) * (2.0 * math.pi / patch)
    return (jnp.cos(angle).astype(jnp.bfloat16), (-jnp.sin(angle)).astype(jnp.bfloat16))


def _sum_all(x):
    return jnp.sum(jnp.sum(x, axis=1, keepdims=True), axis=0, keepdims=True)


def _flow_kernel(
    skip_ref, skip_next_ref, flag_ref, own_ref, prev_ref, next_ref, cs_ref, c_ref, s_ref, out_ref,
    half_ref, x_ref, y_ref, br_ref, bi_ref,
    *, cols, row0,
):
    f32, bf16 = jnp.float32, jnp.bfloat16
    p = PATCH
    pairs = cols // 2
    i = pl.program_id(0) + row0
    cos_t = c_ref[...]
    sin_t = s_ref[...]
    both_t = cs_ref[...]
    size = float(p * p)

    def window(ref, j):
        return ref[:, j * STRIDE : j * STRIDE + p]

    use_own = flag_ref[0] == 1
    blocks = []
    for k in range(pairs):
        left, right = 2 * k, 2 * k + 1
        first_near = skip_ref[i * cols + left] == 0
        blocks.append(jnp.where(first_near, window(own_ref, left), window(own_ref, right)))
        blocks.append(jnp.where(first_near, window(prev_ref, left), window(prev_ref, right)))
    for k in range(pairs):
        left, right = 2 * k, 2 * k + 1
        second_far = skip_next_ref[i * cols + right] == 1
        blocks.append(jnp.where(second_far, window(next_ref, right), window(next_ref, left)))
        col_prev = jnp.where(second_far, window(prev_ref, right), window(prev_ref, left))
        col_own = jnp.where(second_far, window(own_ref, right), window(own_ref, left))
        blocks.append(jnp.where(use_own, col_own, col_prev))

    for t, blk in enumerate(blocks):
        x = blk.astype(f32)
        centered = x - _sum_all(x) / size
        spread = _sum_all(centered * centered) / size
        normed = (centered * lax.rsqrt(spread + EPSILON)).astype(bf16)
        half_ref[2 * p * t : 2 * p * (t + 1), :] = jnp.dot(
            both_t, normed, preferred_element_type=f32
        ).astype(bf16)
    halves = half_ref[...]
    x_ref[...] = jnp.dot(halves, cos_t, preferred_element_type=f32)
    y_ref[...] = jnp.dot(halves, sin_t, preferred_element_type=f32)

    def spectrum(t):
        base = 2 * p * t
        re = x_ref[base : base + p, :] - y_ref[base + p : base + 2 * p, :]
        im = y_ref[base : base + p, :] + x_ref[base + p : base + 2 * p, :]
        return re, im

    for c in range(cols):
        o_re, o_im = spectrum(2 * c)
        t_re, t_im = spectrum(2 * c + 1)
        c_re = (o_re * t_re + o_im * t_im).astype(bf16)
        c_im = (o_re * t_im - o_im * t_re).astype(bf16)
        a = jnp.dot(both_t, c_re, preferred_element_type=f32)
        b = jnp.dot(both_t, c_im, preferred_element_type=f32)
        br_ref[p * c : p * (c + 1), :] = (a[:p] + b[p:]).astype(bf16)
        bi_ref[p * c : p * (c + 1), :] = (b[:p] - a[p:]).astype(bf16)

    corr = (
        jnp.dot(br_ref[...], cos_t, preferred_element_type=f32)
        + jnp.dot(bi_ref[...], sin_t, preferred_element_type=f32)
    ) / float(p) ** 4
    w = jnp.exp(SHARPNESS * corr)
    u_col = lax.broadcasted_iota(jnp.int32, (cols * p, 1), 0) % p
    off_col = jnp.where(u_col < p // 2, u_col, u_col - p).astype(f32)
    u_row = lax.broadcasted_iota(jnp.int32, (1, p), 1)
    off_row = jnp.where(u_row < p // 2, u_row, u_row - p).astype(f32)
    rows_sum = jnp.sum(w, axis=1, keepdims=True)
    total = jnp.sum(rows_sum.reshape(cols, p, 1), axis=1)
    along_rows = jnp.sum((rows_sum * off_col).reshape(cols, p, 1), axis=1)
    cols_sum = jnp.sum(w.reshape(cols, p, p), axis=1)
    along_cols = jnp.sum(cols_sum * off_row, axis=1, keepdims=True)
    ar = along_rows / total / float(RIM)
    ac = along_cols / total / float(RIM)
    lane = lax.broadcasted_iota(jnp.int32, (cols, 128), 1)
    res = jnp.where(lane == 0, ar, jnp.where(lane == 1, ac, 0.0))
    height = out_ref.shape[1]
    if height > cols:
        res = jnp.concatenate([res, jnp.zeros((height - cols, 128), f32)], axis=0)
    out_ref[0] = res


def pair_flows(own_pad, prev_pad, next_pad, skip_flat, skip_next_flat, use_own, row0, tables):
    tall, broad = own_pad.shape
    rows = (tall - (PATCH - STRIDE)) // STRIDE
    cols = (broad - (PATCH - STRIDE)) // STRIDE
    assert cols % 2 == 0
    height = max(8, -(-cols // 8) * 8)
    both_t, cos_t, sin_t = tables
    band = pl.BlockSpec((pl.Element(PATCH), pl.Element(broad)), lambda i, *_: (i * STRIDE, 0))
    table = pl.BlockSpec((PATCH, PATCH), lambda i, *_: (0, 0))
    grid_spec = pltpu.PrefetchScalarGridSpec(
        num_scalar_prefetch=3,
        grid=(rows,),
        in_specs=[band, band, band, pl.BlockSpec((2 * PATCH, PATCH), lambda i, *_: (0, 0)), table, table],
        out_specs=pl.BlockSpec((1, height, 128), lambda i, *_: (i, 0, 0)),
        scratch_shapes=[
            pltpu.VMEM((4 * cols * PATCH, PATCH), jnp.bfloat16),
            pltpu.VMEM((4 * cols * PATCH, PATCH), jnp.float32),
            pltpu.VMEM((4 * cols * PATCH, PATCH), jnp.float32),
            pltpu.VMEM((cols * PATCH, PATCH), jnp.bfloat16),
            pltpu.VMEM((cols * PATCH, PATCH), jnp.bfloat16),
        ],
    )
    out = pl.pallas_call(
        functools.partial(_flow_kernel, cols=cols, row0=row0),
        grid_spec=grid_spec,
        out_shape=jax.ShapeDtypeStruct((rows, height, 128), jnp.float32),
        compiler_params=pltpu.CompilerParams(
            dimension_semantics=("arbitrary",), vmem_limit_bytes=48 * 1024 * 1024
        ),
    )(skip_flat, skip_next_flat, use_own.reshape(1), own_pad, prev_pad, next_pad, both_t, cos_t, sin_t)
    half = cols // 2
    first = jnp.repeat(jnp.transpose(out[:, :half, 0:2], (2, 0, 1)), 2, axis=2)
    second = jnp.repeat(jnp.transpose(out[:, half:cols, 0:2], (2, 0, 1)), 2, axis=2)
    return first, second


def gather_sections(value, axis):
    count = lax.axis_size(axis)
    spread = jnp.broadcast_to(value[None], (count,) + value.shape)
    return lax.all_to_all(spread, axis, 0, 0, tiled=True)


def earlier(values, steps, axis):
    width = values.shape[axis]
    widths = [(0, 0)] * values.ndim
    widths[axis] = (steps, 0)
    return lax.slice_in_dim(jnp.pad(values, widths), 0, width, axis=axis)


def later(values, steps, axis):
    width = values.shape[axis]
    widths = [(0, 0)] * values.ndim
    widths[axis] = (0, steps)
    return lax.slice_in_dim(jnp.pad(values, widths), steps, steps + width, axis=axis)


def relax(flow_field, weight, distance):
    near = (distance == 1).astype(jnp.float32)
    far = 1.0 - near
    diag = STIFFNESS + weight + later(weight * near, 1, 0) + later(weight * far, 2, 0)
    positions = jnp.zeros_like(flow_field)
    for sweep in range(RELAX):
        partner = near * earlier(positions, 1, 1) + far * earlier(positions, 2, 1)
        error = weight * (positions - partner - flow_field)
        gradient = (
            STIFFNESS * positions + error - later(error * near, 1, 1) - later(error * far, 2, 1)
        )
        positions = positions - RELAXATION * gradient / diag
    return positions


def body(images, skipped, patch_mask):
    index = lax.axis_index("sec")
    own_distance = jnp.where(index >= 2, 1 + skipped, 1)
    own_pad = extended(images, (("sub", 1), ("tile", 2)), RIM)[0]
    skip_next = shifted(skipped, "sec", -1)
    use_own = (index == 0).astype(jnp.int32)
    rows_count = (own_pad.shape[0] - (PATCH - STRIDE)) // STRIDE
    chunks = max(n for n in (1, 2, 4) if rows_count % n == 0)
    per = rows_count // chunks
    cos_t, sin_t = dft_tables(PATCH)
    tables = (jnp.concatenate([cos_t, sin_t], axis=0), cos_t, sin_t)
    skip_flat = skipped.reshape(-1)
    skip_next_flat = skip_next.reshape(-1)
    firsts, seconds = [], []
    for c in range(chunks):
        start = c * per * STRIDE
        own_c = own_pad[start : start + per * STRIDE + PATCH - STRIDE]
        prev_c = shifted(own_c, "sec", 1)
        next_c = shifted(own_c, "sec", -1)
        first_c, second_c = pair_flows(
            own_c, prev_c, next_c, skip_flat, skip_next_flat, use_own, c * per, tables
        )
        firsts.append(first_c)
        seconds.append(second_c)
    first = jnp.concatenate(firsts, axis=1)
    second = jnp.concatenate(seconds, axis=1)
    first = jnp.where(skipped[0] == 0, first, 0.0)
    second = jnp.where(skip_next[0] == 1, second, 0.0)
    weight = patch_mask.astype(jnp.float32) * (index >= 1).astype(jnp.float32)
    stacked = jnp.concatenate(
        [first, second, weight, own_distance.astype(jnp.float32)], axis=0
    )
    every = jnp.moveaxis(gather_sections(stacked, "sec"), 0, 1)
    raw_all = every[0:2] + earlier(every[2:4], 1, 1)
    flow_all = raw_all * every[4]
    positions_all = relax(flow_all, every[4], every[5])
    flow_field = lax.dynamic_slice_in_dim(flow_all, index, 1, 1)
    positions = lax.dynamic_slice_in_dim(positions_all, index, 1, 1)
    return (flow_field, positions)


def solution(mesh):
    placed = (
        P(("groups", "sec"), "sub", "tile"),
        P(("groups", "sec"), "sub", "tile"),
        P(("groups", "sec"), "sub", "tile"),
    )
    return jax.shard_map(
        body,
        mesh=mesh,
        in_specs=placed,
        out_specs=(
            P(None, ("groups", "sec"), "sub", "tile"),
            P(None, ("groups", "sec"), "sub", "tile"),
        ),
        check_vma=False,
    )
```

```python
import functools
import math

import jax
import jax.numpy as jnp
from jax import lax
from jax.experimental import pallas as pl
from jax.experimental.pallas import tpu as pltpu
from jax.sharding import PartitionSpec as P

PATCH = 160
STRIDE = 128
RELAX = 6
RIM = 16


SHARPNESS = 48.0
STIFFNESS = 0.25
RELAXATION = 0.8
EPSILON = 1e-05


def shifted(value, axis, steps):
    count = lax.axis_size(axis)
    first, last = (max(0, -steps), min(count, count - steps))
    return lax.ppermute(value, axis, [(source, source + steps) for source in range(first, last)])


def _strip_send(strip, dim):
    return jnp.swapaxes(strip, 1, 2) if dim == 2 else strip


def _strip_recv(strip, dim):
    return jnp.swapaxes(strip, 1, 2) if dim == 2 else strip


def extended(block, sides, width):
    for axis, dim in sides:
        count = lax.axis_size(axis)
        top = lax.slice_in_dim(block, 0, width, axis=dim)
        bottom = lax.slice_in_dim(block, block.shape[dim] - width, None, axis=dim)
        if count == 2:
            index = lax.axis_index(axis)
            send = _strip_send(jnp.where(index == 0, bottom, top), dim)
            got = _strip_recv(lax.ppermute(send, axis, [(0, 1), (1, 0)]), dim)
            low = jnp.where(index == 1, got, jnp.zeros_like(got))
            high = jnp.where(index == 0, got, jnp.zeros_like(got))
        else:
            forward = [(i, i + 1) for i in range(count - 1)]
            backward = [(target, source) for source, target in forward]
            low = _strip_recv(lax.ppermute(_strip_send(bottom, dim), axis, forward), dim)
            high = _strip_recv(lax.ppermute(_strip_send(top, dim), axis, backward), dim)
        block = jnp.concatenate([low, block, high], axis=dim)
    return block


def dft_tables(patch):
    index = jnp.arange(patch, dtype=jnp.int32)
    product = index[:, None] * index[None, :] % patch
    angle = product.astype(jnp.float32) * (2.0 * math.pi / patch)
    return (jnp.cos(angle).astype(jnp.bfloat16), (-jnp.sin(angle)).astype(jnp.bfloat16))


def _sum_all(x):
    return jnp.sum(jnp.sum(x, axis=1, keepdims=True), axis=0, keepdims=True)


def _flow_kernel(
    skip_ref, skip_next_ref, flag_ref, own_ref, prev_ref, next_ref, cs_ref, c_ref, s_ref, out_ref,
    half_ref, x_ref, y_ref, br_ref, bi_ref,
    *, cols, row0,
):
    f32, bf16 = jnp.float32, jnp.bfloat16
    p = PATCH
    pairs = cols // 2
    i = pl.program_id(0) + row0
    cos_t = c_ref[...]
    sin_t = s_ref[...]
    both_t = cs_ref[...]
    size = float(p * p)

    def window(ref, j):
        return ref[:, j * STRIDE : j * STRIDE + p]

    use_own = flag_ref[0] == 1
    blocks = []
    for k in range(pairs):
        left, right = 2 * k, 2 * k + 1
        first_near = skip_ref[i * cols + left] == 0
        blocks.append(jnp.where(first_near, window(own_ref, left), window(own_ref, right)))
        blocks.append(jnp.where(first_near, window(prev_ref, left), window(prev_ref, right)))
    for k in range(pairs):
        left, right = 2 * k, 2 * k + 1
        second_far = skip_next_ref[i * cols + right] == 1
        blocks.append(jnp.where(second_far, window(next_ref, right), window(next_ref, left)))
        col_prev = jnp.where(second_far, window(prev_ref, right), window(prev_ref, left))
        col_own = jnp.where(second_far, window(own_ref, right), window(own_ref, left))
        blocks.append(jnp.where(use_own, col_own, col_prev))

    for t, blk in enumerate(blocks):
        x = blk.astype(f32)
        centered = x - _sum_all(x) / size
        spread = _sum_all(centered * centered) / size
        normed = (centered * lax.rsqrt(spread + EPSILON)).astype(bf16)
        half_ref[2 * p * t : 2 * p * (t + 1), :] = jnp.dot(
            both_t, normed, preferred_element_type=f32
        ).astype(bf16)
    halves = half_ref[...]
    x_ref[...] = jnp.dot(halves, cos_t, preferred_element_type=f32)
    y_ref[...] = jnp.dot(halves, sin_t, preferred_element_type=f32)

    def spectrum(t):
        base = 2 * p * t
        re = x_ref[base : base + p, :] - y_ref[base + p : base + 2 * p, :]
        im = y_ref[base : base + p, :] + x_ref[base + p : base + 2 * p, :]
        return re, im

    for c in range(cols):
        o_re, o_im = spectrum(2 * c)
        t_re, t_im = spectrum(2 * c + 1)
        c_re = (o_re * t_re + o_im * t_im).astype(bf16)
        c_im = (o_re * t_im - o_im * t_re).astype(bf16)
        a = jnp.dot(both_t, c_re, preferred_element_type=f32)
        b = jnp.dot(both_t, c_im, preferred_element_type=f32)
        br_ref[p * c : p * (c + 1), :] = (a[:p] + b[p:]).astype(bf16)
        bi_ref[p * c : p * (c + 1), :] = (b[:p] - a[p:]).astype(bf16)

    corr = (
        jnp.dot(br_ref[...], cos_t, preferred_element_type=f32)
        + jnp.dot(bi_ref[...], sin_t, preferred_element_type=f32)
    ) / float(p) ** 4
    w = jnp.exp(SHARPNESS * corr)
    u_col = lax.broadcasted_iota(jnp.int32, (cols * p, 1), 0) % p
    off_col = jnp.where(u_col < p // 2, u_col, u_col - p).astype(f32)
    u_row = lax.broadcasted_iota(jnp.int32, (1, p), 1)
    off_row = jnp.where(u_row < p // 2, u_row, u_row - p).astype(f32)
    rows_sum = jnp.sum(w, axis=1, keepdims=True)
    total = jnp.sum(rows_sum.reshape(cols, p, 1), axis=1)
    along_rows = jnp.sum((rows_sum * off_col).reshape(cols, p, 1), axis=1)
    cols_sum = jnp.sum(w.reshape(cols, p, p), axis=1)
    along_cols = jnp.sum(cols_sum * off_row, axis=1, keepdims=True)
    ar = along_rows / total / float(RIM)
    ac = along_cols / total / float(RIM)
    lane = lax.broadcasted_iota(jnp.int32, (cols, 128), 1)
    res = jnp.where(lane == 0, ar, jnp.where(lane == 1, ac, 0.0))
    height = out_ref.shape[1]
    if height > cols:
        res = jnp.concatenate([res, jnp.zeros((height - cols, 128), f32)], axis=0)
    out_ref[0] = res


def pair_flows(own_pad, prev_pad, next_pad, skip_flat, skip_next_flat, use_own, row0, tables):
    tall, broad = own_pad.shape
    rows = (tall - (PATCH - STRIDE)) // STRIDE
    cols = (broad - (PATCH - STRIDE)) // STRIDE
    assert cols % 2 == 0
    height = max(8, -(-cols // 8) * 8)
    both_t, cos_t, sin_t = tables
    band = pl.BlockSpec((pl.Element(PATCH), pl.Element(broad)), lambda i, *_: (i * STRIDE, 0))
    table = pl.BlockSpec((PATCH, PATCH), lambda i, *_: (0, 0))
    grid_spec = pltpu.PrefetchScalarGridSpec(
        num_scalar_prefetch=3,
        grid=(rows,),
        in_specs=[band, band, band, pl.BlockSpec((2 * PATCH, PATCH), lambda i, *_: (0, 0)), table, table],
        out_specs=pl.BlockSpec((1, height, 128), lambda i, *_: (i, 0, 0)),
        scratch_shapes=[
            pltpu.VMEM((4 * cols * PATCH, PATCH), jnp.bfloat16),
            pltpu.VMEM((4 * cols * PATCH, PATCH), jnp.float32),
            pltpu.VMEM((4 * cols * PATCH, PATCH), jnp.float32),
            pltpu.VMEM((cols * PATCH, PATCH), jnp.bfloat16),
            pltpu.VMEM((cols * PATCH, PATCH), jnp.bfloat16),
        ],
    )
    out = pl.pallas_call(
        functools.partial(_flow_kernel, cols=cols, row0=row0),
        grid_spec=grid_spec,
        out_shape=jax.ShapeDtypeStruct((rows, height, 128), jnp.float32),
        compiler_params=pltpu.CompilerParams(
            dimension_semantics=("arbitrary",), vmem_limit_bytes=48 * 1024 * 1024
        ),
    )(skip_flat, skip_next_flat, use_own.reshape(1), own_pad, prev_pad, next_pad, both_t, cos_t, sin_t)
    half = cols // 2
    first = jnp.repeat(jnp.transpose(out[:, :half, 0:2], (2, 0, 1)), 2, axis=2)
    second = jnp.repeat(jnp.transpose(out[:, half:cols, 0:2], (2, 0, 1)), 2, axis=2)
    return first, second


def gather_sections(value, axis):
    count = lax.axis_size(axis)
    spread = jnp.broadcast_to(value[None], (count,) + value.shape)
    return lax.all_to_all(spread, axis, 0, 0, tiled=True)


def earlier(values, steps, axis):
    width = values.shape[axis]
    widths = [(0, 0)] * values.ndim
    widths[axis] = (steps, 0)
    return lax.slice_in_dim(jnp.pad(values, widths), 0, width, axis=axis)


def later(values, steps, axis):
    width = values.shape[axis]
    widths = [(0, 0)] * values.ndim
    widths[axis] = (0, steps)
    return lax.slice_in_dim(jnp.pad(values, widths), steps, steps + width, axis=axis)


def relax(flow_field, weight, distance):
    near = (distance == 1).astype(jnp.float32)
    far = 1.0 - near
    diag = STIFFNESS + weight + later(weight * near, 1, 0) + later(weight * far, 2, 0)
    positions = jnp.zeros_like(flow_field)
    for sweep in range(RELAX):
        partner = near * earlier(positions, 1, 1) + far * earlier(positions, 2, 1)
        error = weight * (positions - partner - flow_field)
        gradient = (
            STIFFNESS * positions + error - later(error * near, 1, 1) - later(error * far, 2, 1)
        )
        positions = positions - RELAXATION * gradient / diag
    return positions


def body(images, skipped, patch_mask):
    index = lax.axis_index("sec")
    own_distance = jnp.where(index >= 2, 1 + skipped, 1)
    own_pad = extended(images, (("sub", 1), ("tile", 2)), RIM)[0]
    skip_next = shifted(skipped, "sec", -1)
    use_own = (index == 0).astype(jnp.int32)
    rows_count = (own_pad.shape[0] - (PATCH - STRIDE)) // STRIDE
    chunks = 2 if rows_count % 2 == 0 else 1
    per = rows_count // chunks
    cos_t, sin_t = dft_tables(PATCH)
    tables = (jnp.concatenate([cos_t, sin_t], axis=0), cos_t, sin_t)
    skip_flat = skipped.reshape(-1)
    skip_next_flat = skip_next.reshape(-1)
    firsts, seconds = [], []
    for c in range(chunks):
        start = c * per * STRIDE
        own_c = own_pad[start : start + per * STRIDE + PATCH - STRIDE]
        prev_c = shifted(own_c, "sec", 1)
        next_c = shifted(own_c, "sec", -1)
        first_c, second_c = pair_flows(
            own_c, prev_c, next_c, skip_flat, skip_next_flat, use_own, c * per, tables
        )
        firsts.append(first_c)
        seconds.append(second_c)
    first = jnp.concatenate(firsts, axis=1)
    second = jnp.concatenate(seconds, axis=1)
    first = jnp.where(skipped[0] == 0, first, 0.0)
    second = jnp.where(skip_next[0] == 1, second, 0.0)
    weight = patch_mask.astype(jnp.float32) * (index >= 1).astype(jnp.float32)
    stacked = jnp.concatenate(
        [first, second, weight, own_distance.astype(jnp.float32)], axis=0
    )
    every = jnp.moveaxis(gather_sections(stacked, "sec"), 0, 1)
    raw_all = every[0:2] + earlier(every[2:4], 1, 1)
    flow_all = raw_all * every[4]
    positions_all = relax(flow_all, every[4], every[5])
    flow_field = lax.dynamic_slice_in_dim(flow_all, index, 1, 1)
    positions = lax.dynamic_slice_in_dim(positions_all, index, 1, 1)
    return (flow_field, positions)


def solution(mesh):
    placed = (
        P(("groups", "sec"), "sub", "tile"),
        P(("groups", "sec"), "sub", "tile"),
        P(("groups", "sec"), "sub", "tile"),
    )
    return jax.shard_map(
        body,
        mesh=mesh,
        in_specs=placed,
        out_specs=(
            P(None, ("groups", "sec"), "sub", "tile"),
            P(None, ("groups", "sec"), "sub", "tile"),
        ),
        check_vma=False,
    )
```

```python
import functools
import math

import jax
import jax.numpy as jnp
from jax import lax
from jax.experimental import pallas as pl
from jax.experimental.pallas import tpu as pltpu
from jax.sharding import PartitionSpec as P

PATCH = 160
STRIDE = 128
RELAX = 6
RIM = 16


SHARPNESS = 48.0
STIFFNESS = 0.25
RELAXATION = 0.8
EPSILON = 1e-05


def shifted(value, axis, steps):
    count = lax.axis_size(axis)
    first, last = (max(0, -steps), min(count, count - steps))
    return lax.ppermute(value, axis, [(source, source + steps) for source in range(first, last)])


def _strip_send(strip, dim):
    return jnp.swapaxes(strip, 1, 2) if dim == 2 else strip


def _strip_recv(strip, dim):
    return jnp.swapaxes(strip, 1, 2) if dim == 2 else strip


def extended(block, sides, width):
    for axis, dim in sides:
        count = lax.axis_size(axis)
        top = lax.slice_in_dim(block, 0, width, axis=dim)
        bottom = lax.slice_in_dim(block, block.shape[dim] - width, None, axis=dim)
        if count == 2:
            index = lax.axis_index(axis)
            send = _strip_send(jnp.where(index == 0, bottom, top), dim)
            got = _strip_recv(lax.ppermute(send, axis, [(0, 1), (1, 0)]), dim)
            low = jnp.where(index == 1, got, jnp.zeros_like(got))
            high = jnp.where(index == 0, got, jnp.zeros_like(got))
        else:
            forward = [(i, i + 1) for i in range(count - 1)]
            backward = [(target, source) for source, target in forward]
            low = _strip_recv(lax.ppermute(_strip_send(bottom, dim), axis, forward), dim)
            high = _strip_recv(lax.ppermute(_strip_send(top, dim), axis, backward), dim)
        block = jnp.concatenate([low, block, high], axis=dim)
    return block


def extended_pairs(block, width):
    sub = lax.axis_index("sub")
    tile = lax.axis_index("tile")
    swap = [(0, 1), (1, 0)]
    rows_send = jnp.where(
        sub == 0, block[:, -width:, :], block[:, :width, :]
    )
    cols_send = jnp.swapaxes(jnp.where(tile == 0, block[:, :, -width:], block[:, :, :width]), 1, 2)
    corner_rows = jnp.where(sub == 0, block[:, -width:, :], block[:, :width, :])
    corner_send = jnp.where(tile == 0, corner_rows[:, :, -width:], corner_rows[:, :, :width])
    rows_got = lax.ppermute(rows_send, "sub", swap)
    cols_got = jnp.swapaxes(lax.ppermute(cols_send, "tile", swap), 1, 2)
    corner_got = lax.ppermute(corner_send, ("tile", "sub"), [(0, 3), (3, 0), (1, 2), (2, 1)])

    def keep(flag, value):
        return jnp.where(flag, value, jnp.zeros_like(value))

    top, bottom = sub == 1, sub == 0
    left, right = tile == 1, tile == 0
    middle = jnp.concatenate([keep(left, cols_got), block, keep(right, cols_got)], axis=2)
    upper = jnp.concatenate(
        [keep(top & left, corner_got), keep(top, rows_got), keep(top & right, corner_got)], axis=2
    )
    lower = jnp.concatenate(
        [keep(bottom & left, corner_got), keep(bottom, rows_got), keep(bottom & right, corner_got)],
        axis=2,
    )
    return jnp.concatenate([upper, middle, lower], axis=1)


def dft_tables(patch):
    index = jnp.arange(patch, dtype=jnp.int32)
    product = index[:, None] * index[None, :] % patch
    angle = product.astype(jnp.float32) * (2.0 * math.pi / patch)
    return (jnp.cos(angle).astype(jnp.bfloat16), (-jnp.sin(angle)).astype(jnp.bfloat16))


def _sum_all(x):
    return jnp.sum(jnp.sum(x, axis=1, keepdims=True), axis=0, keepdims=True)


def _flow_kernel(
    skip_ref, skip_next_ref, flag_ref, own_ref, prev_ref, next_ref, cs_ref, c_ref, s_ref, out_ref,
    half_ref, x_ref, y_ref, br_ref, bi_ref,
    *, cols, row0,
):
    f32, bf16 = jnp.float32, jnp.bfloat16
    p = PATCH
    pairs = cols // 2
    i = pl.program_id(0) + row0
    cos_t = c_ref[...]
    sin_t = s_ref[...]
    both_t = cs_ref[...]
    size = float(p * p)

    def window(ref, j):
        return ref[:, j * STRIDE : j * STRIDE + p]

    use_own = flag_ref[0] == 1
    blocks = []
    for k in range(pairs):
        left, right = 2 * k, 2 * k + 1
        first_near = skip_ref[i * cols + left] == 0
        blocks.append(jnp.where(first_near, window(own_ref, left), window(own_ref, right)))
        blocks.append(jnp.where(first_near, window(prev_ref, left), window(prev_ref, right)))
    for k in range(pairs):
        left, right = 2 * k, 2 * k + 1
        second_far = skip_next_ref[i * cols + right] == 1
        blocks.append(jnp.where(second_far, window(next_ref, right), window(next_ref, left)))
        col_prev = jnp.where(second_far, window(prev_ref, right), window(prev_ref, left))
        col_own = jnp.where(second_far, window(own_ref, right), window(own_ref, left))
        blocks.append(jnp.where(use_own, col_own, col_prev))

    for t, blk in enumerate(blocks):
        x = blk.astype(f32)
        centered = x - _sum_all(x) / size
        spread = _sum_all(centered * centered) / size
        normed = (centered * lax.rsqrt(spread + EPSILON)).astype(bf16)
        half_ref[2 * p * t : 2 * p * (t + 1), :] = jnp.dot(
            both_t, normed, preferred_element_type=f32
        ).astype(bf16)
    halves = half_ref[...]
    x_ref[...] = jnp.dot(halves, cos_t, preferred_element_type=f32)
    y_ref[...] = jnp.dot(halves, sin_t, preferred_element_type=f32)

    def spectrum(t):
        base = 2 * p * t
        re = x_ref[base : base + p, :] - y_ref[base + p : base + 2 * p, :]
        im = y_ref[base : base + p, :] + x_ref[base + p : base + 2 * p, :]
        return re, im

    for c in range(cols):
        o_re, o_im = spectrum(2 * c)
        t_re, t_im = spectrum(2 * c + 1)
        c_re = (o_re * t_re + o_im * t_im).astype(bf16)
        c_im = (o_re * t_im - o_im * t_re).astype(bf16)
        a = jnp.dot(both_t, c_re, preferred_element_type=f32)
        b = jnp.dot(both_t, c_im, preferred_element_type=f32)
        br_ref[p * c : p * (c + 1), :] = (a[:p] + b[p:]).astype(bf16)
        bi_ref[p * c : p * (c + 1), :] = (b[:p] - a[p:]).astype(bf16)

    corr = (
        jnp.dot(br_ref[...], cos_t, preferred_element_type=f32)
        + jnp.dot(bi_ref[...], sin_t, preferred_element_type=f32)
    ) / float(p) ** 4
    w = jnp.exp(SHARPNESS * corr)
    u_col = lax.broadcasted_iota(jnp.int32, (cols * p, 1), 0) % p
    off_col = jnp.where(u_col < p // 2, u_col, u_col - p).astype(f32)
    u_row = lax.broadcasted_iota(jnp.int32, (1, p), 1)
    off_row = jnp.where(u_row < p // 2, u_row, u_row - p).astype(f32)
    rows_sum = jnp.sum(w, axis=1, keepdims=True)
    total = jnp.sum(rows_sum.reshape(cols, p, 1), axis=1)
    along_rows = jnp.sum((rows_sum * off_col).reshape(cols, p, 1), axis=1)
    cols_sum = jnp.sum(w.reshape(cols, p, p), axis=1)
    along_cols = jnp.sum(cols_sum * off_row, axis=1, keepdims=True)
    ar = along_rows / total / float(RIM)
    ac = along_cols / total / float(RIM)
    lane = lax.broadcasted_iota(jnp.int32, (cols, 128), 1)
    res = jnp.where(lane == 0, ar, jnp.where(lane == 1, ac, 0.0))
    height = out_ref.shape[1]
    if height > cols:
        res = jnp.concatenate([res, jnp.zeros((height - cols, 128), f32)], axis=0)
    out_ref[0] = res


def pair_flows(own_pad, prev_pad, next_pad, skip_flat, skip_next_flat, use_own, row0, tables):
    tall, broad = own_pad.shape
    rows = (tall - (PATCH - STRIDE)) // STRIDE
    cols = (broad - (PATCH - STRIDE)) // STRIDE
    assert cols % 2 == 0
    height = max(8, -(-cols // 8) * 8)
    both_t, cos_t, sin_t = tables
    band = pl.BlockSpec((pl.Element(PATCH), pl.Element(broad)), lambda i, *_: (i * STRIDE, 0))
    table = pl.BlockSpec((PATCH, PATCH), lambda i, *_: (0, 0))
    grid_spec = pltpu.PrefetchScalarGridSpec(
        num_scalar_prefetch=3,
        grid=(rows,),
        in_specs=[band, band, band, pl.BlockSpec((2 * PATCH, PATCH), lambda i, *_: (0, 0)), table, table],
        out_specs=pl.BlockSpec((1, height, 128), lambda i, *_: (i, 0, 0)),
        scratch_shapes=[
            pltpu.VMEM((4 * cols * PATCH, PATCH), jnp.bfloat16),
            pltpu.VMEM((4 * cols * PATCH, PATCH), jnp.float32),
            pltpu.VMEM((4 * cols * PATCH, PATCH), jnp.float32),
            pltpu.VMEM((cols * PATCH, PATCH), jnp.bfloat16),
            pltpu.VMEM((cols * PATCH, PATCH), jnp.bfloat16),
        ],
    )
    out = pl.pallas_call(
        functools.partial(_flow_kernel, cols=cols, row0=row0),
        grid_spec=grid_spec,
        out_shape=jax.ShapeDtypeStruct((rows, height, 128), jnp.float32),
        compiler_params=pltpu.CompilerParams(
            dimension_semantics=("arbitrary",), vmem_limit_bytes=48 * 1024 * 1024
        ),
    )(skip_flat, skip_next_flat, use_own.reshape(1), own_pad, prev_pad, next_pad, both_t, cos_t, sin_t)
    half = cols // 2
    first = jnp.repeat(jnp.transpose(out[:, :half, 0:2], (2, 0, 1)), 2, axis=2)
    second = jnp.repeat(jnp.transpose(out[:, half:cols, 0:2], (2, 0, 1)), 2, axis=2)
    return first, second


def gather_sections(value, axis):
    count = lax.axis_size(axis)
    spread = jnp.broadcast_to(value[None], (count,) + value.shape)
    return lax.all_to_all(spread, axis, 0, 0, tiled=True)


def earlier(values, steps, axis):
    width = values.shape[axis]
    widths = [(0, 0)] * values.ndim
    widths[axis] = (steps, 0)
    return lax.slice_in_dim(jnp.pad(values, widths), 0, width, axis=axis)


def later(values, steps, axis):
    width = values.shape[axis]
    widths = [(0, 0)] * values.ndim
    widths[axis] = (0, steps)
    return lax.slice_in_dim(jnp.pad(values, widths), steps, steps + width, axis=axis)


def relax(flow_field, weight, distance):
    near = (distance == 1).astype(jnp.float32)
    far = 1.0 - near
    diag = STIFFNESS + weight + later(weight * near, 1, 0) + later(weight * far, 2, 0)
    positions = jnp.zeros_like(flow_field)
    for sweep in range(RELAX):
        partner = near * earlier(positions, 1, 1) + far * earlier(positions, 2, 1)
        error = weight * (positions - partner - flow_field)
        gradient = (
            STIFFNESS * positions + error - later(error * near, 1, 1) - later(error * far, 2, 1)
        )
        positions = positions - RELAXATION * gradient / diag
    return positions


def body(images, skipped, patch_mask):
    index = lax.axis_index("sec")
    own_distance = jnp.where(index >= 2, 1 + skipped, 1)
    if lax.axis_size("sub") == 2 and lax.axis_size("tile") == 2:
        own_pad = extended_pairs(images, RIM)[0]
    else:
        own_pad = extended(images, (("sub", 1), ("tile", 2)), RIM)[0]
    skip_next = shifted(skipped, "sec", -1)
    use_own = (index == 0).astype(jnp.int32)
    rows_count = (own_pad.shape[0] - (PATCH - STRIDE)) // STRIDE
    chunks = max(n for n in (1, 2, 4) if rows_count % n == 0)
    per = rows_count // chunks
    cos_t, sin_t = dft_tables(PATCH)
    tables = (jnp.concatenate([cos_t, sin_t], axis=0), cos_t, sin_t)
    skip_flat = skipped.reshape(-1)
    skip_next_flat = skip_next.reshape(-1)
    firsts, seconds = [], []
    for c in range(chunks):
        start = c * per * STRIDE
        own_c = own_pad[start : start + per * STRIDE + PATCH - STRIDE]
        prev_c = shifted(own_c, "sec", 1)
        next_c = shifted(own_c, "sec", -1)
        first_c, second_c = pair_flows(
            own_c, prev_c, next_c, skip_flat, skip_next_flat, use_own, c * per, tables
        )
        firsts.append(first_c)
        seconds.append(second_c)
    first = jnp.concatenate(firsts, axis=1)
    second = jnp.concatenate(seconds, axis=1)
    first = jnp.where(skipped[0] == 0, first, 0.0)
    second = jnp.where(skip_next[0] == 1, second, 0.0)
    weight = patch_mask.astype(jnp.float32) * (index >= 1).astype(jnp.float32)
    stacked = jnp.concatenate(
        [first, second, weight, own_distance.astype(jnp.float32)], axis=0
    )
    every = jnp.moveaxis(gather_sections(stacked, "sec"), 0, 1)
    raw_all = every[0:2] + earlier(every[2:4], 1, 1)
    flow_all = raw_all * every[4]
    positions_all = relax(flow_all, every[4], every[5])
    flow_field = lax.dynamic_slice_in_dim(flow_all, index, 1, 1)
    positions = lax.dynamic_slice_in_dim(positions_all, index, 1, 1)
    return (flow_field, positions)


def solution(mesh):
    placed = (
        P(("groups", "sec"), "sub", "tile"),
        P(("groups", "sec"), "sub", "tile"),
        P(("groups", "sec"), "sub", "tile"),
    )
    return jax.shard_map(
        body,
        mesh=mesh,
        in_specs=placed,
        out_specs=(
            P(None, ("groups", "sec"), "sub", "tile"),
            P(None, ("groups", "sec"), "sub", "tile"),
        ),
        check_vma=False,
    )
```

```python
import functools
import math

import jax
import jax.numpy as jnp
from jax import lax
from jax.experimental import pallas as pl
from jax.experimental.pallas import tpu as pltpu
from jax.sharding import PartitionSpec as P

PATCH = 160
STRIDE = 128
RELAX = 6
RIM = 16


SHARPNESS = 48.0
STIFFNESS = 0.25
RELAXATION = 0.8
EPSILON = 1e-05


def shifted(value, axis, steps):
    count = lax.axis_size(axis)
    first, last = (max(0, -steps), min(count, count - steps))
    return lax.ppermute(value, axis, [(source, source + steps) for source in range(first, last)])


def _strip_send(strip, dim):
    return jnp.swapaxes(strip, 1, 2) if dim == 2 else strip


def _strip_recv(strip, dim):
    return jnp.swapaxes(strip, 1, 2) if dim == 2 else strip


def extended(block, sides, width):
    for axis, dim in sides:
        count = lax.axis_size(axis)
        top = lax.slice_in_dim(block, 0, width, axis=dim)
        bottom = lax.slice_in_dim(block, block.shape[dim] - width, None, axis=dim)
        if count == 2:
            index = lax.axis_index(axis)
            send = _strip_send(jnp.where(index == 0, bottom, top), dim)
            got = _strip_recv(lax.ppermute(send, axis, [(0, 1), (1, 0)]), dim)
            low = jnp.where(index == 1, got, jnp.zeros_like(got))
            high = jnp.where(index == 0, got, jnp.zeros_like(got))
        else:
            forward = [(i, i + 1) for i in range(count - 1)]
            backward = [(target, source) for source, target in forward]
            low = _strip_recv(lax.ppermute(_strip_send(bottom, dim), axis, forward), dim)
            high = _strip_recv(lax.ppermute(_strip_send(top, dim), axis, backward), dim)
        block = jnp.concatenate([low, block, high], axis=dim)
    return block


def extended_pairs(block, width):
    sub = lax.axis_index("sub")
    tile = lax.axis_index("tile")
    swap = [(0, 1), (1, 0)]
    rows_send = jnp.where(
        sub == 0, block[:, -width:, :], block[:, :width, :]
    )
    cols_send = jnp.swapaxes(jnp.where(tile == 0, block[:, :, -width:], block[:, :, :width]), 1, 2)
    corner_rows = jnp.where(sub == 0, block[:, -width:, :], block[:, :width, :])
    corner_send = jnp.where(tile == 0, corner_rows[:, :, -width:], corner_rows[:, :, :width])
    rows_got = lax.ppermute(rows_send, "sub", swap)
    cols_got = jnp.swapaxes(lax.ppermute(cols_send, "tile", swap), 1, 2)
    corner_got = lax.ppermute(corner_send, ("tile", "sub"), [(0, 3), (3, 0), (1, 2), (2, 1)])

    def keep(flag, value):
        return jnp.where(flag, value, jnp.zeros_like(value))

    top, bottom = sub == 1, sub == 0
    left, right = tile == 1, tile == 0
    middle = jnp.concatenate([keep(left, cols_got), block, keep(right, cols_got)], axis=2)
    upper = jnp.concatenate(
        [keep(top & left, corner_got), keep(top, rows_got), keep(top & right, corner_got)], axis=2
    )
    lower = jnp.concatenate(
        [keep(bottom & left, corner_got), keep(bottom, rows_got), keep(bottom & right, corner_got)],
        axis=2,
    )
    return jnp.concatenate([upper, middle, lower], axis=1)


def dft_tables(patch):
    index = jnp.arange(patch, dtype=jnp.int32)
    product = index[:, None] * index[None, :] % patch
    angle = product.astype(jnp.float32) * (2.0 * math.pi / patch)
    return (jnp.cos(angle).astype(jnp.bfloat16), (-jnp.sin(angle)).astype(jnp.bfloat16))


def _sum_all(x):
    return jnp.sum(jnp.sum(x, axis=1, keepdims=True), axis=0, keepdims=True)


def _flow_kernel(
    skip_ref, skip_next_ref, flag_ref, own_ref, prev_ref, next_ref, cs_ref, c_ref, s_ref, inv_ref,
    out_ref, half_ref, x_ref, y_ref, br_ref, bi_ref,
    *, cols, row0,
):
    f32, bf16 = jnp.float32, jnp.bfloat16
    p = PATCH
    pairs = cols // 2
    i = pl.program_id(0) + row0
    cos_t = c_ref[...]
    sin_t = s_ref[...]
    both_t = cs_ref[...]
    inverse_t = inv_ref[...]
    size = float(p * p)

    def window(ref, j):
        return ref[:, j * STRIDE : j * STRIDE + p]

    use_own = flag_ref[0] == 1
    blocks = []
    for k in range(pairs):
        left, right = 2 * k, 2 * k + 1
        first_near = skip_ref[i * cols + left] == 0
        blocks.append(jnp.where(first_near, window(own_ref, left), window(own_ref, right)))
        blocks.append(jnp.where(first_near, window(prev_ref, left), window(prev_ref, right)))
    for k in range(pairs):
        left, right = 2 * k, 2 * k + 1
        second_far = skip_next_ref[i * cols + right] == 1
        blocks.append(jnp.where(second_far, window(next_ref, right), window(next_ref, left)))
        col_prev = jnp.where(second_far, window(prev_ref, right), window(prev_ref, left))
        col_own = jnp.where(second_far, window(own_ref, right), window(own_ref, left))
        blocks.append(jnp.where(use_own, col_own, col_prev))

    for t, blk in enumerate(blocks):
        x = blk.astype(f32)
        centered = x - _sum_all(x) / size
        spread = _sum_all(centered * centered) / size
        normed = (centered * lax.rsqrt(spread + EPSILON)).astype(bf16)
        half_ref[2 * p * t : 2 * p * (t + 1), :] = jnp.dot(
            both_t, normed, preferred_element_type=f32
        ).astype(bf16)
    halves = half_ref[...]
    x_ref[...] = jnp.dot(halves, cos_t, preferred_element_type=f32)
    y_ref[...] = jnp.dot(halves, sin_t, preferred_element_type=f32)

    def spectrum(t):
        base = 2 * p * t
        re = x_ref[base : base + p, :] - y_ref[base + p : base + 2 * p, :]
        im = y_ref[base : base + p, :] + x_ref[base + p : base + 2 * p, :]
        return re, im

    for c in range(cols):
        o_re, o_im = spectrum(2 * c)
        t_re, t_im = spectrum(2 * c + 1)
        c_re = (o_re * t_re + o_im * t_im).astype(bf16)
        c_im = (o_re * t_im - o_im * t_re).astype(bf16)
        back = jnp.dot(
            inverse_t, jnp.concatenate([c_re, c_im], axis=0), preferred_element_type=f32
        ).astype(bf16)
        br_ref[p * c : p * (c + 1), :] = back[:p]
        bi_ref[p * c : p * (c + 1), :] = back[p:]

    corr = (
        jnp.dot(br_ref[...], cos_t, preferred_element_type=f32)
        + jnp.dot(bi_ref[...], sin_t, preferred_element_type=f32)
    ) / float(p) ** 4
    w = jnp.exp(SHARPNESS * corr)
    u_col = lax.broadcasted_iota(jnp.int32, (cols * p, 1), 0) % p
    off_col = jnp.where(u_col < p // 2, u_col, u_col - p).astype(f32)
    u_row = lax.broadcasted_iota(jnp.int32, (1, p), 1)
    off_row = jnp.where(u_row < p // 2, u_row, u_row - p).astype(f32)
    rows_sum = jnp.sum(w, axis=1, keepdims=True)
    total = jnp.sum(rows_sum.reshape(cols, p, 1), axis=1)
    along_rows = jnp.sum((rows_sum * off_col).reshape(cols, p, 1), axis=1)
    cols_sum = jnp.sum(w.reshape(cols, p, p), axis=1)
    along_cols = jnp.sum(cols_sum * off_row, axis=1, keepdims=True)
    ar = along_rows / total / float(RIM)
    ac = along_cols / total / float(RIM)
    lane = lax.broadcasted_iota(jnp.int32, (cols, 128), 1)
    res = jnp.where(lane == 0, ar, jnp.where(lane == 1, ac, 0.0))
    height = out_ref.shape[1]
    if height > cols:
        res = jnp.concatenate([res, jnp.zeros((height - cols, 128), f32)], axis=0)
    out_ref[0] = res


def pair_flows(own_pad, prev_pad, next_pad, skip_flat, skip_next_flat, use_own, row0, tables):
    tall, broad = own_pad.shape
    rows = (tall - (PATCH - STRIDE)) // STRIDE
    cols = (broad - (PATCH - STRIDE)) // STRIDE
    assert cols % 2 == 0
    height = max(8, -(-cols // 8) * 8)
    both_t, cos_t, sin_t, inverse_t = tables
    band = pl.BlockSpec((pl.Element(PATCH), pl.Element(broad)), lambda i, *_: (i * STRIDE, 0))
    table = pl.BlockSpec((PATCH, PATCH), lambda i, *_: (0, 0))
    grid_spec = pltpu.PrefetchScalarGridSpec(
        num_scalar_prefetch=3,
        grid=(rows,),
        in_specs=[
            band, band, band, pl.BlockSpec((2 * PATCH, PATCH), lambda i, *_: (0, 0)), table, table,
            pl.BlockSpec((2 * PATCH, 2 * PATCH), lambda i, *_: (0, 0)),
        ],
        out_specs=pl.BlockSpec((1, height, 128), lambda i, *_: (i, 0, 0)),
        scratch_shapes=[
            pltpu.VMEM((4 * cols * PATCH, PATCH), jnp.bfloat16),
            pltpu.VMEM((4 * cols * PATCH, PATCH), jnp.float32),
            pltpu.VMEM((4 * cols * PATCH, PATCH), jnp.float32),
            pltpu.VMEM((cols * PATCH, PATCH), jnp.bfloat16),
            pltpu.VMEM((cols * PATCH, PATCH), jnp.bfloat16),
        ],
    )
    out = pl.pallas_call(
        functools.partial(_flow_kernel, cols=cols, row0=row0),
        grid_spec=grid_spec,
        out_shape=jax.ShapeDtypeStruct((rows, height, 128), jnp.float32),
        compiler_params=pltpu.CompilerParams(
            dimension_semantics=("arbitrary",), vmem_limit_bytes=48 * 1024 * 1024
        ),
    )(skip_flat, skip_next_flat, use_own.reshape(1), own_pad, prev_pad, next_pad, both_t, cos_t, sin_t, inverse_t)
    half = cols // 2
    first = jnp.repeat(jnp.transpose(out[:, :half, 0:2], (2, 0, 1)), 2, axis=2)
    second = jnp.repeat(jnp.transpose(out[:, half:cols, 0:2], (2, 0, 1)), 2, axis=2)
    return first, second


def gather_sections(value, axis):
    count = lax.axis_size(axis)
    spread = jnp.broadcast_to(value[None], (count,) + value.shape)
    return lax.all_to_all(spread, axis, 0, 0, tiled=True)


def earlier(values, steps, axis):
    width = values.shape[axis]
    widths = [(0, 0)] * values.ndim
    widths[axis] = (steps, 0)
    return lax.slice_in_dim(jnp.pad(values, widths), 0, width, axis=axis)


def later(values, steps, axis):
    width = values.shape[axis]
    widths = [(0, 0)] * values.ndim
    widths[axis] = (0, steps)
    return lax.slice_in_dim(jnp.pad(values, widths), steps, steps + width, axis=axis)


def relax(flow_field, weight, distance):
    near = (distance == 1).astype(jnp.float32)
    far = 1.0 - near
    diag = STIFFNESS + weight + later(weight * near, 1, 0) + later(weight * far, 2, 0)
    positions = jnp.zeros_like(flow_field)
    for sweep in range(RELAX):
        partner = near * earlier(positions, 1, 1) + far * earlier(positions, 2, 1)
        error = weight * (positions - partner - flow_field)
        gradient = (
            STIFFNESS * positions + error - later(error * near, 1, 1) - later(error * far, 2, 1)
        )
        positions = positions - RELAXATION * gradient / diag
    return positions


def body(images, skipped, patch_mask):
    index = lax.axis_index("sec")
    own_distance = jnp.where(index >= 2, 1 + skipped, 1)
    if lax.axis_size("sub") == 2 and lax.axis_size("tile") == 2:
        own_pad = extended_pairs(images, RIM)[0]
    else:
        own_pad = extended(images, (("sub", 1), ("tile", 2)), RIM)[0]
    skip_next = shifted(skipped, "sec", -1)
    use_own = (index == 0).astype(jnp.int32)
    rows_count = (own_pad.shape[0] - (PATCH - STRIDE)) // STRIDE
    chunks = max(n for n in (1, 2, 4) if rows_count % n == 0)
    per = rows_count // chunks
    cos_t, sin_t = dft_tables(PATCH)
    inverse_t = jnp.concatenate(
        [jnp.concatenate([cos_t, sin_t], axis=1), jnp.concatenate([-sin_t, cos_t], axis=1)], axis=0
    )
    tables = (jnp.concatenate([cos_t, sin_t], axis=0), cos_t, sin_t, inverse_t)
    skip_flat = skipped.reshape(-1)
    skip_next_flat = skip_next.reshape(-1)
    firsts, seconds = [], []
    for c in range(chunks):
        start = c * per * STRIDE
        own_c = own_pad[start : start + per * STRIDE + PATCH - STRIDE]
        prev_c = shifted(own_c, "sec", 1)
        next_c = shifted(own_c, "sec", -1)
        first_c, second_c = pair_flows(
            own_c, prev_c, next_c, skip_flat, skip_next_flat, use_own, c * per, tables
        )
        firsts.append(first_c)
        seconds.append(second_c)
    first = jnp.concatenate(firsts, axis=1)
    second = jnp.concatenate(seconds, axis=1)
    first = jnp.where(skipped[0] == 0, first, 0.0)
    second = jnp.where(skip_next[0] == 1, second, 0.0)
    weight = patch_mask.astype(jnp.float32) * (index >= 1).astype(jnp.float32)
    stacked = jnp.concatenate(
        [first, second, weight, own_distance.astype(jnp.float32)], axis=0
    )
    every = jnp.moveaxis(gather_sections(stacked, "sec"), 0, 1)
    raw_all = every[0:2] + earlier(every[2:4], 1, 1)
    flow_all = raw_all * every[4]
    positions_all = relax(flow_all, every[4], every[5])
    flow_field = lax.dynamic_slice_in_dim(flow_all, index, 1, 1)
    positions = lax.dynamic_slice_in_dim(positions_all, index, 1, 1)
    return (flow_field, positions)


def solution(mesh):
    placed = (
        P(("groups", "sec"), "sub", "tile"),
        P(("groups", "sec"), "sub", "tile"),
        P(("groups", "sec"), "sub", "tile"),
    )
    return jax.shard_map(
        body,
        mesh=mesh,
        in_specs=placed,
        out_specs=(
            P(None, ("groups", "sec"), "sub", "tile"),
            P(None, ("groups", "sec"), "sub", "tile"),
        ),
        check_vma=False,
    )
```

```python
import functools
import math

import jax
import jax.numpy as jnp
from jax import lax
from jax.experimental import pallas as pl
from jax.experimental.pallas import tpu as pltpu
from jax.sharding import PartitionSpec as P

PATCH = 160
STRIDE = 128
RELAX = 6
RIM = 16


SHARPNESS = 48.0
STIFFNESS = 0.25
RELAXATION = 0.8
EPSILON = 1e-05


def shifted(value, axis, steps):
    count = lax.axis_size(axis)
    first, last = (max(0, -steps), min(count, count - steps))
    return lax.ppermute(value, axis, [(source, source + steps) for source in range(first, last)])


def _strip_send(strip, dim):
    return jnp.swapaxes(strip, 1, 2) if dim == 2 else strip


def _strip_recv(strip, dim):
    return jnp.swapaxes(strip, 1, 2) if dim == 2 else strip


def extended(block, sides, width):
    for axis, dim in sides:
        count = lax.axis_size(axis)
        top = lax.slice_in_dim(block, 0, width, axis=dim)
        bottom = lax.slice_in_dim(block, block.shape[dim] - width, None, axis=dim)
        if count == 2:
            index = lax.axis_index(axis)
            send = _strip_send(jnp.where(index == 0, bottom, top), dim)
            got = _strip_recv(lax.ppermute(send, axis, [(0, 1), (1, 0)]), dim)
            low = jnp.where(index == 1, got, jnp.zeros_like(got))
            high = jnp.where(index == 0, got, jnp.zeros_like(got))
        else:
            forward = [(i, i + 1) for i in range(count - 1)]
            backward = [(target, source) for source, target in forward]
            low = _strip_recv(lax.ppermute(_strip_send(bottom, dim), axis, forward), dim)
            high = _strip_recv(lax.ppermute(_strip_send(top, dim), axis, backward), dim)
        block = jnp.concatenate([low, block, high], axis=dim)
    return block


def extended_pairs(block, width):
    sub = lax.axis_index("sub")
    tile = lax.axis_index("tile")
    swap = [(0, 1), (1, 0)]
    rows_send = jnp.where(
        sub == 0, block[:, -width:, :], block[:, :width, :]
    )
    cols_send = jnp.swapaxes(jnp.where(tile == 0, block[:, :, -width:], block[:, :, :width]), 1, 2)
    corner_rows = jnp.where(sub == 0, block[:, -width:, :], block[:, :width, :])
    corner_send = jnp.where(tile == 0, corner_rows[:, :, -width:], corner_rows[:, :, :width])
    rows_got = lax.ppermute(rows_send, "sub", swap)
    cols_got = jnp.swapaxes(lax.ppermute(cols_send, "tile", swap), 1, 2)
    corner_got = lax.ppermute(corner_send, ("tile", "sub"), [(0, 3), (3, 0), (1, 2), (2, 1)])

    def keep(flag, value):
        return jnp.where(flag, value, jnp.zeros_like(value))

    top, bottom = sub == 1, sub == 0
    left, right = tile == 1, tile == 0
    middle = jnp.concatenate([keep(left, cols_got), block, keep(right, cols_got)], axis=2)
    upper = jnp.concatenate(
        [keep(top & left, corner_got), keep(top, rows_got), keep(top & right, corner_got)], axis=2
    )
    lower = jnp.concatenate(
        [keep(bottom & left, corner_got), keep(bottom, rows_got), keep(bottom & right, corner_got)],
        axis=2,
    )
    return jnp.concatenate([upper, middle, lower], axis=1)


def dft_tables(patch):
    index = jnp.arange(patch, dtype=jnp.int32)
    product = index[:, None] * index[None, :] % patch
    angle = product.astype(jnp.float32) * (2.0 * math.pi / patch)
    return (jnp.cos(angle).astype(jnp.bfloat16), (-jnp.sin(angle)).astype(jnp.bfloat16))


def _sum_all(x):
    return jnp.sum(jnp.sum(x, axis=1, keepdims=True), axis=0, keepdims=True)


def _flow_kernel(
    skip_ref, skip_next_ref, flag_ref, own_ref, prev_ref, next_ref, cs_ref, c_ref, s_ref, inv_ref,
    out_ref, half_ref, x_ref, y_ref, br_ref, bi_ref,
    *, cols, row0,
):
    f32, bf16 = jnp.float32, jnp.bfloat16
    p = PATCH
    pairs = cols // 2
    i = pl.program_id(0) + row0
    cos_t = c_ref[...]
    sin_t = s_ref[...]
    both_t = cs_ref[...]
    inverse_t = inv_ref[...]
    size = float(p * p)

    def window(ref, j):
        return ref[:, j * STRIDE : j * STRIDE + p]

    use_own = flag_ref[0] == 1
    blocks = []
    for k in range(pairs):
        left, right = 2 * k, 2 * k + 1
        first_near = skip_ref[i * cols + left] == 0
        blocks.append(jnp.where(first_near, window(own_ref, left), window(own_ref, right)))
        blocks.append(jnp.where(first_near, window(prev_ref, left), window(prev_ref, right)))
    for k in range(pairs):
        left, right = 2 * k, 2 * k + 1
        second_far = skip_next_ref[i * cols + right] == 1
        blocks.append(jnp.where(second_far, window(next_ref, right), window(next_ref, left)))
        col_prev = jnp.where(second_far, window(prev_ref, right), window(prev_ref, left))
        col_own = jnp.where(second_far, window(own_ref, right), window(own_ref, left))
        blocks.append(jnp.where(use_own, col_own, col_prev))

    for t, blk in enumerate(blocks):
        x = blk.astype(f32)
        centered = x - _sum_all(x) / size
        spread = _sum_all(centered * centered) / size
        normed = (centered * lax.rsqrt(spread + EPSILON)).astype(bf16)
        half_ref[2 * p * t : 2 * p * (t + 1), :] = jnp.dot(
            both_t, normed, preferred_element_type=f32
        ).astype(bf16)
    halves = half_ref[...]
    x_ref[...] = jnp.dot(halves, cos_t, preferred_element_type=f32)
    y_ref[...] = jnp.dot(halves, sin_t, preferred_element_type=f32)

    def spectrum(t):
        base = 2 * p * t
        re = x_ref[base : base + p, :] - y_ref[base + p : base + 2 * p, :]
        im = y_ref[base : base + p, :] + x_ref[base + p : base + 2 * p, :]
        return re, im

    for c in range(cols):
        o_re, o_im = spectrum(2 * c)
        t_re, t_im = spectrum(2 * c + 1)
        c_re = (o_re * t_re + o_im * t_im).astype(bf16)
        c_im = (o_re * t_im - o_im * t_re).astype(bf16)
        back = jnp.dot(
            inverse_t, jnp.concatenate([c_re, c_im], axis=0), preferred_element_type=f32
        ).astype(bf16)
        br_ref[p * c : p * (c + 1), :] = back[:p]
        bi_ref[p * c : p * (c + 1), :] = back[p:]

    corr = (
        jnp.dot(br_ref[...], cos_t, preferred_element_type=f32)
        + jnp.dot(bi_ref[...], sin_t, preferred_element_type=f32)
    ) / float(p) ** 4
    w = jnp.exp(SHARPNESS * corr)
    u_col = lax.broadcasted_iota(jnp.int32, (cols * p, 1), 0) % p
    off_col = jnp.where(u_col < p // 2, u_col, u_col - p).astype(f32)
    u_row = lax.broadcasted_iota(jnp.int32, (1, p), 1)
    off_row = jnp.where(u_row < p // 2, u_row, u_row - p).astype(f32)
    rows_sum = jnp.sum(w, axis=1, keepdims=True)
    total = jnp.sum(rows_sum.reshape(cols, p, 1), axis=1)
    along_rows = jnp.sum((rows_sum * off_col).reshape(cols, p, 1), axis=1)
    cols_sum = jnp.sum(w.reshape(cols, p, p), axis=1)
    along_cols = jnp.sum(cols_sum * off_row, axis=1, keepdims=True)
    ar = along_rows / total / float(RIM)
    ac = along_cols / total / float(RIM)
    lane = lax.broadcasted_iota(jnp.int32, (cols, 128), 1)
    res = jnp.where(lane == 0, ar, jnp.where(lane == 1, ac, 0.0))
    height = out_ref.shape[1]
    if height > cols:
        res = jnp.concatenate([res, jnp.zeros((height - cols, 128), f32)], axis=0)
    out_ref[0] = res


def pair_flows(own_pad, prev_pad, next_pad, skip_flat, skip_next_flat, use_own, row0, tables):
    tall, broad = own_pad.shape
    rows = (tall - (PATCH - STRIDE)) // STRIDE
    cols = (broad - (PATCH - STRIDE)) // STRIDE
    assert cols % 2 == 0
    height = max(8, -(-cols // 8) * 8)
    both_t, cos_t, sin_t, inverse_t = tables
    band = pl.BlockSpec((pl.Element(PATCH), pl.Element(broad)), lambda i, *_: (i * STRIDE, 0))
    table = pl.BlockSpec((PATCH, PATCH), lambda i, *_: (0, 0))
    grid_spec = pltpu.PrefetchScalarGridSpec(
        num_scalar_prefetch=3,
        grid=(rows,),
        in_specs=[
            band, band, band, pl.BlockSpec((2 * PATCH, PATCH), lambda i, *_: (0, 0)), table, table,
            pl.BlockSpec((2 * PATCH, 2 * PATCH), lambda i, *_: (0, 0)),
        ],
        out_specs=pl.BlockSpec((1, height, 128), lambda i, *_: (i, 0, 0)),
        scratch_shapes=[
            pltpu.VMEM((4 * cols * PATCH, PATCH), jnp.bfloat16),
            pltpu.VMEM((4 * cols * PATCH, PATCH), jnp.float32),
            pltpu.VMEM((4 * cols * PATCH, PATCH), jnp.float32),
            pltpu.VMEM((cols * PATCH, PATCH), jnp.bfloat16),
            pltpu.VMEM((cols * PATCH, PATCH), jnp.bfloat16),
        ],
    )
    out = pl.pallas_call(
        functools.partial(_flow_kernel, cols=cols, row0=row0),
        grid_spec=grid_spec,
        out_shape=jax.ShapeDtypeStruct((rows, height, 128), jnp.float32),
        compiler_params=pltpu.CompilerParams(
            dimension_semantics=("arbitrary",), vmem_limit_bytes=48 * 1024 * 1024
        ),
    )(skip_flat, skip_next_flat, use_own.reshape(1), own_pad, prev_pad, next_pad, both_t, cos_t, sin_t, inverse_t)
    half = cols // 2
    first = jnp.repeat(jnp.transpose(out[:, :half, 0:2], (2, 0, 1)), 2, axis=2)
    second = jnp.repeat(jnp.transpose(out[:, half:cols, 0:2], (2, 0, 1)), 2, axis=2)
    return first, second


def gather_sections(value, axis):
    count = lax.axis_size(axis)
    spread = jnp.broadcast_to(value[None], (count,) + value.shape)
    return lax.all_to_all(spread, axis, 0, 0, tiled=True)


def earlier(values, steps, axis):
    width = values.shape[axis]
    widths = [(0, 0)] * values.ndim
    widths[axis] = (steps, 0)
    return lax.slice_in_dim(jnp.pad(values, widths), 0, width, axis=axis)


def later(values, steps, axis):
    width = values.shape[axis]
    widths = [(0, 0)] * values.ndim
    widths[axis] = (0, steps)
    return lax.slice_in_dim(jnp.pad(values, widths), steps, steps + width, axis=axis)


def relax(flow_field, weight, distance):
    near = (distance == 1).astype(jnp.float32)
    far = 1.0 - near
    diag = STIFFNESS + weight + later(weight * near, 1, 0) + later(weight * far, 2, 0)
    positions = jnp.zeros_like(flow_field)
    for sweep in range(RELAX):
        partner = near * earlier(positions, 1, 1) + far * earlier(positions, 2, 1)
        error = weight * (positions - partner - flow_field)
        gradient = (
            STIFFNESS * positions + error - later(error * near, 1, 1) - later(error * far, 2, 1)
        )
        positions = positions - RELAXATION * gradient / diag
    return positions


def body(images, skipped, patch_mask):
    index = lax.axis_index("sec")
    own_distance = jnp.where(index >= 2, 1 + skipped, 1)
    if lax.axis_size("sub") == 2 and lax.axis_size("tile") == 2:
        own_pad = extended_pairs(images, RIM)[0]
    else:
        own_pad = extended(images, (("sub", 1), ("tile", 2)), RIM)[0]
    skip_next = shifted(skipped, "sec", -1)
    use_own = (index == 0).astype(jnp.int32)
    rows_count = (own_pad.shape[0] - (PATCH - STRIDE)) // STRIDE
    if rows_count >= 8:
        extra = rows_count - 8
        sizes = [1, 2, 2, 3 + extra]
    else:
        sizes = [rows_count]
    offsets = [sum(sizes[:n]) for n in range(len(sizes))]
    cos_t, sin_t = dft_tables(PATCH)
    inverse_t = jnp.concatenate(
        [jnp.concatenate([cos_t, sin_t], axis=1), jnp.concatenate([-sin_t, cos_t], axis=1)], axis=0
    )
    tables = (jnp.concatenate([cos_t, sin_t], axis=0), cos_t, sin_t, inverse_t)
    skip_flat = skipped.reshape(-1)
    skip_next_flat = skip_next.reshape(-1)
    firsts, seconds = [], []
    for first_row, count in zip(offsets, sizes):
        start = first_row * STRIDE
        own_c = own_pad[start : start + count * STRIDE + PATCH - STRIDE]
        prev_c = shifted(own_c, "sec", 1)
        next_c = shifted(own_c, "sec", -1)
        first_c, second_c = pair_flows(
            own_c, prev_c, next_c, skip_flat, skip_next_flat, use_own, first_row, tables
        )
        firsts.append(first_c)
        seconds.append(second_c)
    first = jnp.concatenate(firsts, axis=1)
    second = jnp.concatenate(seconds, axis=1)
    first = jnp.where(skipped[0] == 0, first, 0.0)
    second = jnp.where(skip_next[0] == 1, second, 0.0)
    weight = patch_mask.astype(jnp.float32) * (index >= 1).astype(jnp.float32)
    stacked = jnp.concatenate(
        [first, second, weight, own_distance.astype(jnp.float32)], axis=0
    )
    every = jnp.moveaxis(gather_sections(stacked, "sec"), 0, 1)
    raw_all = every[0:2] + earlier(every[2:4], 1, 1)
    flow_all = raw_all * every[4]
    positions_all = relax(flow_all, every[4], every[5])
    flow_field = lax.dynamic_slice_in_dim(flow_all, index, 1, 1)
    positions = lax.dynamic_slice_in_dim(positions_all, index, 1, 1)
    return (flow_field, positions)


def solution(mesh):
    placed = (
        P(("groups", "sec"), "sub", "tile"),
        P(("groups", "sec"), "sub", "tile"),
        P(("groups", "sec"), "sub", "tile"),
    )
    return jax.shard_map(
        body,
        mesh=mesh,
        in_specs=placed,
        out_specs=(
            P(None, ("groups", "sec"), "sub", "tile"),
            P(None, ("groups", "sec"), "sub", "tile"),
        ),
        check_vma=False,
    )
```

```python
import functools
import math

import jax
import jax.numpy as jnp
from jax import lax
from jax.experimental import pallas as pl
from jax.experimental.pallas import tpu as pltpu
from jax.sharding import PartitionSpec as P

PATCH = 160
STRIDE = 128
RELAX = 6
RIM = 16


SHARPNESS = 48.0
STIFFNESS = 0.25
RELAXATION = 0.8
EPSILON = 1e-05


def shifted(value, axis, steps):
    count = lax.axis_size(axis)
    first, last = (max(0, -steps), min(count, count - steps))
    return lax.ppermute(value, axis, [(source, source + steps) for source in range(first, last)])


def _strip_send(strip, dim):
    return jnp.swapaxes(strip, 1, 2) if dim == 2 else strip


def _strip_recv(strip, dim):
    return jnp.swapaxes(strip, 1, 2) if dim == 2 else strip


def extended(block, sides, width):
    for axis, dim in sides:
        count = lax.axis_size(axis)
        top = lax.slice_in_dim(block, 0, width, axis=dim)
        bottom = lax.slice_in_dim(block, block.shape[dim] - width, None, axis=dim)
        if count == 2:
            index = lax.axis_index(axis)
            send = _strip_send(jnp.where(index == 0, bottom, top), dim)
            got = _strip_recv(lax.ppermute(send, axis, [(0, 1), (1, 0)]), dim)
            low = jnp.where(index == 1, got, jnp.zeros_like(got))
            high = jnp.where(index == 0, got, jnp.zeros_like(got))
        else:
            forward = [(i, i + 1) for i in range(count - 1)]
            backward = [(target, source) for source, target in forward]
            low = _strip_recv(lax.ppermute(_strip_send(bottom, dim), axis, forward), dim)
            high = _strip_recv(lax.ppermute(_strip_send(top, dim), axis, backward), dim)
        block = jnp.concatenate([low, block, high], axis=dim)
    return block


def extended_pairs(block, width):
    sub = lax.axis_index("sub")
    tile = lax.axis_index("tile")
    swap = [(0, 1), (1, 0)]
    rows_send = jnp.where(
        sub == 0, block[:, -width:, :], block[:, :width, :]
    )
    cols_send = jnp.swapaxes(jnp.where(tile == 0, block[:, :, -width:], block[:, :, :width]), 1, 2)
    corner_rows = jnp.where(sub == 0, block[:, -width:, :], block[:, :width, :])
    corner_send = jnp.where(tile == 0, corner_rows[:, :, -width:], corner_rows[:, :, :width])
    rows_got = lax.ppermute(rows_send, "sub", swap)
    cols_got = jnp.swapaxes(lax.ppermute(cols_send, "tile", swap), 1, 2)
    corner_got = lax.ppermute(corner_send, ("tile", "sub"), [(0, 3), (3, 0), (1, 2), (2, 1)])

    def keep(flag, value):
        return jnp.where(flag, value, jnp.zeros_like(value))

    top, bottom = sub == 1, sub == 0
    left, right = tile == 1, tile == 0
    middle = jnp.concatenate([keep(left, cols_got), block, keep(right, cols_got)], axis=2)
    upper = jnp.concatenate(
        [keep(top & left, corner_got), keep(top, rows_got), keep(top & right, corner_got)], axis=2
    )
    lower = jnp.concatenate(
        [keep(bottom & left, corner_got), keep(bottom, rows_got), keep(bottom & right, corner_got)],
        axis=2,
    )
    return jnp.concatenate([upper, middle, lower], axis=1)


def dft_tables(patch):
    index = jnp.arange(patch, dtype=jnp.int32)
    product = index[:, None] * index[None, :] % patch
    angle = product.astype(jnp.float32) * (2.0 * math.pi / patch)
    return (jnp.cos(angle).astype(jnp.bfloat16), (-jnp.sin(angle)).astype(jnp.bfloat16))


def _sum_all(x):
    return jnp.sum(jnp.sum(x, axis=1, keepdims=True), axis=0, keepdims=True)


def _flow_kernel(
    skip_ref, skip_next_ref, flag_ref, own_ref, prev_ref, next_ref, cs_ref, c_ref, s_ref, inv_ref,
    out_ref, half_ref, x_ref, y_ref, br_ref, bi_ref,
    *, cols, row0,
):
    f32, bf16 = jnp.float32, jnp.bfloat16
    p = PATCH
    pairs = cols // 2
    i = pl.program_id(0) + row0
    cos_t = c_ref[...]
    sin_t = s_ref[...]
    both_t = cs_ref[...]
    inverse_t = inv_ref[...]
    size = float(p * p)

    def window(ref, j):
        return ref[:, j * STRIDE : j * STRIDE + p]

    use_own = flag_ref[0] == 1
    blocks = []
    for k in range(pairs):
        left, right = 2 * k, 2 * k + 1
        first_near = skip_ref[i * cols + left] == 0
        blocks.append(jnp.where(first_near, window(own_ref, left), window(own_ref, right)))
        blocks.append(jnp.where(first_near, window(prev_ref, left), window(prev_ref, right)))
    for k in range(pairs):
        left, right = 2 * k, 2 * k + 1
        second_far = skip_next_ref[i * cols + right] == 1
        blocks.append(jnp.where(second_far, window(next_ref, right), window(next_ref, left)))
        col_prev = jnp.where(second_far, window(prev_ref, right), window(prev_ref, left))
        col_own = jnp.where(second_far, window(own_ref, right), window(own_ref, left))
        blocks.append(jnp.where(use_own, col_own, col_prev))

    for t, blk in enumerate(blocks):
        x = blk.astype(f32)
        centered = x - _sum_all(x) / size
        spread = _sum_all(centered * centered) / size
        normed = (centered * lax.rsqrt(spread + EPSILON)).astype(bf16)
        half_ref[2 * p * t : 2 * p * (t + 1), :] = jnp.dot(
            both_t, normed, preferred_element_type=f32
        ).astype(bf16)
    halves = half_ref[...]
    x_ref[...] = jnp.dot(halves, cos_t, preferred_element_type=f32)
    y_ref[...] = jnp.dot(halves, sin_t, preferred_element_type=f32)

    def spectrum(t):
        base = 2 * p * t
        re = x_ref[base : base + p, :] - y_ref[base + p : base + 2 * p, :]
        im = y_ref[base : base + p, :] + x_ref[base + p : base + 2 * p, :]
        return re, im

    for c in range(cols):
        o_re, o_im = spectrum(2 * c)
        t_re, t_im = spectrum(2 * c + 1)
        c_re = (o_re * t_re + o_im * t_im).astype(bf16)
        c_im = (o_re * t_im - o_im * t_re).astype(bf16)
        back = jnp.dot(
            inverse_t, jnp.concatenate([c_re, c_im], axis=0), preferred_element_type=f32
        ).astype(bf16)
        br_ref[p * c : p * (c + 1), :] = back[:p]
        bi_ref[p * c : p * (c + 1), :] = back[p:]

    corr = (
        jnp.dot(br_ref[...], cos_t, preferred_element_type=f32)
        + jnp.dot(bi_ref[...], sin_t, preferred_element_type=f32)
    ) / float(p) ** 4
    w = jnp.exp(SHARPNESS * corr)
    u_col = lax.broadcasted_iota(jnp.int32, (cols * p, 1), 0) % p
    off_col = jnp.where(u_col < p // 2, u_col, u_col - p).astype(f32)
    u_row = lax.broadcasted_iota(jnp.int32, (1, p), 1)
    off_row = jnp.where(u_row < p // 2, u_row, u_row - p).astype(f32)
    rows_sum = jnp.sum(w, axis=1, keepdims=True)
    total = jnp.sum(rows_sum.reshape(cols, p, 1), axis=1)
    along_rows = jnp.sum((rows_sum * off_col).reshape(cols, p, 1), axis=1)
    cols_sum = jnp.sum(w.reshape(cols, p, p), axis=1)
    along_cols = jnp.sum(cols_sum * off_row, axis=1, keepdims=True)
    ar = along_rows / total / float(RIM)
    ac = along_cols / total / float(RIM)
    lane = lax.broadcasted_iota(jnp.int32, (cols, 128), 1)
    res = jnp.where(lane == 0, ar, jnp.where(lane == 1, ac, 0.0))
    height = out_ref.shape[1]
    if height > cols:
        res = jnp.concatenate([res, jnp.zeros((height - cols, 128), f32)], axis=0)
    out_ref[0] = res


def pair_flows(own_pad, prev_pad, next_pad, skip_flat, skip_next_flat, use_own, row0, tables):
    tall, broad = own_pad.shape
    rows = (tall - (PATCH - STRIDE)) // STRIDE
    cols = (broad - (PATCH - STRIDE)) // STRIDE
    assert cols % 2 == 0
    height = max(8, -(-cols // 8) * 8)
    both_t, cos_t, sin_t, inverse_t = tables
    band = pl.BlockSpec((pl.Element(PATCH), pl.Element(broad)), lambda i, *_: (i * STRIDE, 0))
    table = pl.BlockSpec((PATCH, PATCH), lambda i, *_: (0, 0))
    grid_spec = pltpu.PrefetchScalarGridSpec(
        num_scalar_prefetch=3,
        grid=(rows,),
        in_specs=[
            band, band, band, pl.BlockSpec((2 * PATCH, PATCH), lambda i, *_: (0, 0)), table, table,
            pl.BlockSpec((2 * PATCH, 2 * PATCH), lambda i, *_: (0, 0)),
        ],
        out_specs=pl.BlockSpec((1, height, 128), lambda i, *_: (i, 0, 0)),
        scratch_shapes=[
            pltpu.VMEM((4 * cols * PATCH, PATCH), jnp.bfloat16),
            pltpu.VMEM((4 * cols * PATCH, PATCH), jnp.float32),
            pltpu.VMEM((4 * cols * PATCH, PATCH), jnp.float32),
            pltpu.VMEM((cols * PATCH, PATCH), jnp.bfloat16),
            pltpu.VMEM((cols * PATCH, PATCH), jnp.bfloat16),
        ],
    )
    out = pl.pallas_call(
        functools.partial(_flow_kernel, cols=cols, row0=row0),
        grid_spec=grid_spec,
        out_shape=jax.ShapeDtypeStruct((rows, height, 128), jnp.float32),
        compiler_params=pltpu.CompilerParams(
            dimension_semantics=("arbitrary",), vmem_limit_bytes=48 * 1024 * 1024
        ),
    )(skip_flat, skip_next_flat, use_own.reshape(1), own_pad, prev_pad, next_pad, both_t, cos_t, sin_t, inverse_t)
    half = cols // 2
    first = jnp.repeat(jnp.transpose(out[:, :half, 0:2], (2, 0, 1)), 2, axis=2)
    second = jnp.repeat(jnp.transpose(out[:, half:cols, 0:2], (2, 0, 1)), 2, axis=2)
    return first, second


def gather_sections(value, axis):
    count = lax.axis_size(axis)
    spread = jnp.broadcast_to(value[None], (count,) + value.shape)
    return lax.all_to_all(spread, axis, 0, 0, tiled=True)


def earlier(values, steps, axis):
    width = values.shape[axis]
    widths = [(0, 0)] * values.ndim
    widths[axis] = (steps, 0)
    return lax.slice_in_dim(jnp.pad(values, widths), 0, width, axis=axis)


def later(values, steps, axis):
    width = values.shape[axis]
    widths = [(0, 0)] * values.ndim
    widths[axis] = (0, steps)
    return lax.slice_in_dim(jnp.pad(values, widths), steps, steps + width, axis=axis)


def relax(flow_field, weight, distance):
    near = (distance == 1).astype(jnp.float32)
    far = 1.0 - near
    diag = STIFFNESS + weight + later(weight * near, 1, 0) + later(weight * far, 2, 0)
    positions = jnp.zeros_like(flow_field)
    for sweep in range(RELAX):
        partner = near * earlier(positions, 1, 1) + far * earlier(positions, 2, 1)
        error = weight * (positions - partner - flow_field)
        gradient = (
            STIFFNESS * positions + error - later(error * near, 1, 1) - later(error * far, 2, 1)
        )
        positions = positions - RELAXATION * gradient / diag
    return positions


def body(images, skipped, patch_mask):
    index = lax.axis_index("sec")
    own_distance = jnp.where(index >= 2, 1 + skipped, 1)
    if lax.axis_size("sub") == 2 and lax.axis_size("tile") == 2:
        own_pad = extended_pairs(images, RIM)[0]
    else:
        own_pad = extended(images, (("sub", 1), ("tile", 2)), RIM)[0]
    skip_next = shifted(skipped, "sec", -1)
    use_own = (index == 0).astype(jnp.int32)
    rows_count = (own_pad.shape[0] - (PATCH - STRIDE)) // STRIDE
    if rows_count >= 8:
        sizes = [2, (rows_count - 2) // 2, rows_count - 2 - (rows_count - 2) // 2]
    else:
        sizes = [rows_count]
    offsets = [sum(sizes[:n]) for n in range(len(sizes))]
    cos_t, sin_t = dft_tables(PATCH)
    inverse_t = jnp.concatenate(
        [jnp.concatenate([cos_t, sin_t], axis=1), jnp.concatenate([-sin_t, cos_t], axis=1)], axis=0
    )
    tables = (jnp.concatenate([cos_t, sin_t], axis=0), cos_t, sin_t, inverse_t)
    skip_flat = skipped.reshape(-1)
    skip_next_flat = skip_next.reshape(-1)
    firsts, seconds = [], []
    for first_row, count in zip(offsets, sizes):
        start = first_row * STRIDE
        own_c = own_pad[start : start + count * STRIDE + PATCH - STRIDE]
        prev_c = shifted(own_c, "sec", 1)
        next_c = shifted(own_c, "sec", -1)
        first_c, second_c = pair_flows(
            own_c, prev_c, next_c, skip_flat, skip_next_flat, use_own, first_row, tables
        )
        firsts.append(first_c)
        seconds.append(second_c)
    first = jnp.concatenate(firsts, axis=1)
    second = jnp.concatenate(seconds, axis=1)
    first = jnp.where(skipped[0] == 0, first, 0.0)
    second = jnp.where(skip_next[0] == 1, second, 0.0)
    weight = patch_mask.astype(jnp.float32) * (index >= 1).astype(jnp.float32)
    stacked = jnp.concatenate(
        [first, second, weight, own_distance.astype(jnp.float32)], axis=0
    )
    every = jnp.moveaxis(gather_sections(stacked, "sec"), 0, 1)
    raw_all = every[0:2] + earlier(every[2:4], 1, 1)
    flow_all = raw_all * every[4]
    positions_all = relax(flow_all, every[4], every[5])
    flow_field = lax.dynamic_slice_in_dim(flow_all, index, 1, 1)
    positions = lax.dynamic_slice_in_dim(positions_all, index, 1, 1)
    return (flow_field, positions)


def solution(mesh):
    placed = (
        P(("groups", "sec"), "sub", "tile"),
        P(("groups", "sec"), "sub", "tile"),
        P(("groups", "sec"), "sub", "tile"),
    )
    return jax.shard_map(
        body,
        mesh=mesh,
        in_specs=placed,
        out_specs=(
            P(None, ("groups", "sec"), "sub", "tile"),
            P(None, ("groups", "sec"), "sub", "tile"),
        ),
        check_vma=False,
    )
```

```python
import functools
import math

import jax
import jax.numpy as jnp
from jax import lax
from jax.experimental import pallas as pl
from jax.experimental.pallas import tpu as pltpu
from jax.sharding import PartitionSpec as P

PATCH = 160
STRIDE = 128
RELAX = 6
RIM = 16


SHARPNESS = 48.0
STIFFNESS = 0.25
RELAXATION = 0.8
EPSILON = 1e-05


def shifted(value, axis, steps):
    count = lax.axis_size(axis)
    first, last = (max(0, -steps), min(count, count - steps))
    return lax.ppermute(value, axis, [(source, source + steps) for source in range(first, last)])


def _strip_send(strip, dim):
    return jnp.swapaxes(strip, 1, 2) if dim == 2 else strip


def _strip_recv(strip, dim):
    return jnp.swapaxes(strip, 1, 2) if dim == 2 else strip


def extended(block, sides, width):
    for axis, dim in sides:
        count = lax.axis_size(axis)
        top = lax.slice_in_dim(block, 0, width, axis=dim)
        bottom = lax.slice_in_dim(block, block.shape[dim] - width, None, axis=dim)
        if count == 2:
            index = lax.axis_index(axis)
            send = _strip_send(jnp.where(index == 0, bottom, top), dim)
            got = _strip_recv(lax.ppermute(send, axis, [(0, 1), (1, 0)]), dim)
            low = jnp.where(index == 1, got, jnp.zeros_like(got))
            high = jnp.where(index == 0, got, jnp.zeros_like(got))
        else:
            forward = [(i, i + 1) for i in range(count - 1)]
            backward = [(target, source) for source, target in forward]
            low = _strip_recv(lax.ppermute(_strip_send(bottom, dim), axis, forward), dim)
            high = _strip_recv(lax.ppermute(_strip_send(top, dim), axis, backward), dim)
        block = jnp.concatenate([low, block, high], axis=dim)
    return block


def extended_pairs(block, width):
    sub = lax.axis_index("sub")
    tile = lax.axis_index("tile")
    swap = [(0, 1), (1, 0)]
    rows_send = jnp.where(
        sub == 0, block[:, -width:, :], block[:, :width, :]
    )
    cols_send = jnp.swapaxes(jnp.where(tile == 0, block[:, :, -width:], block[:, :, :width]), 1, 2)
    corner_rows = jnp.where(sub == 0, block[:, -width:, :], block[:, :width, :])
    corner_send = jnp.where(tile == 0, corner_rows[:, :, -width:], corner_rows[:, :, :width])
    rows_got = lax.ppermute(rows_send, "sub", swap)
    cols_got = jnp.swapaxes(lax.ppermute(cols_send, "tile", swap), 1, 2)
    corner_got = lax.ppermute(corner_send, ("tile", "sub"), [(0, 3), (3, 0), (1, 2), (2, 1)])

    def keep(flag, value):
        return jnp.where(flag, value, jnp.zeros_like(value))

    top, bottom = sub == 1, sub == 0
    left, right = tile == 1, tile == 0
    middle = jnp.concatenate([keep(left, cols_got), block, keep(right, cols_got)], axis=2)
    upper = jnp.concatenate(
        [keep(top & left, corner_got), keep(top, rows_got), keep(top & right, corner_got)], axis=2
    )
    lower = jnp.concatenate(
        [keep(bottom & left, corner_got), keep(bottom, rows_got), keep(bottom & right, corner_got)],
        axis=2,
    )
    return jnp.concatenate([upper, middle, lower], axis=1)


def dft_tables(patch):
    index = jnp.arange(patch, dtype=jnp.int32)
    product = index[:, None] * index[None, :] % patch
    angle = product.astype(jnp.float32) * (2.0 * math.pi / patch)
    return (jnp.cos(angle).astype(jnp.bfloat16), (-jnp.sin(angle)).astype(jnp.bfloat16))


def _sum_all(x):
    return jnp.sum(jnp.sum(x, axis=1, keepdims=True), axis=0, keepdims=True)


def _flow_kernel(
    skip_ref, skip_next_ref, flag_ref, own_ref, prev_ref, next_ref, cs_ref, c_ref, s_ref, inv_ref,
    out_ref, half_ref, x_ref, y_ref, br_ref, bi_ref,
    *, cols, row0,
):
    f32, bf16 = jnp.float32, jnp.bfloat16
    p = PATCH
    pairs = cols // 2
    i = pl.program_id(0) + row0
    cos_t = c_ref[...]
    sin_t = s_ref[...]
    both_t = cs_ref[...]
    inverse_t = inv_ref[...]
    size = float(p * p)

    def window(ref, j):
        return ref[:, j * STRIDE : j * STRIDE + p]

    use_own = flag_ref[0] == 1
    blocks = []
    for k in range(pairs):
        left, right = 2 * k, 2 * k + 1
        first_near = skip_ref[i * cols + left] == 0
        blocks.append(jnp.where(first_near, window(own_ref, left), window(own_ref, right)))
        blocks.append(jnp.where(first_near, window(prev_ref, left), window(prev_ref, right)))
    for k in range(pairs):
        left, right = 2 * k, 2 * k + 1
        second_far = skip_next_ref[i * cols + right] == 1
        blocks.append(jnp.where(second_far, window(next_ref, right), window(next_ref, left)))
        col_prev = jnp.where(second_far, window(prev_ref, right), window(prev_ref, left))
        col_own = jnp.where(second_far, window(own_ref, right), window(own_ref, left))
        blocks.append(jnp.where(use_own, col_own, col_prev))

    for t, blk in enumerate(blocks):
        x = blk.astype(f32)
        centered = x - _sum_all(x) / size
        spread = _sum_all(centered * centered) / size
        normed = (centered * lax.rsqrt(spread + EPSILON)).astype(bf16)
        half_ref[2 * p * t : 2 * p * (t + 1), :] = jnp.dot(
            both_t, normed, preferred_element_type=f32
        ).astype(bf16)
    halves = half_ref[...]
    x_ref[...] = jnp.dot(halves, cos_t, preferred_element_type=f32)
    y_ref[...] = jnp.dot(halves, sin_t, preferred_element_type=f32)

    def spectrum(t):
        base = 2 * p * t
        re = x_ref[base : base + p, :] - y_ref[base + p : base + 2 * p, :]
        im = y_ref[base : base + p, :] + x_ref[base + p : base + 2 * p, :]
        return re, im

    for c in range(cols):
        o_re, o_im = spectrum(2 * c)
        t_re, t_im = spectrum(2 * c + 1)
        c_re = (o_re * t_re + o_im * t_im).astype(bf16)
        c_im = (o_re * t_im - o_im * t_re).astype(bf16)
        back = jnp.dot(
            inverse_t, jnp.concatenate([c_re, c_im], axis=0), preferred_element_type=f32
        ).astype(bf16)
        br_ref[p * c : p * (c + 1), :] = back[:p]
        bi_ref[p * c : p * (c + 1), :] = back[p:]

    corr = (
        jnp.dot(br_ref[...], cos_t, preferred_element_type=f32)
        + jnp.dot(bi_ref[...], sin_t, preferred_element_type=f32)
    ) / float(p) ** 4
    w = jnp.exp(SHARPNESS * corr)
    u_col = lax.broadcasted_iota(jnp.int32, (cols * p, 1), 0) % p
    off_col = jnp.where(u_col < p // 2, u_col, u_col - p).astype(f32)
    u_row = lax.broadcasted_iota(jnp.int32, (1, p), 1)
    off_row = jnp.where(u_row < p // 2, u_row, u_row - p).astype(f32)
    rows_sum = jnp.sum(w, axis=1, keepdims=True)
    total = jnp.sum(rows_sum.reshape(cols, p, 1), axis=1)
    along_rows = jnp.sum((rows_sum * off_col).reshape(cols, p, 1), axis=1)
    cols_sum = jnp.sum(w.reshape(cols, p, p), axis=1)
    along_cols = jnp.sum(cols_sum * off_row, axis=1, keepdims=True)
    ar = along_rows / total / float(RIM)
    ac = along_cols / total / float(RIM)
    lane = lax.broadcasted_iota(jnp.int32, (cols, 128), 1)
    res = jnp.where(lane == 0, ar, jnp.where(lane == 1, ac, 0.0))
    height = out_ref.shape[1]
    if height > cols:
        res = jnp.concatenate([res, jnp.zeros((height - cols, 128), f32)], axis=0)
    out_ref[0] = res


def pair_flows(own_pad, prev_pad, next_pad, skip_flat, skip_next_flat, use_own, row0, tables):
    tall, broad = own_pad.shape
    rows = (tall - (PATCH - STRIDE)) // STRIDE
    cols = (broad - (PATCH - STRIDE)) // STRIDE
    assert cols % 2 == 0
    height = max(8, -(-cols // 8) * 8)
    both_t, cos_t, sin_t, inverse_t = tables
    band = pl.BlockSpec((pl.Element(PATCH), pl.Element(broad)), lambda i, *_: (i * STRIDE, 0))
    table = pl.BlockSpec((PATCH, PATCH), lambda i, *_: (0, 0))
    grid_spec = pltpu.PrefetchScalarGridSpec(
        num_scalar_prefetch=3,
        grid=(rows,),
        in_specs=[
            band, band, band, pl.BlockSpec((2 * PATCH, PATCH), lambda i, *_: (0, 0)), table, table,
            pl.BlockSpec((2 * PATCH, 2 * PATCH), lambda i, *_: (0, 0)),
        ],
        out_specs=pl.BlockSpec((1, height, 128), lambda i, *_: (i, 0, 0)),
        scratch_shapes=[
            pltpu.VMEM((4 * cols * PATCH, PATCH), jnp.bfloat16),
            pltpu.VMEM((4 * cols * PATCH, PATCH), jnp.float32),
            pltpu.VMEM((4 * cols * PATCH, PATCH), jnp.float32),
            pltpu.VMEM((cols * PATCH, PATCH), jnp.bfloat16),
            pltpu.VMEM((cols * PATCH, PATCH), jnp.bfloat16),
        ],
    )
    out = pl.pallas_call(
        functools.partial(_flow_kernel, cols=cols, row0=row0),
        grid_spec=grid_spec,
        out_shape=jax.ShapeDtypeStruct((rows, height, 128), jnp.float32),
        compiler_params=pltpu.CompilerParams(
            dimension_semantics=("arbitrary",), vmem_limit_bytes=48 * 1024 * 1024
        ),
    )(skip_flat, skip_next_flat, use_own.reshape(1), own_pad, prev_pad, next_pad, both_t, cos_t, sin_t, inverse_t)
    half = cols // 2
    first = jnp.repeat(jnp.transpose(out[:, :half, 0:2], (2, 0, 1)), 2, axis=2)
    second = jnp.repeat(jnp.transpose(out[:, half:cols, 0:2], (2, 0, 1)), 2, axis=2)
    return first, second


def gather_sections(value, axis):
    count = lax.axis_size(axis)
    spread = jnp.broadcast_to(value[None], (count,) + value.shape)
    return lax.all_to_all(spread, axis, 0, 0, tiled=True)


def earlier(values, steps, axis):
    width = values.shape[axis]
    widths = [(0, 0)] * values.ndim
    widths[axis] = (steps, 0)
    return lax.slice_in_dim(jnp.pad(values, widths), 0, width, axis=axis)


def later(values, steps, axis):
    width = values.shape[axis]
    widths = [(0, 0)] * values.ndim
    widths[axis] = (0, steps)
    return lax.slice_in_dim(jnp.pad(values, widths), steps, steps + width, axis=axis)


def relax(flow_field, weight, distance):
    near = (distance == 1).astype(jnp.float32)
    far = 1.0 - near
    diag = STIFFNESS + weight + later(weight * near, 1, 0) + later(weight * far, 2, 0)
    positions = jnp.zeros_like(flow_field)
    for sweep in range(RELAX):
        partner = near * earlier(positions, 1, 1) + far * earlier(positions, 2, 1)
        error = weight * (positions - partner - flow_field)
        gradient = (
            STIFFNESS * positions + error - later(error * near, 1, 1) - later(error * far, 2, 1)
        )
        positions = positions - RELAXATION * gradient / diag
    return positions


def body(images, skipped, patch_mask):
    index = lax.axis_index("sec")
    own_distance = jnp.where(index >= 2, 1 + skipped, 1)
    if lax.axis_size("sub") == 2 and lax.axis_size("tile") == 2:
        own_pad = extended_pairs(images, RIM)[0]
    else:
        own_pad = extended(images, (("sub", 1), ("tile", 2)), RIM)[0]
    use_own = (index == 0).astype(jnp.int32)
    rows_count = (own_pad.shape[0] - (PATCH - STRIDE)) // STRIDE
    chunks = max(n for n in (1, 2, 4) if rows_count % n == 0)
    per = rows_count // chunks
    cos_t, sin_t = dft_tables(PATCH)
    inverse_t = jnp.concatenate(
        [jnp.concatenate([cos_t, sin_t], axis=1), jnp.concatenate([-sin_t, cos_t], axis=1)], axis=0
    )
    tables = (jnp.concatenate([cos_t, sin_t], axis=0), cos_t, sin_t, inverse_t)
    skip_flat = skipped.reshape(-1)
    broad = own_pad.shape[1]
    cols_count = (broad - (PATCH - STRIDE)) // STRIDE
    riding = rows_count <= 16
    if not riding:
        skip_next = shifted(skipped, "sec", -1)
    firsts, seconds = [], []
    for c in range(chunks):
        start = c * per * STRIDE
        own_c = own_pad[start : start + per * STRIDE + PATCH - STRIDE]
        if c == 0 and riding:
            flags = jnp.zeros((16, broad), jnp.bfloat16)
            flags = lax.dynamic_update_slice(flags, skipped[0].astype(jnp.bfloat16), (0, 0))
            own_c = jnp.concatenate([own_c, flags], axis=0)
        prev_c = shifted(own_c, "sec", 1)
        next_c = shifted(own_c, "sec", -1)
        if c == 0 and riding:
            tall_c = own_c.shape[0] - 16
            skip_next = next_c[tall_c : tall_c + rows_count, :cols_count].astype(jnp.int32)[None]
        skip_next_flat = skip_next.reshape(-1)
        first_c, second_c = pair_flows(
            own_c, prev_c, next_c, skip_flat, skip_next_flat, use_own, c * per, tables
        )
        firsts.append(first_c)
        seconds.append(second_c)
    first = jnp.concatenate(firsts, axis=1)
    second = jnp.concatenate(seconds, axis=1)
    first = jnp.where(skipped[0] == 0, first, 0.0)
    second = jnp.where(skip_next[0] == 1, second, 0.0)
    weight = patch_mask.astype(jnp.float32) * (index >= 1).astype(jnp.float32)
    stacked = jnp.concatenate(
        [first, second, weight, own_distance.astype(jnp.float32)], axis=0
    )
    every = jnp.moveaxis(gather_sections(stacked, "sec"), 0, 1)
    raw_all = every[0:2] + earlier(every[2:4], 1, 1)
    flow_all = raw_all * every[4]
    positions_all = relax(flow_all, every[4], every[5])
    flow_field = lax.dynamic_slice_in_dim(flow_all, index, 1, 1)
    positions = lax.dynamic_slice_in_dim(positions_all, index, 1, 1)
    return (flow_field, positions)


def solution(mesh):
    placed = (
        P(("groups", "sec"), "sub", "tile"),
        P(("groups", "sec"), "sub", "tile"),
        P(("groups", "sec"), "sub", "tile"),
    )
    return jax.shard_map(
        body,
        mesh=mesh,
        in_specs=placed,
        out_specs=(
            P(None, ("groups", "sec"), "sub", "tile"),
            P(None, ("groups", "sec"), "sub", "tile"),
        ),
        check_vma=False,
    )
```

```python
import functools
import math

import jax
import jax.numpy as jnp
from jax import lax
from jax.experimental import pallas as pl
from jax.experimental.pallas import tpu as pltpu
from jax.sharding import PartitionSpec as P

PATCH = 160
STRIDE = 128
RELAX = 6
RIM = 16


SHARPNESS = 48.0
STIFFNESS = 0.25
RELAXATION = 0.8
EPSILON = 1e-05


def shifted(value, axis, steps):
    count = lax.axis_size(axis)
    first, last = (max(0, -steps), min(count, count - steps))
    return lax.ppermute(value, axis, [(source, source + steps) for source in range(first, last)])


def _strip_send(strip, dim):
    return jnp.swapaxes(strip, 1, 2) if dim == 2 else strip


def _strip_recv(strip, dim):
    return jnp.swapaxes(strip, 1, 2) if dim == 2 else strip


def extended(block, sides, width):
    for axis, dim in sides:
        count = lax.axis_size(axis)
        top = lax.slice_in_dim(block, 0, width, axis=dim)
        bottom = lax.slice_in_dim(block, block.shape[dim] - width, None, axis=dim)
        if count == 2:
            index = lax.axis_index(axis)
            send = _strip_send(jnp.where(index == 0, bottom, top), dim)
            got = _strip_recv(lax.ppermute(send, axis, [(0, 1), (1, 0)]), dim)
            low = jnp.where(index == 1, got, jnp.zeros_like(got))
            high = jnp.where(index == 0, got, jnp.zeros_like(got))
        else:
            forward = [(i, i + 1) for i in range(count - 1)]
            backward = [(target, source) for source, target in forward]
            low = _strip_recv(lax.ppermute(_strip_send(bottom, dim), axis, forward), dim)
            high = _strip_recv(lax.ppermute(_strip_send(top, dim), axis, backward), dim)
        block = jnp.concatenate([low, block, high], axis=dim)
    return block


def extended_pairs(block, width):
    sub = lax.axis_index("sub")
    tile = lax.axis_index("tile")
    swap = [(0, 1), (1, 0)]
    rows_send = jnp.where(
        sub == 0, block[:, -width:, :], block[:, :width, :]
    )
    cols_send = jnp.swapaxes(jnp.where(tile == 0, block[:, :, -width:], block[:, :, :width]), 1, 2)
    corner_rows = jnp.where(sub == 0, block[:, -width:, :], block[:, :width, :])
    corner_send = jnp.where(tile == 0, corner_rows[:, :, -width:], corner_rows[:, :, :width])
    rows_got = lax.ppermute(rows_send, "sub", swap)
    cols_got = jnp.swapaxes(lax.ppermute(cols_send, "tile", swap), 1, 2)
    corner_got = lax.ppermute(corner_send, ("tile", "sub"), [(0, 3), (3, 0), (1, 2), (2, 1)])

    def keep(flag, value):
        return jnp.where(flag, value, jnp.zeros_like(value))

    top, bottom = sub == 1, sub == 0
    left, right = tile == 1, tile == 0
    middle = jnp.concatenate([keep(left, cols_got), block, keep(right, cols_got)], axis=2)
    upper = jnp.concatenate(
        [keep(top & left, corner_got), keep(top, rows_got), keep(top & right, corner_got)], axis=2
    )
    lower = jnp.concatenate(
        [keep(bottom & left, corner_got), keep(bottom, rows_got), keep(bottom & right, corner_got)],
        axis=2,
    )
    return jnp.concatenate([upper, middle, lower], axis=1)


def dft_tables(patch):
    index = jnp.arange(patch, dtype=jnp.int32)
    product = index[:, None] * index[None, :] % patch
    angle = product.astype(jnp.float32) * (2.0 * math.pi / patch)
    return (jnp.cos(angle).astype(jnp.bfloat16), (-jnp.sin(angle)).astype(jnp.bfloat16))


def _sum_all(x):
    return jnp.sum(jnp.sum(x, axis=1, keepdims=True), axis=0, keepdims=True)


def _flow_kernel(
    skip_ref, skip_next_ref, flag_ref, own_ref, prev_ref, next_ref, cs_ref, c_ref, s_ref, inv_ref,
    out_ref, half_ref, imag_ref, x_ref, y_ref, br_ref, bi_ref,
    *, cols, row0,
):
    f32, bf16 = jnp.float32, jnp.bfloat16
    p = PATCH
    pairs = cols // 2
    i = pl.program_id(0) + row0
    cos_t = c_ref[...]
    sin_t = s_ref[...]
    both_t = cs_ref[...]
    inverse_t = inv_ref[...]
    size = float(p * p)

    def window(ref, j):
        return ref[:, j * STRIDE : j * STRIDE + p]

    use_own = flag_ref[0] == 1
    blocks = []
    for k in range(pairs):
        left, right = 2 * k, 2 * k + 1
        first_near = skip_ref[i * cols + left] == 0
        blocks.append(jnp.where(first_near, window(own_ref, left), window(own_ref, right)))
        blocks.append(jnp.where(first_near, window(prev_ref, left), window(prev_ref, right)))
    for k in range(pairs):
        left, right = 2 * k, 2 * k + 1
        second_far = skip_next_ref[i * cols + right] == 1
        blocks.append(jnp.where(second_far, window(next_ref, right), window(next_ref, left)))
        col_prev = jnp.where(second_far, window(prev_ref, right), window(prev_ref, left))
        col_own = jnp.where(second_far, window(own_ref, right), window(own_ref, left))
        blocks.append(jnp.where(use_own, col_own, col_prev))

    for t, blk in enumerate(blocks):
        x = blk.astype(f32)
        centered = x - _sum_all(x) / size
        spread = _sum_all(centered * centered) / size
        normed = (centered * lax.rsqrt(spread + EPSILON)).astype(bf16)
        half = jnp.dot(both_t, normed, preferred_element_type=f32).astype(bf16)
        half_ref[p * t : p * (t + 1), :] = half[:p]
        imag_ref[p * t : p * (t + 1), :] = half[p:]
    h_re = half_ref[...]
    h_im = imag_ref[...]
    x_ref[...] = jnp.dot(h_re, cos_t, preferred_element_type=f32) - jnp.dot(
        h_im, sin_t, preferred_element_type=f32
    )
    y_ref[...] = jnp.dot(h_re, sin_t, preferred_element_type=f32) + jnp.dot(
        h_im, cos_t, preferred_element_type=f32
    )

    def spectrum(t):
        return x_ref[p * t : p * (t + 1), :], y_ref[p * t : p * (t + 1), :]

    for c in range(cols):
        o_re, o_im = spectrum(2 * c)
        t_re, t_im = spectrum(2 * c + 1)
        c_re = (o_re * t_re + o_im * t_im).astype(bf16)
        c_im = (o_re * t_im - o_im * t_re).astype(bf16)
        back = jnp.dot(
            inverse_t, jnp.concatenate([c_re, c_im], axis=0), preferred_element_type=f32
        ).astype(bf16)
        br_ref[p * c : p * (c + 1), :] = back[:p]
        bi_ref[p * c : p * (c + 1), :] = back[p:]

    corr = (
        jnp.dot(br_ref[...], cos_t, preferred_element_type=f32)
        + jnp.dot(bi_ref[...], sin_t, preferred_element_type=f32)
    ) / float(p) ** 4
    w = jnp.exp(SHARPNESS * corr)
    u_col = lax.broadcasted_iota(jnp.int32, (cols * p, 1), 0) % p
    off_col = jnp.where(u_col < p // 2, u_col, u_col - p).astype(f32)
    u_row = lax.broadcasted_iota(jnp.int32, (1, p), 1)
    off_row = jnp.where(u_row < p // 2, u_row, u_row - p).astype(f32)
    rows_sum = jnp.sum(w, axis=1, keepdims=True)
    total = jnp.sum(rows_sum.reshape(cols, p, 1), axis=1)
    along_rows = jnp.sum((rows_sum * off_col).reshape(cols, p, 1), axis=1)
    cols_sum = jnp.sum(w.reshape(cols, p, p), axis=1)
    along_cols = jnp.sum(cols_sum * off_row, axis=1, keepdims=True)
    ar = along_rows / total / float(RIM)
    ac = along_cols / total / float(RIM)
    lane = lax.broadcasted_iota(jnp.int32, (cols, 128), 1)
    res = jnp.where(lane == 0, ar, jnp.where(lane == 1, ac, 0.0))
    height = out_ref.shape[1]
    if height > cols:
        res = jnp.concatenate([res, jnp.zeros((height - cols, 128), f32)], axis=0)
    out_ref[0] = res


def pair_flows(own_pad, prev_pad, next_pad, skip_flat, skip_next_flat, use_own, row0, tables):
    tall, broad = own_pad.shape
    rows = (tall - (PATCH - STRIDE)) // STRIDE
    cols = (broad - (PATCH - STRIDE)) // STRIDE
    assert cols % 2 == 0
    height = max(8, -(-cols // 8) * 8)
    both_t, cos_t, sin_t, inverse_t = tables
    band = pl.BlockSpec((pl.Element(PATCH), pl.Element(broad)), lambda i, *_: (i * STRIDE, 0))
    table = pl.BlockSpec((PATCH, PATCH), lambda i, *_: (0, 0))
    grid_spec = pltpu.PrefetchScalarGridSpec(
        num_scalar_prefetch=3,
        grid=(rows,),
        in_specs=[
            band, band, band, pl.BlockSpec((2 * PATCH, PATCH), lambda i, *_: (0, 0)), table, table,
            pl.BlockSpec((2 * PATCH, 2 * PATCH), lambda i, *_: (0, 0)),
        ],
        out_specs=pl.BlockSpec((1, height, 128), lambda i, *_: (i, 0, 0)),
        scratch_shapes=[
            pltpu.VMEM((2 * cols * PATCH, PATCH), jnp.bfloat16),
            pltpu.VMEM((2 * cols * PATCH, PATCH), jnp.bfloat16),
            pltpu.VMEM((2 * cols * PATCH, PATCH), jnp.float32),
            pltpu.VMEM((2 * cols * PATCH, PATCH), jnp.float32),
            pltpu.VMEM((cols * PATCH, PATCH), jnp.bfloat16),
            pltpu.VMEM((cols * PATCH, PATCH), jnp.bfloat16),
        ],
    )
    out = pl.pallas_call(
        functools.partial(_flow_kernel, cols=cols, row0=row0),
        grid_spec=grid_spec,
        out_shape=jax.ShapeDtypeStruct((rows, height, 128), jnp.float32),
        compiler_params=pltpu.CompilerParams(
            dimension_semantics=("arbitrary",), vmem_limit_bytes=48 * 1024 * 1024
        ),
    )(skip_flat, skip_next_flat, use_own.reshape(1), own_pad, prev_pad, next_pad, both_t, cos_t, sin_t, inverse_t)
    half = cols // 2
    first = jnp.repeat(jnp.transpose(out[:, :half, 0:2], (2, 0, 1)), 2, axis=2)
    second = jnp.repeat(jnp.transpose(out[:, half:cols, 0:2], (2, 0, 1)), 2, axis=2)
    return first, second


def gather_sections(value, axis):
    count = lax.axis_size(axis)
    spread = jnp.broadcast_to(value[None], (count,) + value.shape)
    return lax.all_to_all(spread, axis, 0, 0, tiled=True)


def earlier(values, steps, axis):
    width = values.shape[axis]
    widths = [(0, 0)] * values.ndim
    widths[axis] = (steps, 0)
    return lax.slice_in_dim(jnp.pad(values, widths), 0, width, axis=axis)


def later(values, steps, axis):
    width = values.shape[axis]
    widths = [(0, 0)] * values.ndim
    widths[axis] = (0, steps)
    return lax.slice_in_dim(jnp.pad(values, widths), steps, steps + width, axis=axis)


def relax(flow_field, weight, distance):
    near = (distance == 1).astype(jnp.float32)
    far = 1.0 - near
    diag = STIFFNESS + weight + later(weight * near, 1, 0) + later(weight * far, 2, 0)
    positions = jnp.zeros_like(flow_field)
    for sweep in range(RELAX):
        partner = near * earlier(positions, 1, 1) + far * earlier(positions, 2, 1)
        error = weight * (positions - partner - flow_field)
        gradient = (
            STIFFNESS * positions + error - later(error * near, 1, 1) - later(error * far, 2, 1)
        )
        positions = positions - RELAXATION * gradient / diag
    return positions


def body(images, skipped, patch_mask):
    index = lax.axis_index("sec")
    own_distance = jnp.where(index >= 2, 1 + skipped, 1)
    if lax.axis_size("sub") == 2 and lax.axis_size("tile") == 2:
        own_pad = extended_pairs(images, RIM)[0]
    else:
        own_pad = extended(images, (("sub", 1), ("tile", 2)), RIM)[0]
    skip_next = shifted(skipped, "sec", -1)
    use_own = (index == 0).astype(jnp.int32)
    rows_count = (own_pad.shape[0] - (PATCH - STRIDE)) // STRIDE
    chunks = max(n for n in (1, 2, 4) if rows_count % n == 0)
    per = rows_count // chunks
    cos_t, sin_t = dft_tables(PATCH)
    inverse_t = jnp.concatenate(
        [jnp.concatenate([cos_t, sin_t], axis=1), jnp.concatenate([-sin_t, cos_t], axis=1)], axis=0
    )
    tables = (jnp.concatenate([cos_t, sin_t], axis=0), cos_t, sin_t, inverse_t)
    skip_flat = skipped.reshape(-1)
    skip_next_flat = skip_next.reshape(-1)
    firsts, seconds = [], []
    for c in range(chunks):
        start = c * per * STRIDE
        own_c = own_pad[start : start + per * STRIDE + PATCH - STRIDE]
        prev_c = shifted(own_c, "sec", 1)
        next_c = shifted(own_c, "sec", -1)
        first_c, second_c = pair_flows(
            own_c, prev_c, next_c, skip_flat, skip_next_flat, use_own, c * per, tables
        )
        firsts.append(first_c)
        seconds.append(second_c)
    first = jnp.concatenate(firsts, axis=1)
    second = jnp.concatenate(seconds, axis=1)
    first = jnp.where(skipped[0] == 0, first, 0.0)
    second = jnp.where(skip_next[0] == 1, second, 0.0)
    weight = patch_mask.astype(jnp.float32) * (index >= 1).astype(jnp.float32)
    stacked = jnp.concatenate(
        [first, second, weight, own_distance.astype(jnp.float32)], axis=0
    )
    every = jnp.moveaxis(gather_sections(stacked, "sec"), 0, 1)
    raw_all = every[0:2] + earlier(every[2:4], 1, 1)
    flow_all = raw_all * every[4]
    positions_all = relax(flow_all, every[4], every[5])
    flow_field = lax.dynamic_slice_in_dim(flow_all, index, 1, 1)
    positions = lax.dynamic_slice_in_dim(positions_all, index, 1, 1)
    return (flow_field, positions)


def solution(mesh):
    placed = (
        P(("groups", "sec"), "sub", "tile"),
        P(("groups", "sec"), "sub", "tile"),
        P(("groups", "sec"), "sub", "tile"),
    )
    return jax.shard_map(
        body,
        mesh=mesh,
        in_specs=placed,
        out_specs=(
            P(None, ("groups", "sec"), "sub", "tile"),
            P(None, ("groups", "sec"), "sub", "tile"),
        ),
        check_vma=False,
    )
```

```python
import functools
import math

import jax
import jax.numpy as jnp
from jax import lax
from jax.experimental import pallas as pl
from jax.experimental.pallas import tpu as pltpu
from jax.sharding import PartitionSpec as P

PATCH = 160
STRIDE = 128
RELAX = 6
RIM = 16


SHARPNESS = 48.0
STIFFNESS = 0.25
RELAXATION = 0.8
EPSILON = 1e-05


def shifted(value, axis, steps):
    count = lax.axis_size(axis)
    first, last = (max(0, -steps), min(count, count - steps))
    return lax.ppermute(value, axis, [(source, source + steps) for source in range(first, last)])


def _strip_send(strip, dim):
    return jnp.swapaxes(strip, 1, 2) if dim == 2 else strip


def _strip_recv(strip, dim):
    return jnp.swapaxes(strip, 1, 2) if dim == 2 else strip


def extended(block, sides, width):
    for axis, dim in sides:
        count = lax.axis_size(axis)
        top = lax.slice_in_dim(block, 0, width, axis=dim)
        bottom = lax.slice_in_dim(block, block.shape[dim] - width, None, axis=dim)
        if count == 2:
            index = lax.axis_index(axis)
            send = _strip_send(jnp.where(index == 0, bottom, top), dim)
            got = _strip_recv(lax.ppermute(send, axis, [(0, 1), (1, 0)]), dim)
            low = jnp.where(index == 1, got, jnp.zeros_like(got))
            high = jnp.where(index == 0, got, jnp.zeros_like(got))
        else:
            forward = [(i, i + 1) for i in range(count - 1)]
            backward = [(target, source) for source, target in forward]
            low = _strip_recv(lax.ppermute(_strip_send(bottom, dim), axis, forward), dim)
            high = _strip_recv(lax.ppermute(_strip_send(top, dim), axis, backward), dim)
        block = jnp.concatenate([low, block, high], axis=dim)
    return block


def extended_pairs(block, width):
    sub = lax.axis_index("sub")
    tile = lax.axis_index("tile")
    swap = [(0, 1), (1, 0)]
    rows_send = jnp.where(
        sub == 0, block[:, -width:, :], block[:, :width, :]
    )
    cols_send = jnp.swapaxes(jnp.where(tile == 0, block[:, :, -width:], block[:, :, :width]), 1, 2)
    corner_rows = jnp.where(sub == 0, block[:, -width:, :], block[:, :width, :])
    corner_send = jnp.where(tile == 0, corner_rows[:, :, -width:], corner_rows[:, :, :width])
    rows_got = lax.ppermute(rows_send, "sub", swap)
    cols_got = jnp.swapaxes(lax.ppermute(cols_send, "tile", swap), 1, 2)
    corner_got = lax.ppermute(corner_send, ("tile", "sub"), [(0, 3), (3, 0), (1, 2), (2, 1)])

    def keep(flag, value):
        return jnp.where(flag, value, jnp.zeros_like(value))

    top, bottom = sub == 1, sub == 0
    left, right = tile == 1, tile == 0
    middle = jnp.concatenate([keep(left, cols_got), block, keep(right, cols_got)], axis=2)
    upper = jnp.concatenate(
        [keep(top & left, corner_got), keep(top, rows_got), keep(top & right, corner_got)], axis=2
    )
    lower = jnp.concatenate(
        [keep(bottom & left, corner_got), keep(bottom, rows_got), keep(bottom & right, corner_got)],
        axis=2,
    )
    return jnp.concatenate([upper, middle, lower], axis=1)


def dft_tables(patch):
    index = jnp.arange(patch, dtype=jnp.int32)
    product = index[:, None] * index[None, :] % patch
    angle = product.astype(jnp.float32) * (2.0 * math.pi / patch)
    return (jnp.cos(angle).astype(jnp.bfloat16), (-jnp.sin(angle)).astype(jnp.bfloat16))


def _sum_all(x):
    return jnp.sum(jnp.sum(x, axis=1, keepdims=True), axis=0, keepdims=True)


def _flow_kernel(
    skip_ref, skip_next_ref, flag_ref, own_ref, prev_ref, next_ref, cs_ref, c_ref, s_ref, inv_ref,
    out_ref, half_ref, x_ref, y_ref, br_ref, bi_ref, blk_ref,
    *, cols, row0,
):
    f32, bf16 = jnp.float32, jnp.bfloat16
    p = PATCH
    pairs = cols // 2
    i = pl.program_id(0) + row0
    cos_t = c_ref[...]
    sin_t = s_ref[...]
    both_t = cs_ref[...]
    inverse_t = inv_ref[...]
    size = float(p * p)

    def window(ref, j):
        return ref[:, j * STRIDE : j * STRIDE + p]

    use_own = flag_ref[0] == 1
    blocks = []
    for k in range(pairs):
        left, right = 2 * k, 2 * k + 1
        first_near = skip_ref[i * cols + left] == 0
        blocks.append(jnp.where(first_near, window(own_ref, left), window(own_ref, right)))
        blocks.append(jnp.where(first_near, window(prev_ref, left), window(prev_ref, right)))
    for k in range(pairs):
        left, right = 2 * k, 2 * k + 1
        second_far = skip_next_ref[i * cols + right] == 1
        blocks.append(jnp.where(second_far, window(next_ref, right), window(next_ref, left)))
        col_prev = jnp.where(second_far, window(prev_ref, right), window(prev_ref, left))
        col_own = jnp.where(second_far, window(own_ref, right), window(own_ref, left))
        blocks.append(jnp.where(use_own, col_own, col_prev))

    for t, blk in enumerate(blocks):
        blk_ref[p * t : p * (t + 1), :] = blk

    def first_dft(t, carry):
        x = blk_ref[pl.ds(pl.multiple_of(t * p, 16), p), :].astype(f32)
        centered = x - _sum_all(x) / size
        spread = _sum_all(centered * centered) / size
        normed = (centered * lax.rsqrt(spread + EPSILON)).astype(bf16)
        half_ref[pl.ds(pl.multiple_of(t * 2 * p, 16), 2 * p), :] = jnp.dot(
            both_t, normed, preferred_element_type=f32
        ).astype(bf16)
        return carry

    lax.fori_loop(0, len(blocks), first_dft, 0)
    halves = half_ref[...]
    x_ref[...] = jnp.dot(halves, cos_t, preferred_element_type=f32)
    y_ref[...] = jnp.dot(halves, sin_t, preferred_element_type=f32)

    def spectrum(t):
        base = pl.multiple_of(2 * p * t, 16)
        re = x_ref[pl.ds(base, p), :] - y_ref[pl.ds(base + p, p), :]
        im = y_ref[pl.ds(base, p), :] + x_ref[pl.ds(base + p, p), :]
        return re, im

    def inverse(c, carry):
        o_re, o_im = spectrum(2 * c)
        t_re, t_im = spectrum(2 * c + 1)
        c_re = (o_re * t_re + o_im * t_im).astype(bf16)
        c_im = (o_re * t_im - o_im * t_re).astype(bf16)
        back = jnp.dot(
            inverse_t, jnp.concatenate([c_re, c_im], axis=0), preferred_element_type=f32
        ).astype(bf16)
        base = pl.multiple_of(p * c, 16)
        br_ref[pl.ds(base, p), :] = back[:p]
        bi_ref[pl.ds(base, p), :] = back[p:]
        return carry

    lax.fori_loop(0, cols, inverse, 0)

    corr = (
        jnp.dot(br_ref[...], cos_t, preferred_element_type=f32)
        + jnp.dot(bi_ref[...], sin_t, preferred_element_type=f32)
    ) / float(p) ** 4
    w = jnp.exp(SHARPNESS * corr)
    u_col = lax.broadcasted_iota(jnp.int32, (cols * p, 1), 0) % p
    off_col = jnp.where(u_col < p // 2, u_col, u_col - p).astype(f32)
    u_row = lax.broadcasted_iota(jnp.int32, (1, p), 1)
    off_row = jnp.where(u_row < p // 2, u_row, u_row - p).astype(f32)
    rows_sum = jnp.sum(w, axis=1, keepdims=True)
    total = jnp.sum(rows_sum.reshape(cols, p, 1), axis=1)
    along_rows = jnp.sum((rows_sum * off_col).reshape(cols, p, 1), axis=1)
    cols_sum = jnp.sum(w.reshape(cols, p, p), axis=1)
    along_cols = jnp.sum(cols_sum * off_row, axis=1, keepdims=True)
    ar = along_rows / total / float(RIM)
    ac = along_cols / total / float(RIM)
    lane = lax.broadcasted_iota(jnp.int32, (cols, 128), 1)
    res = jnp.where(lane == 0, ar, jnp.where(lane == 1, ac, 0.0))
    height = out_ref.shape[1]
    if height > cols:
        res = jnp.concatenate([res, jnp.zeros((height - cols, 128), f32)], axis=0)
    out_ref[0] = res


def pair_flows(own_pad, prev_pad, next_pad, skip_flat, skip_next_flat, use_own, row0, tables):
    tall, broad = own_pad.shape
    rows = (tall - (PATCH - STRIDE)) // STRIDE
    cols = (broad - (PATCH - STRIDE)) // STRIDE
    assert cols % 2 == 0
    height = max(8, -(-cols // 8) * 8)
    both_t, cos_t, sin_t, inverse_t = tables
    band = pl.BlockSpec((pl.Element(PATCH), pl.Element(broad)), lambda i, *_: (i * STRIDE, 0))
    table = pl.BlockSpec((PATCH, PATCH), lambda i, *_: (0, 0))
    grid_spec = pltpu.PrefetchScalarGridSpec(
        num_scalar_prefetch=3,
        grid=(rows,),
        in_specs=[
            band, band, band, pl.BlockSpec((2 * PATCH, PATCH), lambda i, *_: (0, 0)), table, table,
            pl.BlockSpec((2 * PATCH, 2 * PATCH), lambda i, *_: (0, 0)),
        ],
        out_specs=pl.BlockSpec((1, height, 128), lambda i, *_: (i, 0, 0)),
        scratch_shapes=[
            pltpu.VMEM((4 * cols * PATCH, PATCH), jnp.bfloat16),
            pltpu.VMEM((4 * cols * PATCH, PATCH), jnp.float32),
            pltpu.VMEM((4 * cols * PATCH, PATCH), jnp.float32),
            pltpu.VMEM((cols * PATCH, PATCH), jnp.bfloat16),
            pltpu.VMEM((cols * PATCH, PATCH), jnp.bfloat16),
            pltpu.VMEM((2 * cols * PATCH, PATCH), jnp.bfloat16),
        ],
    )
    out = pl.pallas_call(
        functools.partial(_flow_kernel, cols=cols, row0=row0),
        grid_spec=grid_spec,
        out_shape=jax.ShapeDtypeStruct((rows, height, 128), jnp.float32),
        compiler_params=pltpu.CompilerParams(
            dimension_semantics=("arbitrary",), vmem_limit_bytes=48 * 1024 * 1024
        ),
    )(skip_flat, skip_next_flat, use_own.reshape(1), own_pad, prev_pad, next_pad, both_t, cos_t, sin_t, inverse_t)
    half = cols // 2
    first = jnp.repeat(jnp.transpose(out[:, :half, 0:2], (2, 0, 1)), 2, axis=2)
    second = jnp.repeat(jnp.transpose(out[:, half:cols, 0:2], (2, 0, 1)), 2, axis=2)
    return first, second


def gather_sections(value, axis):
    count = lax.axis_size(axis)
    spread = jnp.broadcast_to(value[None], (count,) + value.shape)
    return lax.all_to_all(spread, axis, 0, 0, tiled=True)


def earlier(values, steps, axis):
    width = values.shape[axis]
    widths = [(0, 0)] * values.ndim
    widths[axis] = (steps, 0)
    return lax.slice_in_dim(jnp.pad(values, widths), 0, width, axis=axis)


def later(values, steps, axis):
    width = values.shape[axis]
    widths = [(0, 0)] * values.ndim
    widths[axis] = (0, steps)
    return lax.slice_in_dim(jnp.pad(values, widths), steps, steps + width, axis=axis)


def relax(flow_field, weight, distance):
    near = (distance == 1).astype(jnp.float32)
    far = 1.0 - near
    diag = STIFFNESS + weight + later(weight * near, 1, 0) + later(weight * far, 2, 0)
    positions = jnp.zeros_like(flow_field)
    for sweep in range(RELAX):
        partner = near * earlier(positions, 1, 1) + far * earlier(positions, 2, 1)
        error = weight * (positions - partner - flow_field)
        gradient = (
            STIFFNESS * positions + error - later(error * near, 1, 1) - later(error * far, 2, 1)
        )
        positions = positions - RELAXATION * gradient / diag
    return positions


def body(images, skipped, patch_mask):
    index = lax.axis_index("sec")
    own_distance = jnp.where(index >= 2, 1 + skipped, 1)
    if lax.axis_size("sub") == 2 and lax.axis_size("tile") == 2:
        own_pad = extended_pairs(images, RIM)[0]
    else:
        own_pad = extended(images, (("sub", 1), ("tile", 2)), RIM)[0]
    skip_next = shifted(skipped, "sec", -1)
    use_own = (index == 0).astype(jnp.int32)
    rows_count = (own_pad.shape[0] - (PATCH - STRIDE)) // STRIDE
    chunks = max(n for n in (1, 2, 4) if rows_count % n == 0)
    per = rows_count // chunks
    cos_t, sin_t = dft_tables(PATCH)
    inverse_t = jnp.concatenate(
        [jnp.concatenate([cos_t, sin_t], axis=1), jnp.concatenate([-sin_t, cos_t], axis=1)], axis=0
    )
    tables = (jnp.concatenate([cos_t, sin_t], axis=0), cos_t, sin_t, inverse_t)
    skip_flat = skipped.reshape(-1)
    skip_next_flat = skip_next.reshape(-1)
    firsts, seconds = [], []
    for c in range(chunks):
        start = c * per * STRIDE
        own_c = own_pad[start : start + per * STRIDE + PATCH - STRIDE]
        prev_c = shifted(own_c, "sec", 1)
        next_c = shifted(own_c, "sec", -1)
        first_c, second_c = pair_flows(
            own_c, prev_c, next_c, skip_flat, skip_next_flat, use_own, c * per, tables
        )
        firsts.append(first_c)
        seconds.append(second_c)
    first = jnp.concatenate(firsts, axis=1)
    second = jnp.concatenate(seconds, axis=1)
    first = jnp.where(skipped[0] == 0, first, 0.0)
    second = jnp.where(skip_next[0] == 1, second, 0.0)
    weight = patch_mask.astype(jnp.float32) * (index >= 1).astype(jnp.float32)
    stacked = jnp.concatenate(
        [first, second, weight, own_distance.astype(jnp.float32)], axis=0
    )
    every = jnp.moveaxis(gather_sections(stacked, "sec"), 0, 1)
    raw_all = every[0:2] + earlier(every[2:4], 1, 1)
    flow_all = raw_all * every[4]
    positions_all = relax(flow_all, every[4], every[5])
    flow_field = lax.dynamic_slice_in_dim(flow_all, index, 1, 1)
    positions = lax.dynamic_slice_in_dim(positions_all, index, 1, 1)
    return (flow_field, positions)


def solution(mesh):
    placed = (
        P(("groups", "sec"), "sub", "tile"),
        P(("groups", "sec"), "sub", "tile"),
        P(("groups", "sec"), "sub", "tile"),
    )
    return jax.shard_map(
        body,
        mesh=mesh,
        in_specs=placed,
        out_specs=(
            P(None, ("groups", "sec"), "sub", "tile"),
            P(None, ("groups", "sec"), "sub", "tile"),
        ),
        check_vma=False,
    )
```

```python
import functools
import math

import jax
import jax.numpy as jnp
from jax import lax
from jax.experimental import pallas as pl
from jax.experimental.pallas import tpu as pltpu
from jax.sharding import PartitionSpec as P

PATCH = 160
STRIDE = 128
RELAX = 6
RIM = 16


SHARPNESS = 48.0
STIFFNESS = 0.25
RELAXATION = 0.8
EPSILON = 1e-05


def shifted(value, axis, steps):
    count = lax.axis_size(axis)
    first, last = (max(0, -steps), min(count, count - steps))
    return lax.ppermute(value, axis, [(source, source + steps) for source in range(first, last)])


def _strip_send(strip, dim):
    return jnp.swapaxes(strip, 1, 2) if dim == 2 else strip


def _strip_recv(strip, dim):
    return jnp.swapaxes(strip, 1, 2) if dim == 2 else strip


def extended(block, sides, width):
    for axis, dim in sides:
        count = lax.axis_size(axis)
        top = lax.slice_in_dim(block, 0, width, axis=dim)
        bottom = lax.slice_in_dim(block, block.shape[dim] - width, None, axis=dim)
        if count == 2:
            index = lax.axis_index(axis)
            send = _strip_send(jnp.where(index == 0, bottom, top), dim)
            got = _strip_recv(lax.ppermute(send, axis, [(0, 1), (1, 0)]), dim)
            low = jnp.where(index == 1, got, jnp.zeros_like(got))
            high = jnp.where(index == 0, got, jnp.zeros_like(got))
        else:
            forward = [(i, i + 1) for i in range(count - 1)]
            backward = [(target, source) for source, target in forward]
            low = _strip_recv(lax.ppermute(_strip_send(bottom, dim), axis, forward), dim)
            high = _strip_recv(lax.ppermute(_strip_send(top, dim), axis, backward), dim)
        block = jnp.concatenate([low, block, high], axis=dim)
    return block


def extended_pairs(block, width):
    sub = lax.axis_index("sub")
    tile = lax.axis_index("tile")
    swap = [(0, 1), (1, 0)]
    rows_send = jnp.where(
        sub == 0, block[:, -width:, :], block[:, :width, :]
    )
    cols_send = jnp.swapaxes(jnp.where(tile == 0, block[:, :, -width:], block[:, :, :width]), 1, 2)
    corner_rows = jnp.where(sub == 0, block[:, -width:, :], block[:, :width, :])
    corner_send = jnp.where(tile == 0, corner_rows[:, :, -width:], corner_rows[:, :, :width])
    rows_got = lax.ppermute(rows_send, "sub", swap)
    cols_got = jnp.swapaxes(lax.ppermute(cols_send, "tile", swap), 1, 2)
    corner_got = lax.ppermute(corner_send, ("tile", "sub"), [(0, 3), (3, 0), (1, 2), (2, 1)])

    def keep(flag, value):
        return jnp.where(flag, value, jnp.zeros_like(value))

    top, bottom = sub == 1, sub == 0
    left, right = tile == 1, tile == 0
    middle = jnp.concatenate([keep(left, cols_got), block, keep(right, cols_got)], axis=2)
    upper = jnp.concatenate(
        [keep(top & left, corner_got), keep(top, rows_got), keep(top & right, corner_got)], axis=2
    )
    lower = jnp.concatenate(
        [keep(bottom & left, corner_got), keep(bottom, rows_got), keep(bottom & right, corner_got)],
        axis=2,
    )
    return jnp.concatenate([upper, middle, lower], axis=1)


def dft_tables(patch):
    index = jnp.arange(patch, dtype=jnp.int32)
    product = index[:, None] * index[None, :] % patch
    angle = product.astype(jnp.float32) * (2.0 * math.pi / patch)
    return (jnp.cos(angle).astype(jnp.bfloat16), (-jnp.sin(angle)).astype(jnp.bfloat16))


def _sum_all(x):
    return jnp.sum(jnp.sum(x, axis=1, keepdims=True), axis=0, keepdims=True)


def _flow_kernel(
    skip_ref, skip_next_ref, flag_ref, own_ref, prev_ref, next_ref, cs_ref, c_ref, s_ref, inv_ref,
    out_ref, half_ref, x_ref, y_ref, br_ref, bi_ref,
    *, cols, row0,
):
    f32, bf16 = jnp.float32, jnp.bfloat16
    p = PATCH
    pairs = cols // 2
    i = pl.program_id(0) + row0
    cos_t = c_ref[...]
    sin_t = s_ref[...]
    both_t = cs_ref[...]
    inverse_t = inv_ref[...]
    size = float(p * p)

    def window(ref, j):
        return ref[:, j * STRIDE : j * STRIDE + p]

    use_own = flag_ref[0] == 1
    blocks = []
    for k in range(pairs):
        left, right = 2 * k, 2 * k + 1
        first_near = skip_ref[i * cols + left] == 0
        blocks.append(jnp.where(first_near, window(own_ref, left), window(own_ref, right)))
        blocks.append(jnp.where(first_near, window(prev_ref, left), window(prev_ref, right)))
    for k in range(pairs):
        left, right = 2 * k, 2 * k + 1
        second_far = skip_next_ref[i * cols + right] == 1
        blocks.append(jnp.where(second_far, window(next_ref, right), window(next_ref, left)))
        col_prev = jnp.where(second_far, window(prev_ref, right), window(prev_ref, left))
        col_own = jnp.where(second_far, window(own_ref, right), window(own_ref, left))
        blocks.append(jnp.where(use_own, col_own, col_prev))

    for t, blk in enumerate(blocks):
        x = blk.astype(f32)
        centered = x - _sum_all(x) / size
        spread = _sum_all(centered * centered) / size
        normed = (centered * lax.rsqrt(spread + EPSILON)).astype(bf16)
        half_ref[2 * p * t : 2 * p * (t + 1), :] = jnp.dot(
            both_t, normed, preferred_element_type=f32
        ).astype(bf16)
    for c in range(cols):
        pair = half_ref[4 * p * c : 4 * p * (c + 1), :]
        xs = jnp.dot(pair, cos_t, preferred_element_type=f32)
        ys = jnp.dot(pair, sin_t, preferred_element_type=f32)
        o_re = xs[:p] - ys[p : 2 * p]
        o_im = ys[:p] + xs[p : 2 * p]
        t_re = xs[2 * p : 3 * p] - ys[3 * p :]
        t_im = ys[2 * p : 3 * p] + xs[3 * p :]
        c_re = (o_re * t_re + o_im * t_im).astype(bf16)
        c_im = (o_re * t_im - o_im * t_re).astype(bf16)
        back = jnp.dot(
            inverse_t, jnp.concatenate([c_re, c_im], axis=0), preferred_element_type=f32
        ).astype(bf16)
        br_ref[p * c : p * (c + 1), :] = back[:p]
        bi_ref[p * c : p * (c + 1), :] = back[p:]

    corr = (
        jnp.dot(br_ref[...], cos_t, preferred_element_type=f32)
        + jnp.dot(bi_ref[...], sin_t, preferred_element_type=f32)
    ) / float(p) ** 4
    w = jnp.exp(SHARPNESS * corr)
    u_col = lax.broadcasted_iota(jnp.int32, (cols * p, 1), 0) % p
    off_col = jnp.where(u_col < p // 2, u_col, u_col - p).astype(f32)
    u_row = lax.broadcasted_iota(jnp.int32, (1, p), 1)
    off_row = jnp.where(u_row < p // 2, u_row, u_row - p).astype(f32)
    rows_sum = jnp.sum(w, axis=1, keepdims=True)
    total = jnp.sum(rows_sum.reshape(cols, p, 1), axis=1)
    along_rows = jnp.sum((rows_sum * off_col).reshape(cols, p, 1), axis=1)
    cols_sum = jnp.sum(w.reshape(cols, p, p), axis=1)
    along_cols = jnp.sum(cols_sum * off_row, axis=1, keepdims=True)
    ar = along_rows / total / float(RIM)
    ac = along_cols / total / float(RIM)
    lane = lax.broadcasted_iota(jnp.int32, (cols, 128), 1)
    res = jnp.where(lane == 0, ar, jnp.where(lane == 1, ac, 0.0))
    height = out_ref.shape[1]
    if height > cols:
        res = jnp.concatenate([res, jnp.zeros((height - cols, 128), f32)], axis=0)
    out_ref[0] = res


def pair_flows(own_pad, prev_pad, next_pad, skip_flat, skip_next_flat, use_own, row0, tables):
    tall, broad = own_pad.shape
    rows = (tall - (PATCH - STRIDE)) // STRIDE
    cols = (broad - (PATCH - STRIDE)) // STRIDE
    assert cols % 2 == 0
    height = max(8, -(-cols // 8) * 8)
    both_t, cos_t, sin_t, inverse_t = tables
    band = pl.BlockSpec((pl.Element(PATCH), pl.Element(broad)), lambda i, *_: (i * STRIDE, 0))
    table = pl.BlockSpec((PATCH, PATCH), lambda i, *_: (0, 0))
    grid_spec = pltpu.PrefetchScalarGridSpec(
        num_scalar_prefetch=3,
        grid=(rows,),
        in_specs=[
            band, band, band, pl.BlockSpec((2 * PATCH, PATCH), lambda i, *_: (0, 0)), table, table,
            pl.BlockSpec((2 * PATCH, 2 * PATCH), lambda i, *_: (0, 0)),
        ],
        out_specs=pl.BlockSpec((1, height, 128), lambda i, *_: (i, 0, 0)),
        scratch_shapes=[
            pltpu.VMEM((4 * cols * PATCH, PATCH), jnp.bfloat16),
            pltpu.VMEM((4 * cols * PATCH, PATCH), jnp.float32),
            pltpu.VMEM((4 * cols * PATCH, PATCH), jnp.float32),
            pltpu.VMEM((cols * PATCH, PATCH), jnp.bfloat16),
            pltpu.VMEM((cols * PATCH, PATCH), jnp.bfloat16),
        ],
    )
    out = pl.pallas_call(
        functools.partial(_flow_kernel, cols=cols, row0=row0),
        grid_spec=grid_spec,
        out_shape=jax.ShapeDtypeStruct((rows, height, 128), jnp.float32),
        compiler_params=pltpu.CompilerParams(
            dimension_semantics=("arbitrary",), vmem_limit_bytes=48 * 1024 * 1024
        ),
    )(skip_flat, skip_next_flat, use_own.reshape(1), own_pad, prev_pad, next_pad, both_t, cos_t, sin_t, inverse_t)
    half = cols // 2
    first = jnp.repeat(jnp.transpose(out[:, :half, 0:2], (2, 0, 1)), 2, axis=2)
    second = jnp.repeat(jnp.transpose(out[:, half:cols, 0:2], (2, 0, 1)), 2, axis=2)
    return first, second


def gather_sections(value, axis):
    count = lax.axis_size(axis)
    spread = jnp.broadcast_to(value[None], (count,) + value.shape)
    return lax.all_to_all(spread, axis, 0, 0, tiled=True)


def earlier(values, steps, axis):
    width = values.shape[axis]
    widths = [(0, 0)] * values.ndim
    widths[axis] = (steps, 0)
    return lax.slice_in_dim(jnp.pad(values, widths), 0, width, axis=axis)


def later(values, steps, axis):
    width = values.shape[axis]
    widths = [(0, 0)] * values.ndim
    widths[axis] = (0, steps)
    return lax.slice_in_dim(jnp.pad(values, widths), steps, steps + width, axis=axis)


def relax(flow_field, weight, distance):
    near = (distance == 1).astype(jnp.float32)
    far = 1.0 - near
    diag = STIFFNESS + weight + later(weight * near, 1, 0) + later(weight * far, 2, 0)
    positions = jnp.zeros_like(flow_field)
    for sweep in range(RELAX):
        partner = near * earlier(positions, 1, 1) + far * earlier(positions, 2, 1)
        error = weight * (positions - partner - flow_field)
        gradient = (
            STIFFNESS * positions + error - later(error * near, 1, 1) - later(error * far, 2, 1)
        )
        positions = positions - RELAXATION * gradient / diag
    return positions


def body(images, skipped, patch_mask):
    index = lax.axis_index("sec")
    own_distance = jnp.where(index >= 2, 1 + skipped, 1)
    if lax.axis_size("sub") == 2 and lax.axis_size("tile") == 2:
        own_pad = extended_pairs(images, RIM)[0]
    else:
        own_pad = extended(images, (("sub", 1), ("tile", 2)), RIM)[0]
    skip_next = shifted(skipped, "sec", -1)
    use_own = (index == 0).astype(jnp.int32)
    rows_count = (own_pad.shape[0] - (PATCH - STRIDE)) // STRIDE
    chunks = max(n for n in (1, 2, 4) if rows_count % n == 0)
    per = rows_count // chunks
    cos_t, sin_t = dft_tables(PATCH)
    inverse_t = jnp.concatenate(
        [jnp.concatenate([cos_t, sin_t], axis=1), jnp.concatenate([-sin_t, cos_t], axis=1)], axis=0
    )
    tables = (jnp.concatenate([cos_t, sin_t], axis=0), cos_t, sin_t, inverse_t)
    skip_flat = skipped.reshape(-1)
    skip_next_flat = skip_next.reshape(-1)
    firsts, seconds = [], []
    for c in range(chunks):
        start = c * per * STRIDE
        own_c = own_pad[start : start + per * STRIDE + PATCH - STRIDE]
        prev_c = shifted(own_c, "sec", 1)
        next_c = shifted(own_c, "sec", -1)
        first_c, second_c = pair_flows(
            own_c, prev_c, next_c, skip_flat, skip_next_flat, use_own, c * per, tables
        )
        firsts.append(first_c)
        seconds.append(second_c)
    first = jnp.concatenate(firsts, axis=1)
    second = jnp.concatenate(seconds, axis=1)
    first = jnp.where(skipped[0] == 0, first, 0.0)
    second = jnp.where(skip_next[0] == 1, second, 0.0)
    weight = patch_mask.astype(jnp.float32) * (index >= 1).astype(jnp.float32)
    stacked = jnp.concatenate(
        [first, second, weight, own_distance.astype(jnp.float32)], axis=0
    )
    every = jnp.moveaxis(gather_sections(stacked, "sec"), 0, 1)
    raw_all = every[0:2] + earlier(every[2:4], 1, 1)
    flow_all = raw_all * every[4]
    positions_all = relax(flow_all, every[4], every[5])
    flow_field = lax.dynamic_slice_in_dim(flow_all, index, 1, 1)
    positions = lax.dynamic_slice_in_dim(positions_all, index, 1, 1)
    return (flow_field, positions)


def solution(mesh):
    placed = (
        P(("groups", "sec"), "sub", "tile"),
        P(("groups", "sec"), "sub", "tile"),
        P(("groups", "sec"), "sub", "tile"),
    )
    return jax.shard_map(
        body,
        mesh=mesh,
        in_specs=placed,
        out_specs=(
            P(None, ("groups", "sec"), "sub", "tile"),
            P(None, ("groups", "sec"), "sub", "tile"),
        ),
        check_vma=False,
    )
```

```python
import functools
import math

import jax
import jax.numpy as jnp
from jax import lax
from jax.experimental import pallas as pl
from jax.experimental.pallas import tpu as pltpu
from jax.sharding import PartitionSpec as P

PATCH = 160
STRIDE = 128
RELAX = 6
RIM = 16


SHARPNESS = 48.0
STIFFNESS = 0.25
RELAXATION = 0.8
EPSILON = 1e-05


def shifted(value, axis, steps):
    count = lax.axis_size(axis)
    first, last = (max(0, -steps), min(count, count - steps))
    return lax.ppermute(value, axis, [(source, source + steps) for source in range(first, last)])


def _strip_send(strip, dim):
    return jnp.swapaxes(strip, 1, 2) if dim == 2 else strip


def _strip_recv(strip, dim):
    return jnp.swapaxes(strip, 1, 2) if dim == 2 else strip


def extended(block, sides, width):
    for axis, dim in sides:
        count = lax.axis_size(axis)
        top = lax.slice_in_dim(block, 0, width, axis=dim)
        bottom = lax.slice_in_dim(block, block.shape[dim] - width, None, axis=dim)
        if count == 2:
            index = lax.axis_index(axis)
            send = _strip_send(jnp.where(index == 0, bottom, top), dim)
            got = _strip_recv(lax.ppermute(send, axis, [(0, 1), (1, 0)]), dim)
            low = jnp.where(index == 1, got, jnp.zeros_like(got))
            high = jnp.where(index == 0, got, jnp.zeros_like(got))
        else:
            forward = [(i, i + 1) for i in range(count - 1)]
            backward = [(target, source) for source, target in forward]
            low = _strip_recv(lax.ppermute(_strip_send(bottom, dim), axis, forward), dim)
            high = _strip_recv(lax.ppermute(_strip_send(top, dim), axis, backward), dim)
        block = jnp.concatenate([low, block, high], axis=dim)
    return block


def extended_pairs(block, width):
    sub = lax.axis_index("sub")
    tile = lax.axis_index("tile")
    swap = [(0, 1), (1, 0)]
    rows_send = jnp.where(
        sub == 0, block[:, -width:, :], block[:, :width, :]
    )
    cols_send = jnp.swapaxes(jnp.where(tile == 0, block[:, :, -width:], block[:, :, :width]), 1, 2)
    corner_rows = jnp.where(sub == 0, block[:, -width:, :], block[:, :width, :])
    corner_send = jnp.where(tile == 0, corner_rows[:, :, -width:], corner_rows[:, :, :width])
    rows_got = lax.ppermute(rows_send, "sub", swap)
    cols_got = jnp.swapaxes(lax.ppermute(cols_send, "tile", swap), 1, 2)
    corner_got = lax.ppermute(corner_send, ("tile", "sub"), [(0, 3), (3, 0), (1, 2), (2, 1)])

    def keep(flag, value):
        return jnp.where(flag, value, jnp.zeros_like(value))

    top, bottom = sub == 1, sub == 0
    left, right = tile == 1, tile == 0
    middle = jnp.concatenate([keep(left, cols_got), block, keep(right, cols_got)], axis=2)
    upper = jnp.concatenate(
        [keep(top & left, corner_got), keep(top, rows_got), keep(top & right, corner_got)], axis=2
    )
    lower = jnp.concatenate(
        [keep(bottom & left, corner_got), keep(bottom, rows_got), keep(bottom & right, corner_got)],
        axis=2,
    )
    return jnp.concatenate([upper, middle, lower], axis=1)


def dft_tables(patch):
    index = jnp.arange(patch, dtype=jnp.int32)
    product = index[:, None] * index[None, :] % patch
    angle = product.astype(jnp.float32) * (2.0 * math.pi / patch)
    return (jnp.cos(angle).astype(jnp.bfloat16), (-jnp.sin(angle)).astype(jnp.bfloat16))


def _sum_all(x):
    return jnp.sum(jnp.sum(x, axis=1, keepdims=True), axis=0, keepdims=True)


def _flow_kernel(
    skip_ref, skip_next_ref, flag_ref, own_ref, prev_ref, next_ref, cs_ref, c_ref, s_ref, inv_ref,
    out_ref, half_ref, x_ref, y_ref, br_ref, bi_ref,
    *, cols, row0, count,
):
    f32, bf16 = jnp.float32, jnp.bfloat16
    p = PATCH
    pairs = cols // 2
    cos_t = c_ref[...]
    sin_t = s_ref[...]
    both_t = cs_ref[...]
    inverse_t = inv_ref[...]
    size = float(p * p)

    def window(ref, j):
        return ref[r0 : r0 + p, j * STRIDE : j * STRIDE + p]

    use_own = flag_ref[0] == 1
    blocks = []
    for row in range(count):
        i = row0 + count * pl.program_id(0) + row
        r0 = row * STRIDE
        blocks.extend(_row_blocks(skip_ref, skip_next_ref, own_ref, prev_ref, next_ref, use_own, i, r0, cols))
    _rest(blocks, half_ref, x_ref, y_ref, br_ref, bi_ref, out_ref, cos_t, sin_t, both_t, inverse_t, cols * count, count, cols)


def _row_blocks(skip_ref, skip_next_ref, own_ref, prev_ref, next_ref, use_own, i, r0, cols):
    p = PATCH
    pairs = cols // 2

    def window(ref, j):
        return ref[r0 : r0 + p, j * STRIDE : j * STRIDE + p]

    blocks = []
    for k in range(pairs):
        left, right = 2 * k, 2 * k + 1
        first_near = skip_ref[i * cols + left] == 0
        blocks.append(jnp.where(first_near, window(own_ref, left), window(own_ref, right)))
        blocks.append(jnp.where(first_near, window(prev_ref, left), window(prev_ref, right)))
    for k in range(pairs):
        left, right = 2 * k, 2 * k + 1
        second_far = skip_next_ref[i * cols + right] == 1
        blocks.append(jnp.where(second_far, window(next_ref, right), window(next_ref, left)))
        col_prev = jnp.where(second_far, window(prev_ref, right), window(prev_ref, left))
        col_own = jnp.where(second_far, window(own_ref, right), window(own_ref, left))
        blocks.append(jnp.where(use_own, col_own, col_prev))
    return blocks


def _rest(blocks, half_ref, x_ref, y_ref, br_ref, bi_ref, out_ref, cos_t, sin_t, both_t, inverse_t, total_pairs, count, row_cols):
    f32, bf16 = jnp.float32, jnp.bfloat16
    p = PATCH
    size = float(p * p)
    cols = total_pairs
    for t, blk in enumerate(blocks):
        x = blk.astype(f32)
        centered = x - _sum_all(x) / size
        spread = _sum_all(centered * centered) / size
        normed = (centered * lax.rsqrt(spread + EPSILON)).astype(bf16)
        half_ref[2 * p * t : 2 * p * (t + 1), :] = jnp.dot(
            both_t, normed, preferred_element_type=f32
        ).astype(bf16)
    halves = half_ref[...]
    x_ref[...] = jnp.dot(halves, cos_t, preferred_element_type=f32)
    y_ref[...] = jnp.dot(halves, sin_t, preferred_element_type=f32)

    def spectrum(t):
        base = 2 * p * t
        re = x_ref[base : base + p, :] - y_ref[base + p : base + 2 * p, :]
        im = y_ref[base : base + p, :] + x_ref[base + p : base + 2 * p, :]
        return re, im

    for c in range(cols):
        o_re, o_im = spectrum(2 * c)
        t_re, t_im = spectrum(2 * c + 1)
        c_re = (o_re * t_re + o_im * t_im).astype(bf16)
        c_im = (o_re * t_im - o_im * t_re).astype(bf16)
        back = jnp.dot(
            inverse_t, jnp.concatenate([c_re, c_im], axis=0), preferred_element_type=f32
        ).astype(bf16)
        br_ref[p * c : p * (c + 1), :] = back[:p]
        bi_ref[p * c : p * (c + 1), :] = back[p:]

    corr = (
        jnp.dot(br_ref[...], cos_t, preferred_element_type=f32)
        + jnp.dot(bi_ref[...], sin_t, preferred_element_type=f32)
    ) / float(p) ** 4
    w = jnp.exp(SHARPNESS * corr)
    u_col = lax.broadcasted_iota(jnp.int32, (cols * p, 1), 0) % p
    off_col = jnp.where(u_col < p // 2, u_col, u_col - p).astype(f32)
    u_row = lax.broadcasted_iota(jnp.int32, (1, p), 1)
    off_row = jnp.where(u_row < p // 2, u_row, u_row - p).astype(f32)
    rows_sum = jnp.sum(w, axis=1, keepdims=True)
    total = jnp.sum(rows_sum.reshape(cols, p, 1), axis=1)
    along_rows = jnp.sum((rows_sum * off_col).reshape(cols, p, 1), axis=1)
    cols_sum = jnp.sum(w.reshape(cols, p, p), axis=1)
    along_cols = jnp.sum(cols_sum * off_row, axis=1, keepdims=True)
    ar = along_rows / total / float(RIM)
    ac = along_cols / total / float(RIM)
    lane = lax.broadcasted_iota(jnp.int32, (cols, 128), 1)
    res = jnp.where(lane == 0, ar, jnp.where(lane == 1, ac, 0.0))
    height = out_ref.shape[1]
    for row in range(count):
        part = res[row * row_cols : (row + 1) * row_cols]
        if height > row_cols:
            part = jnp.concatenate([part, jnp.zeros((height - row_cols, 128), f32)], axis=0)
        out_ref[row] = part


def pair_flows(own_pad, prev_pad, next_pad, skip_flat, skip_next_flat, use_own, row0, tables):
    tall, broad = own_pad.shape
    rows = (tall - (PATCH - STRIDE)) // STRIDE
    cols = (broad - (PATCH - STRIDE)) // STRIDE
    assert cols % 2 == 0
    height = max(8, -(-cols // 8) * 8)
    both_t, cos_t, sin_t, inverse_t = tables
    step = 2 if rows % 2 == 0 else 1
    band = pl.BlockSpec(
        (pl.Element(step * STRIDE + PATCH - STRIDE), pl.Element(broad)),
        lambda i, *_: (i * step * STRIDE, 0),
    )
    table = pl.BlockSpec((PATCH, PATCH), lambda i, *_: (0, 0))
    grid_spec = pltpu.PrefetchScalarGridSpec(
        num_scalar_prefetch=3,
        grid=(rows // step,),
        in_specs=[
            band, band, band, pl.BlockSpec((2 * PATCH, PATCH), lambda i, *_: (0, 0)), table, table,
            pl.BlockSpec((2 * PATCH, 2 * PATCH), lambda i, *_: (0, 0)),
        ],
        out_specs=pl.BlockSpec((step, height, 128), lambda i, *_: (i, 0, 0)),
        scratch_shapes=[
            pltpu.VMEM((4 * step * cols * PATCH, PATCH), jnp.bfloat16),
            pltpu.VMEM((4 * step * cols * PATCH, PATCH), jnp.float32),
            pltpu.VMEM((4 * step * cols * PATCH, PATCH), jnp.float32),
            pltpu.VMEM((step * cols * PATCH, PATCH), jnp.bfloat16),
            pltpu.VMEM((step * cols * PATCH, PATCH), jnp.bfloat16),
        ],
    )
    out = pl.pallas_call(
        functools.partial(_flow_kernel, cols=cols, row0=row0, count=step),
        grid_spec=grid_spec,
        out_shape=jax.ShapeDtypeStruct((rows, height, 128), jnp.float32),
        compiler_params=pltpu.CompilerParams(
            dimension_semantics=("arbitrary",), vmem_limit_bytes=48 * 1024 * 1024
        ),
    )(skip_flat, skip_next_flat, use_own.reshape(1), own_pad, prev_pad, next_pad, both_t, cos_t, sin_t, inverse_t)
    half = cols // 2
    first = jnp.repeat(jnp.transpose(out[:, :half, 0:2], (2, 0, 1)), 2, axis=2)
    second = jnp.repeat(jnp.transpose(out[:, half:cols, 0:2], (2, 0, 1)), 2, axis=2)
    return first, second


def gather_sections(value, axis):
    count = lax.axis_size(axis)
    spread = jnp.broadcast_to(value[None], (count,) + value.shape)
    return lax.all_to_all(spread, axis, 0, 0, tiled=True)


def earlier(values, steps, axis):
    width = values.shape[axis]
    widths = [(0, 0)] * values.ndim
    widths[axis] = (steps, 0)
    return lax.slice_in_dim(jnp.pad(values, widths), 0, width, axis=axis)


def later(values, steps, axis):
    width = values.shape[axis]
    widths = [(0, 0)] * values.ndim
    widths[axis] = (0, steps)
    return lax.slice_in_dim(jnp.pad(values, widths), steps, steps + width, axis=axis)


def relax(flow_field, weight, distance):
    near = (distance == 1).astype(jnp.float32)
    far = 1.0 - near
    diag = STIFFNESS + weight + later(weight * near, 1, 0) + later(weight * far, 2, 0)
    positions = jnp.zeros_like(flow_field)
    for sweep in range(RELAX):
        partner = near * earlier(positions, 1, 1) + far * earlier(positions, 2, 1)
        error = weight * (positions - partner - flow_field)
        gradient = (
            STIFFNESS * positions + error - later(error * near, 1, 1) - later(error * far, 2, 1)
        )
        positions = positions - RELAXATION * gradient / diag
    return positions


def body(images, skipped, patch_mask):
    index = lax.axis_index("sec")
    own_distance = jnp.where(index >= 2, 1 + skipped, 1)
    if lax.axis_size("sub") == 2 and lax.axis_size("tile") == 2:
        own_pad = extended_pairs(images, RIM)[0]
    else:
        own_pad = extended(images, (("sub", 1), ("tile", 2)), RIM)[0]
    skip_next = shifted(skipped, "sec", -1)
    use_own = (index == 0).astype(jnp.int32)
    rows_count = (own_pad.shape[0] - (PATCH - STRIDE)) // STRIDE
    chunks = 2 if rows_count % 4 == 0 else 1
    per = rows_count // chunks
    cos_t, sin_t = dft_tables(PATCH)
    inverse_t = jnp.concatenate(
        [jnp.concatenate([cos_t, sin_t], axis=1), jnp.concatenate([-sin_t, cos_t], axis=1)], axis=0
    )
    tables = (jnp.concatenate([cos_t, sin_t], axis=0), cos_t, sin_t, inverse_t)
    skip_flat = skipped.reshape(-1)
    skip_next_flat = skip_next.reshape(-1)
    firsts, seconds = [], []
    for c in range(chunks):
        start = c * per * STRIDE
        own_c = own_pad[start : start + per * STRIDE + PATCH - STRIDE]
        prev_c = shifted(own_c, "sec", 1)
        next_c = shifted(own_c, "sec", -1)
        first_c, second_c = pair_flows(
            own_c, prev_c, next_c, skip_flat, skip_next_flat, use_own, c * per, tables
        )
        firsts.append(first_c)
        seconds.append(second_c)
    first = jnp.concatenate(firsts, axis=1)
    second = jnp.concatenate(seconds, axis=1)
    first = jnp.where(skipped[0] == 0, first, 0.0)
    second = jnp.where(skip_next[0] == 1, second, 0.0)
    weight = patch_mask.astype(jnp.float32) * (index >= 1).astype(jnp.float32)
    stacked = jnp.concatenate(
        [first, second, weight, own_distance.astype(jnp.float32)], axis=0
    )
    every = jnp.moveaxis(gather_sections(stacked, "sec"), 0, 1)
    raw_all = every[0:2] + earlier(every[2:4], 1, 1)
    flow_all = raw_all * every[4]
    positions_all = relax(flow_all, every[4], every[5])
    flow_field = lax.dynamic_slice_in_dim(flow_all, index, 1, 1)
    positions = lax.dynamic_slice_in_dim(positions_all, index, 1, 1)
    return (flow_field, positions)


def solution(mesh):
    placed = (
        P(("groups", "sec"), "sub", "tile"),
        P(("groups", "sec"), "sub", "tile"),
        P(("groups", "sec"), "sub", "tile"),
    )
    return jax.shard_map(
        body,
        mesh=mesh,
        in_specs=placed,
        out_specs=(
            P(None, ("groups", "sec"), "sub", "tile"),
            P(None, ("groups", "sec"), "sub", "tile"),
        ),
        check_vma=False,
    )
```

```python
import functools
import math

import jax
import jax.numpy as jnp
from jax import lax
from jax.experimental import pallas as pl
from jax.experimental.pallas import tpu as pltpu
from jax.sharding import PartitionSpec as P

PATCH = 160
STRIDE = 128
RELAX = 6
RIM = 16


SHARPNESS = 48.0
STIFFNESS = 0.25
RELAXATION = 0.8
EPSILON = 1e-05


def shifted(value, axis, steps):
    count = lax.axis_size(axis)
    first, last = (max(0, -steps), min(count, count - steps))
    return lax.ppermute(value, axis, [(source, source + steps) for source in range(first, last)])


def _strip_send(strip, dim):
    return jnp.swapaxes(strip, 1, 2) if dim == 2 else strip


def _strip_recv(strip, dim):
    return jnp.swapaxes(strip, 1, 2) if dim == 2 else strip


def extended(block, sides, width):
    for axis, dim in sides:
        count = lax.axis_size(axis)
        top = lax.slice_in_dim(block, 0, width, axis=dim)
        bottom = lax.slice_in_dim(block, block.shape[dim] - width, None, axis=dim)
        if count == 2:
            index = lax.axis_index(axis)
            send = _strip_send(jnp.where(index == 0, bottom, top), dim)
            got = _strip_recv(lax.ppermute(send, axis, [(0, 1), (1, 0)]), dim)
            low = jnp.where(index == 1, got, jnp.zeros_like(got))
            high = jnp.where(index == 0, got, jnp.zeros_like(got))
        else:
            forward = [(i, i + 1) for i in range(count - 1)]
            backward = [(target, source) for source, target in forward]
            low = _strip_recv(lax.ppermute(_strip_send(bottom, dim), axis, forward), dim)
            high = _strip_recv(lax.ppermute(_strip_send(top, dim), axis, backward), dim)
        block = jnp.concatenate([low, block, high], axis=dim)
    return block


def extended_pairs(block, width):
    sub = lax.axis_index("sub")
    tile = lax.axis_index("tile")
    swap = [(0, 1), (1, 0)]
    rows_send = jnp.where(
        sub == 0, block[:, -width:, :], block[:, :width, :]
    )
    cols_send = jnp.swapaxes(jnp.where(tile == 0, block[:, :, -width:], block[:, :, :width]), 1, 2)
    corner_rows = jnp.where(sub == 0, block[:, -width:, :], block[:, :width, :])
    corner_send = jnp.where(tile == 0, corner_rows[:, :, -width:], corner_rows[:, :, :width])
    rows_got = lax.ppermute(rows_send, "sub", swap)
    cols_got = jnp.swapaxes(lax.ppermute(cols_send, "tile", swap), 1, 2)
    corner_got = lax.ppermute(corner_send, ("tile", "sub"), [(0, 3), (3, 0), (1, 2), (2, 1)])

    def keep(flag, value):
        return jnp.where(flag, value, jnp.zeros_like(value))

    top, bottom = sub == 1, sub == 0
    left, right = tile == 1, tile == 0
    middle = jnp.concatenate([keep(left, cols_got), block, keep(right, cols_got)], axis=2)
    upper = jnp.concatenate(
        [keep(top & left, corner_got), keep(top, rows_got), keep(top & right, corner_got)], axis=2
    )
    lower = jnp.concatenate(
        [keep(bottom & left, corner_got), keep(bottom, rows_got), keep(bottom & right, corner_got)],
        axis=2,
    )
    return jnp.concatenate([upper, middle, lower], axis=1)


def dft_tables(patch):
    index = jnp.arange(patch, dtype=jnp.int32)
    product = index[:, None] * index[None, :] % patch
    angle = product.astype(jnp.float32) * (2.0 * math.pi / patch)
    return (jnp.cos(angle).astype(jnp.bfloat16), (-jnp.sin(angle)).astype(jnp.bfloat16))


def _sum_all(x):
    return jnp.sum(jnp.sum(x, axis=1, keepdims=True), axis=0, keepdims=True)


def _flow_kernel(
    skip_ref, skip_next_ref, flag_ref, own_ref, prev_ref, next_ref, cs_ref, c_ref, s_ref, inv_ref,
    out_ref, half_ref, x_ref, y_ref, br_ref, bi_ref,
    *, cols, row0, count,
):
    f32, bf16 = jnp.float32, jnp.bfloat16
    p = PATCH
    pairs = cols // 2
    cos_t = c_ref[...]
    sin_t = s_ref[...]
    both_t = cs_ref[...]
    inverse_t = inv_ref[...]
    size = float(p * p)

    def window(ref, j):
        return ref[r0 : r0 + p, j * STRIDE : j * STRIDE + p]

    use_own = flag_ref[0] == 1
    blocks = []
    for row in range(count):
        i = row0 + row
        r0 = row * STRIDE
        blocks.extend(_row_blocks(skip_ref, skip_next_ref, own_ref, prev_ref, next_ref, use_own, i, r0, cols))
    _rest(blocks, half_ref, x_ref, y_ref, br_ref, bi_ref, out_ref, cos_t, sin_t, both_t, inverse_t, cols * count, count, cols)


def _row_blocks(skip_ref, skip_next_ref, own_ref, prev_ref, next_ref, use_own, i, r0, cols):
    p = PATCH
    pairs = cols // 2

    def window(ref, j):
        return ref[r0 : r0 + p, j * STRIDE : j * STRIDE + p]

    blocks = []
    for k in range(pairs):
        left, right = 2 * k, 2 * k + 1
        first_near = skip_ref[i * cols + left] == 0
        blocks.append(jnp.where(first_near, window(own_ref, left), window(own_ref, right)))
        blocks.append(jnp.where(first_near, window(prev_ref, left), window(prev_ref, right)))
    for k in range(pairs):
        left, right = 2 * k, 2 * k + 1
        second_far = skip_next_ref[i * cols + right] == 1
        blocks.append(jnp.where(second_far, window(next_ref, right), window(next_ref, left)))
        col_prev = jnp.where(second_far, window(prev_ref, right), window(prev_ref, left))
        col_own = jnp.where(second_far, window(own_ref, right), window(own_ref, left))
        blocks.append(jnp.where(use_own, col_own, col_prev))
    return blocks


def _rest(blocks, half_ref, x_ref, y_ref, br_ref, bi_ref, out_ref, cos_t, sin_t, both_t, inverse_t, total_pairs, count, row_cols):
    f32, bf16 = jnp.float32, jnp.bfloat16
    p = PATCH
    size = float(p * p)
    cols = total_pairs
    for t, blk in enumerate(blocks):
        x = blk.astype(f32)
        centered = x - _sum_all(x) / size
        spread = _sum_all(centered * centered) / size
        normed = (centered * lax.rsqrt(spread + EPSILON)).astype(bf16)
        half_ref[2 * p * t : 2 * p * (t + 1), :] = jnp.dot(
            both_t, normed, preferred_element_type=f32
        ).astype(bf16)
    halves = half_ref[...]
    x_ref[...] = jnp.dot(halves, cos_t, preferred_element_type=f32)
    y_ref[...] = jnp.dot(halves, sin_t, preferred_element_type=f32)

    def spectrum(t):
        base = 2 * p * t
        re = x_ref[base : base + p, :] - y_ref[base + p : base + 2 * p, :]
        im = y_ref[base : base + p, :] + x_ref[base + p : base + 2 * p, :]
        return re, im

    for c in range(cols):
        o_re, o_im = spectrum(2 * c)
        t_re, t_im = spectrum(2 * c + 1)
        c_re = (o_re * t_re + o_im * t_im).astype(bf16)
        c_im = (o_re * t_im - o_im * t_re).astype(bf16)
        back = jnp.dot(
            inverse_t, jnp.concatenate([c_re, c_im], axis=0), preferred_element_type=f32
        ).astype(bf16)
        br_ref[p * c : p * (c + 1), :] = back[:p]
        bi_ref[p * c : p * (c + 1), :] = back[p:]

    corr = (
        jnp.dot(br_ref[...], cos_t, preferred_element_type=f32)
        + jnp.dot(bi_ref[...], sin_t, preferred_element_type=f32)
    ) / float(p) ** 4
    w = jnp.exp(SHARPNESS * corr)
    u_col = lax.broadcasted_iota(jnp.int32, (cols * p, 1), 0) % p
    off_col = jnp.where(u_col < p // 2, u_col, u_col - p).astype(f32)
    u_row = lax.broadcasted_iota(jnp.int32, (1, p), 1)
    off_row = jnp.where(u_row < p // 2, u_row, u_row - p).astype(f32)
    rows_sum = jnp.sum(w, axis=1, keepdims=True)
    total = jnp.sum(rows_sum.reshape(cols, p, 1), axis=1)
    along_rows = jnp.sum((rows_sum * off_col).reshape(cols, p, 1), axis=1)
    cols_sum = jnp.sum(w.reshape(cols, p, p), axis=1)
    along_cols = jnp.sum(cols_sum * off_row, axis=1, keepdims=True)
    ar = along_rows / total / float(RIM)
    ac = along_cols / total / float(RIM)
    lane = lax.broadcasted_iota(jnp.int32, (cols, 128), 1)
    res = jnp.where(lane == 0, ar, jnp.where(lane == 1, ac, 0.0))
    height = out_ref.shape[1]
    for row in range(count):
        part = res[row * row_cols : (row + 1) * row_cols]
        if height > row_cols:
            part = jnp.concatenate([part, jnp.zeros((height - row_cols, 128), f32)], axis=0)
        out_ref[row] = part


def pair_flows(own_pad, prev_pad, next_pad, skip_flat, skip_next_flat, use_own, row0, tables):
    tall, broad = own_pad.shape
    rows = (tall - (PATCH - STRIDE)) // STRIDE
    cols = (broad - (PATCH - STRIDE)) // STRIDE
    assert cols % 2 == 0
    height = max(8, -(-cols // 8) * 8)
    both_t, cos_t, sin_t, inverse_t = tables
    band = pl.BlockSpec((tall, broad), lambda i, *_: (0, 0))
    table = pl.BlockSpec((PATCH, PATCH), lambda i, *_: (0, 0))
    grid_spec = pltpu.PrefetchScalarGridSpec(
        num_scalar_prefetch=3,
        grid=(1,),
        in_specs=[
            band, band, band, pl.BlockSpec((2 * PATCH, PATCH), lambda i, *_: (0, 0)), table, table,
            pl.BlockSpec((2 * PATCH, 2 * PATCH), lambda i, *_: (0, 0)),
        ],
        out_specs=pl.BlockSpec((rows, height, 128), lambda i, *_: (0, 0, 0)),
        scratch_shapes=[
            pltpu.VMEM((4 * rows * cols * PATCH, PATCH), jnp.bfloat16),
            pltpu.VMEM((4 * rows * cols * PATCH, PATCH), jnp.float32),
            pltpu.VMEM((4 * rows * cols * PATCH, PATCH), jnp.float32),
            pltpu.VMEM((rows * cols * PATCH, PATCH), jnp.bfloat16),
            pltpu.VMEM((rows * cols * PATCH, PATCH), jnp.bfloat16),
        ],
    )
    out = pl.pallas_call(
        functools.partial(_flow_kernel, cols=cols, row0=row0, count=rows),
        grid_spec=grid_spec,
        out_shape=jax.ShapeDtypeStruct((rows, height, 128), jnp.float32),
        compiler_params=pltpu.CompilerParams(
            dimension_semantics=("arbitrary",), vmem_limit_bytes=48 * 1024 * 1024
        ),
    )(skip_flat, skip_next_flat, use_own.reshape(1), own_pad, prev_pad, next_pad, both_t, cos_t, sin_t, inverse_t)
    half = cols // 2
    first = jnp.repeat(jnp.transpose(out[:, :half, 0:2], (2, 0, 1)), 2, axis=2)
    second = jnp.repeat(jnp.transpose(out[:, half:cols, 0:2], (2, 0, 1)), 2, axis=2)
    return first, second


def gather_sections(value, axis):
    count = lax.axis_size(axis)
    spread = jnp.broadcast_to(value[None], (count,) + value.shape)
    return lax.all_to_all(spread, axis, 0, 0, tiled=True)


def earlier(values, steps, axis):
    width = values.shape[axis]
    widths = [(0, 0)] * values.ndim
    widths[axis] = (steps, 0)
    return lax.slice_in_dim(jnp.pad(values, widths), 0, width, axis=axis)


def later(values, steps, axis):
    width = values.shape[axis]
    widths = [(0, 0)] * values.ndim
    widths[axis] = (0, steps)
    return lax.slice_in_dim(jnp.pad(values, widths), steps, steps + width, axis=axis)


def relax(flow_field, weight, distance):
    near = (distance == 1).astype(jnp.float32)
    far = 1.0 - near
    diag = STIFFNESS + weight + later(weight * near, 1, 0) + later(weight * far, 2, 0)
    positions = jnp.zeros_like(flow_field)
    for sweep in range(RELAX):
        partner = near * earlier(positions, 1, 1) + far * earlier(positions, 2, 1)
        error = weight * (positions - partner - flow_field)
        gradient = (
            STIFFNESS * positions + error - later(error * near, 1, 1) - later(error * far, 2, 1)
        )
        positions = positions - RELAXATION * gradient / diag
    return positions


def body(images, skipped, patch_mask):
    index = lax.axis_index("sec")
    own_distance = jnp.where(index >= 2, 1 + skipped, 1)
    if lax.axis_size("sub") == 2 and lax.axis_size("tile") == 2:
        own_pad = extended_pairs(images, RIM)[0]
    else:
        own_pad = extended(images, (("sub", 1), ("tile", 2)), RIM)[0]
    skip_next = shifted(skipped, "sec", -1)
    use_own = (index == 0).astype(jnp.int32)
    rows_count = (own_pad.shape[0] - (PATCH - STRIDE)) // STRIDE
    chunks = max(n for n in (1, 2, 4) if rows_count % n == 0)
    per = rows_count // chunks
    cos_t, sin_t = dft_tables(PATCH)
    inverse_t = jnp.concatenate(
        [jnp.concatenate([cos_t, sin_t], axis=1), jnp.concatenate([-sin_t, cos_t], axis=1)], axis=0
    )
    tables = (jnp.concatenate([cos_t, sin_t], axis=0), cos_t, sin_t, inverse_t)
    skip_flat = skipped.reshape(-1)
    skip_next_flat = skip_next.reshape(-1)
    firsts, seconds = [], []
    for c in range(chunks):
        start = c * per * STRIDE
        own_c = own_pad[start : start + per * STRIDE + PATCH - STRIDE]
        prev_c = shifted(own_c, "sec", 1)
        next_c = shifted(own_c, "sec", -1)
        first_c, second_c = pair_flows(
            own_c, prev_c, next_c, skip_flat, skip_next_flat, use_own, c * per, tables
        )
        firsts.append(first_c)
        seconds.append(second_c)
    first = jnp.concatenate(firsts, axis=1)
    second = jnp.concatenate(seconds, axis=1)
    first = jnp.where(skipped[0] == 0, first, 0.0)
    second = jnp.where(skip_next[0] == 1, second, 0.0)
    weight = patch_mask.astype(jnp.float32) * (index >= 1).astype(jnp.float32)
    stacked = jnp.concatenate(
        [first, second, weight, own_distance.astype(jnp.float32)], axis=0
    )
    every = jnp.moveaxis(gather_sections(stacked, "sec"), 0, 1)
    raw_all = every[0:2] + earlier(every[2:4], 1, 1)
    flow_all = raw_all * every[4]
    positions_all = relax(flow_all, every[4], every[5])
    flow_field = lax.dynamic_slice_in_dim(flow_all, index, 1, 1)
    positions = lax.dynamic_slice_in_dim(positions_all, index, 1, 1)
    return (flow_field, positions)


def solution(mesh):
    placed = (
        P(("groups", "sec"), "sub", "tile"),
        P(("groups", "sec"), "sub", "tile"),
        P(("groups", "sec"), "sub", "tile"),
    )
    return jax.shard_map(
        body,
        mesh=mesh,
        in_specs=placed,
        out_specs=(
            P(None, ("groups", "sec"), "sub", "tile"),
            P(None, ("groups", "sec"), "sub", "tile"),
        ),
        check_vma=False,
    )
```

```python
import functools
import math

import jax
import jax.numpy as jnp
from jax import lax
from jax.experimental import pallas as pl
from jax.experimental.pallas import tpu as pltpu
from jax.sharding import PartitionSpec as P

PATCH = 160
STRIDE = 128
RELAX = 6
RIM = 16


SHARPNESS = 48.0
STIFFNESS = 0.25
RELAXATION = 0.8
EPSILON = 1e-05


def shifted(value, axis, steps):
    count = lax.axis_size(axis)
    first, last = (max(0, -steps), min(count, count - steps))
    return lax.ppermute(value, axis, [(source, source + steps) for source in range(first, last)])


def _strip_send(strip, dim):
    return jnp.swapaxes(strip, 1, 2) if dim == 2 else strip


def _strip_recv(strip, dim):
    return jnp.swapaxes(strip, 1, 2) if dim == 2 else strip


def extended(block, sides, width):
    for axis, dim in sides:
        count = lax.axis_size(axis)
        top = lax.slice_in_dim(block, 0, width, axis=dim)
        bottom = lax.slice_in_dim(block, block.shape[dim] - width, None, axis=dim)
        if count == 2:
            index = lax.axis_index(axis)
            send = _strip_send(jnp.where(index == 0, bottom, top), dim)
            got = _strip_recv(lax.ppermute(send, axis, [(0, 1), (1, 0)]), dim)
            low = jnp.where(index == 1, got, jnp.zeros_like(got))
            high = jnp.where(index == 0, got, jnp.zeros_like(got))
        else:
            forward = [(i, i + 1) for i in range(count - 1)]
            backward = [(target, source) for source, target in forward]
            low = _strip_recv(lax.ppermute(_strip_send(bottom, dim), axis, forward), dim)
            high = _strip_recv(lax.ppermute(_strip_send(top, dim), axis, backward), dim)
        block = jnp.concatenate([low, block, high], axis=dim)
    return block


def extended_pairs(block, width):
    sub = lax.axis_index("sub")
    tile = lax.axis_index("tile")
    swap = [(0, 1), (1, 0)]
    rows_send = jnp.where(
        sub == 0, block[:, -width:, :], block[:, :width, :]
    )
    cols_send = jnp.swapaxes(jnp.where(tile == 0, block[:, :, -width:], block[:, :, :width]), 1, 2)
    corner_rows = jnp.where(sub == 0, block[:, -width:, :], block[:, :width, :])
    corner_send = jnp.where(tile == 0, corner_rows[:, :, -width:], corner_rows[:, :, :width])
    rows_got = lax.ppermute(rows_send, "sub", swap)
    cols_got = jnp.swapaxes(lax.ppermute(cols_send, "tile", swap), 1, 2)
    corner_got = lax.ppermute(corner_send, ("tile", "sub"), [(0, 3), (3, 0), (1, 2), (2, 1)])

    def keep(flag, value):
        return jnp.where(flag, value, jnp.zeros_like(value))

    top, bottom = sub == 1, sub == 0
    left, right = tile == 1, tile == 0
    middle = jnp.concatenate([keep(left, cols_got), block, keep(right, cols_got)], axis=2)
    upper = jnp.concatenate(
        [keep(top & left, corner_got), keep(top, rows_got), keep(top & right, corner_got)], axis=2
    )
    lower = jnp.concatenate(
        [keep(bottom & left, corner_got), keep(bottom, rows_got), keep(bottom & right, corner_got)],
        axis=2,
    )
    return jnp.concatenate([upper, middle, lower], axis=1)


def dft_tables(patch):
    index = jnp.arange(patch, dtype=jnp.int32)
    product = index[:, None] * index[None, :] % patch
    angle = product.astype(jnp.float32) * (2.0 * math.pi / patch)
    return (jnp.cos(angle).astype(jnp.bfloat16), (-jnp.sin(angle)).astype(jnp.bfloat16))


def _sum_all(x):
    return jnp.sum(jnp.sum(x, axis=1, keepdims=True), axis=0, keepdims=True)


def _flow_kernel(
    skip_ref, skip_next_ref, flag_ref, own_ref, prev_ref, next_ref, cs_ref, c_ref, s_ref, inv_ref,
    out_ref, half_ref, x_ref, y_ref, br_ref, bi_ref,
    *, cols, row0, count,
):
    f32, bf16 = jnp.float32, jnp.bfloat16
    p = PATCH
    pairs = cols // 2
    cos_t = c_ref[...]
    sin_t = s_ref[...]
    both_t = cs_ref[...]
    inverse_t = inv_ref[...]
    size = float(p * p)

    def window(ref, j):
        return ref[r0 : r0 + p, j * STRIDE : j * STRIDE + p]

    use_own = flag_ref[0] == 1
    blocks = []
    for row in range(count):
        i = row0 + count * pl.program_id(0) + row
        r0 = row * STRIDE
        blocks.extend(_row_blocks(skip_ref, skip_next_ref, own_ref, prev_ref, next_ref, use_own, i, r0, cols))
    _rest(blocks, half_ref, x_ref, y_ref, br_ref, bi_ref, out_ref, cos_t, sin_t, both_t, inverse_t, cols * count, count, cols)


def _row_blocks(skip_ref, skip_next_ref, own_ref, prev_ref, next_ref, use_own, i, r0, cols):
    p = PATCH
    pairs = cols // 2

    def window(ref, j):
        return ref[r0 : r0 + p, j * STRIDE : j * STRIDE + p]

    blocks = []
    for k in range(pairs):
        left, right = 2 * k, 2 * k + 1
        first_near = skip_ref[i * cols + left] == 0
        blocks.append(jnp.where(first_near, window(own_ref, left), window(own_ref, right)))
        blocks.append(jnp.where(first_near, window(prev_ref, left), window(prev_ref, right)))
    for k in range(pairs):
        left, right = 2 * k, 2 * k + 1
        second_far = skip_next_ref[i * cols + right] == 1
        blocks.append(jnp.where(second_far, window(next_ref, right), window(next_ref, left)))
        col_prev = jnp.where(second_far, window(prev_ref, right), window(prev_ref, left))
        col_own = jnp.where(second_far, window(own_ref, right), window(own_ref, left))
        blocks.append(jnp.where(use_own, col_own, col_prev))
    return blocks


def _rest(blocks, half_ref, x_ref, y_ref, br_ref, bi_ref, out_ref, cos_t, sin_t, both_t, inverse_t, total_pairs, count, row_cols):
    f32, bf16 = jnp.float32, jnp.bfloat16
    p = PATCH
    size = float(p * p)
    cols = total_pairs
    for t, blk in enumerate(blocks):
        x = blk.astype(f32)
        centered = x - _sum_all(x) / size
        spread = _sum_all(centered * centered) / size
        normed = (centered * lax.rsqrt(spread + EPSILON)).astype(bf16)
        half_ref[2 * p * t : 2 * p * (t + 1), :] = jnp.dot(
            both_t, normed, preferred_element_type=f32
        ).astype(bf16)
    halves = half_ref[...]
    x_ref[...] = jnp.dot(halves, cos_t, preferred_element_type=f32)
    y_ref[...] = jnp.dot(halves, sin_t, preferred_element_type=f32)

    def spectrum(t):
        base = 2 * p * t
        re = x_ref[base : base + p, :] - y_ref[base + p : base + 2 * p, :]
        im = y_ref[base : base + p, :] + x_ref[base + p : base + 2 * p, :]
        return re, im

    for c in range(cols):
        o_re, o_im = spectrum(2 * c)
        t_re, t_im = spectrum(2 * c + 1)
        c_re = (o_re * t_re + o_im * t_im).astype(bf16)
        c_im = (o_re * t_im - o_im * t_re).astype(bf16)
        back = jnp.dot(
            inverse_t, jnp.concatenate([c_re, c_im], axis=0), preferred_element_type=f32
        ).astype(bf16)
        br_ref[p * c : p * (c + 1), :] = back[:p]
        bi_ref[p * c : p * (c + 1), :] = back[p:]

    corr = (
        jnp.dot(br_ref[...], cos_t, preferred_element_type=f32)
        + jnp.dot(bi_ref[...], sin_t, preferred_element_type=f32)
    ) / float(p) ** 4
    w = jnp.exp(SHARPNESS * corr)
    u_col = lax.broadcasted_iota(jnp.int32, (cols * p, 1), 0) % p
    off_col = jnp.where(u_col < p // 2, u_col, u_col - p).astype(f32)
    u_row = lax.broadcasted_iota(jnp.int32, (1, p), 1)
    off_row = jnp.where(u_row < p // 2, u_row, u_row - p).astype(f32)
    rows_sum = jnp.sum(w, axis=1, keepdims=True)
    total = jnp.sum(rows_sum.reshape(cols, p, 1), axis=1)
    along_rows = jnp.sum((rows_sum * off_col).reshape(cols, p, 1), axis=1)
    cols_sum = jnp.sum(w.reshape(cols, p, p), axis=1)
    along_cols = jnp.sum(cols_sum * off_row, axis=1, keepdims=True)
    ar = along_rows / total / float(RIM)
    ac = along_cols / total / float(RIM)
    lane = lax.broadcasted_iota(jnp.int32, (cols, 128), 1)
    res = jnp.where(lane == 0, ar, jnp.where(lane == 1, ac, 0.0))
    height = out_ref.shape[1]
    for row in range(count):
        part = res[row * row_cols : (row + 1) * row_cols]
        if height > row_cols:
            part = jnp.concatenate([part, jnp.zeros((height - row_cols, 128), f32)], axis=0)
        out_ref[row] = part


def pair_flows(own_pad, prev_pad, next_pad, skip_flat, skip_next_flat, use_own, row0, tables):
    tall, broad = own_pad.shape
    rows = (tall - (PATCH - STRIDE)) // STRIDE
    cols = (broad - (PATCH - STRIDE)) // STRIDE
    assert cols % 2 == 0
    height = max(8, -(-cols // 8) * 8)
    both_t, cos_t, sin_t, inverse_t = tables
    step = 2 if rows % 2 == 0 and rows >= 4 else 1
    band = pl.BlockSpec(
        (pl.Element(step * STRIDE + PATCH - STRIDE), pl.Element(broad)),
        lambda i, *_: (i * step * STRIDE, 0),
    )
    table = pl.BlockSpec((PATCH, PATCH), lambda i, *_: (0, 0))
    grid_spec = pltpu.PrefetchScalarGridSpec(
        num_scalar_prefetch=3,
        grid=(rows // step,),
        in_specs=[
            band, band, band, pl.BlockSpec((2 * PATCH, PATCH), lambda i, *_: (0, 0)), table, table,
            pl.BlockSpec((2 * PATCH, 2 * PATCH), lambda i, *_: (0, 0)),
        ],
        out_specs=pl.BlockSpec((step, height, 128), lambda i, *_: (i, 0, 0)),
        scratch_shapes=[
            pltpu.VMEM((4 * step * cols * PATCH, PATCH), jnp.bfloat16),
            pltpu.VMEM((4 * step * cols * PATCH, PATCH), jnp.float32),
            pltpu.VMEM((4 * step * cols * PATCH, PATCH), jnp.float32),
            pltpu.VMEM((step * cols * PATCH, PATCH), jnp.bfloat16),
            pltpu.VMEM((step * cols * PATCH, PATCH), jnp.bfloat16),
        ],
    )
    out = pl.pallas_call(
        functools.partial(_flow_kernel, cols=cols, row0=row0, count=step),
        grid_spec=grid_spec,
        out_shape=jax.ShapeDtypeStruct((rows, height, 128), jnp.float32),
        compiler_params=pltpu.CompilerParams(
            dimension_semantics=("arbitrary",), vmem_limit_bytes=48 * 1024 * 1024
        ),
    )(skip_flat, skip_next_flat, use_own.reshape(1), own_pad, prev_pad, next_pad, both_t, cos_t, sin_t, inverse_t)
    half = cols // 2
    first = jnp.repeat(jnp.transpose(out[:, :half, 0:2], (2, 0, 1)), 2, axis=2)
    second = jnp.repeat(jnp.transpose(out[:, half:cols, 0:2], (2, 0, 1)), 2, axis=2)
    return first, second


def gather_sections(value, axis):
    count = lax.axis_size(axis)
    spread = jnp.broadcast_to(value[None], (count,) + value.shape)
    return lax.all_to_all(spread, axis, 0, 0, tiled=True)


def earlier(values, steps, axis):
    width = values.shape[axis]
    widths = [(0, 0)] * values.ndim
    widths[axis] = (steps, 0)
    return lax.slice_in_dim(jnp.pad(values, widths), 0, width, axis=axis)


def later(values, steps, axis):
    width = values.shape[axis]
    widths = [(0, 0)] * values.ndim
    widths[axis] = (0, steps)
    return lax.slice_in_dim(jnp.pad(values, widths), steps, steps + width, axis=axis)


def relax(flow_field, weight, distance):
    near = (distance == 1).astype(jnp.float32)
    far = 1.0 - near
    diag = STIFFNESS + weight + later(weight * near, 1, 0) + later(weight * far, 2, 0)
    positions = jnp.zeros_like(flow_field)
    for sweep in range(RELAX):
        partner = near * earlier(positions, 1, 1) + far * earlier(positions, 2, 1)
        error = weight * (positions - partner - flow_field)
        gradient = (
            STIFFNESS * positions + error - later(error * near, 1, 1) - later(error * far, 2, 1)
        )
        positions = positions - RELAXATION * gradient / diag
    return positions


def body(images, skipped, patch_mask):
    index = lax.axis_index("sec")
    own_distance = jnp.where(index >= 2, 1 + skipped, 1)
    if lax.axis_size("sub") == 2 and lax.axis_size("tile") == 2:
        own_pad = extended_pairs(images, RIM)[0]
    else:
        own_pad = extended(images, (("sub", 1), ("tile", 2)), RIM)[0]
    skip_next = shifted(skipped, "sec", -1)
    use_own = (index == 0).astype(jnp.int32)
    rows_count = (own_pad.shape[0] - (PATCH - STRIDE)) // STRIDE
    if rows_count == 8:
        sizes = [2, 2, 4]
    else:
        sizes = [rows_count]
    offsets = [sum(sizes[:n]) for n in range(len(sizes))]
    cos_t, sin_t = dft_tables(PATCH)
    inverse_t = jnp.concatenate(
        [jnp.concatenate([cos_t, sin_t], axis=1), jnp.concatenate([-sin_t, cos_t], axis=1)], axis=0
    )
    tables = (jnp.concatenate([cos_t, sin_t], axis=0), cos_t, sin_t, inverse_t)
    skip_flat = skipped.reshape(-1)
    skip_next_flat = skip_next.reshape(-1)
    firsts, seconds = [], []
    for first_row, count in zip(offsets, sizes):
        start = first_row * STRIDE
        own_c = own_pad[start : start + count * STRIDE + PATCH - STRIDE]
        prev_c = shifted(own_c, "sec", 1)
        next_c = shifted(own_c, "sec", -1)
        first_c, second_c = pair_flows(
            own_c, prev_c, next_c, skip_flat, skip_next_flat, use_own, first_row, tables
        )
        firsts.append(first_c)
        seconds.append(second_c)
    first = jnp.concatenate(firsts, axis=1)
    second = jnp.concatenate(seconds, axis=1)
    first = jnp.where(skipped[0] == 0, first, 0.0)
    second = jnp.where(skip_next[0] == 1, second, 0.0)
    weight = patch_mask.astype(jnp.float32) * (index >= 1).astype(jnp.float32)
    stacked = jnp.concatenate(
        [first, second, weight, own_distance.astype(jnp.float32)], axis=0
    )
    every = jnp.moveaxis(gather_sections(stacked, "sec"), 0, 1)
    raw_all = every[0:2] + earlier(every[2:4], 1, 1)
    flow_all = raw_all * every[4]
    positions_all = relax(flow_all, every[4], every[5])
    flow_field = lax.dynamic_slice_in_dim(flow_all, index, 1, 1)
    positions = lax.dynamic_slice_in_dim(positions_all, index, 1, 1)
    return (flow_field, positions)


def solution(mesh):
    placed = (
        P(("groups", "sec"), "sub", "tile"),
        P(("groups", "sec"), "sub", "tile"),
        P(("groups", "sec"), "sub", "tile"),
    )
    return jax.shard_map(
        body,
        mesh=mesh,
        in_specs=placed,
        out_specs=(
            P(None, ("groups", "sec"), "sub", "tile"),
            P(None, ("groups", "sec"), "sub", "tile"),
        ),
        check_vma=False,
    )
```

```python
import functools
import math

import jax
import jax.numpy as jnp
from jax import lax
from jax.experimental import pallas as pl
from jax.experimental.pallas import tpu as pltpu
from jax.sharding import PartitionSpec as P

PATCH = 160
STRIDE = 128
RELAX = 6
RIM = 16


SHARPNESS = 48.0
STIFFNESS = 0.25
RELAXATION = 0.8
EPSILON = 1e-05


def shifted(value, axis, steps):
    count = lax.axis_size(axis)
    first, last = (max(0, -steps), min(count, count - steps))
    return lax.ppermute(value, axis, [(source, source + steps) for source in range(first, last)])


def _strip_send(strip, dim):
    return jnp.swapaxes(strip, 1, 2) if dim == 2 else strip


def _strip_recv(strip, dim):
    return jnp.swapaxes(strip, 1, 2) if dim == 2 else strip


def extended(block, sides, width):
    for axis, dim in sides:
        count = lax.axis_size(axis)
        top = lax.slice_in_dim(block, 0, width, axis=dim)
        bottom = lax.slice_in_dim(block, block.shape[dim] - width, None, axis=dim)
        if count == 2:
            index = lax.axis_index(axis)
            send = _strip_send(jnp.where(index == 0, bottom, top), dim)
            got = _strip_recv(lax.ppermute(send, axis, [(0, 1), (1, 0)]), dim)
            low = jnp.where(index == 1, got, jnp.zeros_like(got))
            high = jnp.where(index == 0, got, jnp.zeros_like(got))
        else:
            forward = [(i, i + 1) for i in range(count - 1)]
            backward = [(target, source) for source, target in forward]
            low = _strip_recv(lax.ppermute(_strip_send(bottom, dim), axis, forward), dim)
            high = _strip_recv(lax.ppermute(_strip_send(top, dim), axis, backward), dim)
        block = jnp.concatenate([low, block, high], axis=dim)
    return block


def extended_pairs(block, width):
    sub = lax.axis_index("sub")
    tile = lax.axis_index("tile")
    swap = [(0, 1), (1, 0)]
    rows_send = jnp.where(
        sub == 0, block[:, -width:, :], block[:, :width, :]
    )
    cols_send = jnp.swapaxes(jnp.where(tile == 0, block[:, :, -width:], block[:, :, :width]), 1, 2)
    corner_rows = jnp.where(sub == 0, block[:, -width:, :], block[:, :width, :])
    corner_send = jnp.where(tile == 0, corner_rows[:, :, -width:], corner_rows[:, :, :width])
    rows_got = lax.ppermute(rows_send, "sub", swap)
    cols_got = jnp.swapaxes(lax.ppermute(cols_send, "tile", swap), 1, 2)
    corner_got = lax.ppermute(corner_send, ("tile", "sub"), [(0, 3), (3, 0), (1, 2), (2, 1)])

    def keep(flag, value):
        return jnp.where(flag, value, jnp.zeros_like(value))

    top, bottom = sub == 1, sub == 0
    left, right = tile == 1, tile == 0
    middle = jnp.concatenate([keep(left, cols_got), block, keep(right, cols_got)], axis=2)
    upper = jnp.concatenate(
        [keep(top & left, corner_got), keep(top, rows_got), keep(top & right, corner_got)], axis=2
    )
    lower = jnp.concatenate(
        [keep(bottom & left, corner_got), keep(bottom, rows_got), keep(bottom & right, corner_got)],
        axis=2,
    )
    return jnp.concatenate([upper, middle, lower], axis=1)


def dft_tables(patch):
    index = jnp.arange(patch, dtype=jnp.int32)
    product = index[:, None] * index[None, :] % patch
    angle = product.astype(jnp.float32) * (2.0 * math.pi / patch)
    return (jnp.cos(angle).astype(jnp.bfloat16), (-jnp.sin(angle)).astype(jnp.bfloat16))


def _sum_all(x):
    return jnp.sum(jnp.sum(x, axis=1, keepdims=True), axis=0, keepdims=True)


def _flow_kernel(
    skip_ref, skip_next_ref, flag_ref, own_ref, prev_ref, next_ref, cs_ref, c_ref, s_ref, inv_ref,
    out_ref, half_ref, x_ref, y_ref, br_ref, bi_ref,
    *, cols, row0,
):
    f32, bf16 = jnp.float32, jnp.bfloat16
    p = PATCH
    pairs = cols // 2
    i = pl.program_id(0) + row0
    cos_t = c_ref[...]
    sin_t = s_ref[...]
    both_t = cs_ref[...]
    inverse_t = inv_ref[...]
    size = float(p * p)

    def window(ref, j):
        return ref[:, j * STRIDE : j * STRIDE + p]

    use_own = flag_ref[0] == 1
    blocks = []
    for k in range(pairs):
        left, right = 2 * k, 2 * k + 1
        first_near = skip_ref[i * cols + left] == 0
        blocks.append(jnp.where(first_near, window(own_ref, left), window(own_ref, right)))
        blocks.append(jnp.where(first_near, window(prev_ref, left), window(prev_ref, right)))
    for k in range(pairs):
        left, right = 2 * k, 2 * k + 1
        second_far = skip_next_ref[i * cols + right] == 1
        blocks.append(jnp.where(second_far, window(next_ref, right), window(next_ref, left)))
        col_prev = jnp.where(second_far, window(prev_ref, right), window(prev_ref, left))
        col_own = jnp.where(second_far, window(own_ref, right), window(own_ref, left))
        blocks.append(jnp.where(use_own, col_own, col_prev))

    for t, blk in enumerate(blocks):
        x = blk.astype(f32)
        centered = x - _sum_all(x) / size
        spread = _sum_all(centered * centered) / size
        normed = (centered * lax.rsqrt(spread + EPSILON)).astype(bf16)
        half_ref[2 * p * t : 2 * p * (t + 1), :] = jnp.dot(
            both_t, normed, preferred_element_type=f32
        ).astype(bf16)
    halves = half_ref[...]
    x_ref[...] = jnp.dot(halves, cos_t, preferred_element_type=f32)
    y_ref[...] = jnp.dot(halves, sin_t, preferred_element_type=f32)

    def spectrum(t):
        base = 2 * p * t
        re = x_ref[base : base + p, :] - y_ref[base + p : base + 2 * p, :]
        im = y_ref[base : base + p, :] + x_ref[base + p : base + 2 * p, :]
        return re, im

    for c in range(cols):
        o_re, o_im = spectrum(2 * c)
        t_re, t_im = spectrum(2 * c + 1)
        c_re = (o_re * t_re + o_im * t_im).astype(bf16)
        c_im = (o_re * t_im - o_im * t_re).astype(bf16)
        back = jnp.dot(
            inverse_t, jnp.concatenate([c_re, c_im], axis=0), preferred_element_type=f32
        ).astype(bf16)
        br_ref[p * c : p * (c + 1), :] = back[:p]
        bi_ref[p * c : p * (c + 1), :] = back[p:]

    corr = (
        jnp.dot(br_ref[...], cos_t, preferred_element_type=f32)
        + jnp.dot(bi_ref[...], sin_t, preferred_element_type=f32)
    ) / float(p) ** 4
    w = jnp.exp(SHARPNESS * corr)
    u_col = lax.broadcasted_iota(jnp.int32, (cols * p, 1), 0) % p
    off_col = jnp.where(u_col < p // 2, u_col, u_col - p).astype(f32)
    u_row = lax.broadcasted_iota(jnp.int32, (1, p), 1)
    off_row = jnp.where(u_row < p // 2, u_row, u_row - p).astype(f32)
    rows_sum = jnp.sum(w, axis=1, keepdims=True)
    total = jnp.sum(rows_sum.reshape(cols, p, 1), axis=1)
    along_rows = jnp.sum((rows_sum * off_col).reshape(cols, p, 1), axis=1)
    cols_sum = jnp.sum(w.reshape(cols, p, p), axis=1)
    along_cols = jnp.sum(cols_sum * off_row, axis=1, keepdims=True)
    ar = along_rows / total / float(RIM)
    ac = along_cols / total / float(RIM)
    lane = lax.broadcasted_iota(jnp.int32, (cols, 128), 1)
    res = jnp.where(lane == 0, ar, jnp.where(lane == 1, ac, 0.0))
    height = out_ref.shape[1]
    if height > cols:
        res = jnp.concatenate([res, jnp.zeros((height - cols, 128), f32)], axis=0)
    out_ref[0] = res


def pair_flows(own_pad, prev_pad, next_pad, skip_flat, skip_next_flat, use_own, row0, tables):
    tall, broad = own_pad.shape
    rows = (tall - (PATCH - STRIDE)) // STRIDE
    cols = (broad - (PATCH - STRIDE)) // STRIDE
    assert cols % 2 == 0
    height = max(8, -(-cols // 8) * 8)
    both_t, cos_t, sin_t, inverse_t = tables
    band = pl.BlockSpec((pl.Element(PATCH), pl.Element(broad)), lambda i, *_: (i * STRIDE, 0))
    table = pl.BlockSpec((PATCH, PATCH), lambda i, *_: (0, 0))
    grid_spec = pltpu.PrefetchScalarGridSpec(
        num_scalar_prefetch=3,
        grid=(rows,),
        in_specs=[
            band, band, band, pl.BlockSpec((2 * PATCH, PATCH), lambda i, *_: (0, 0)), table, table,
            pl.BlockSpec((2 * PATCH, 2 * PATCH), lambda i, *_: (0, 0)),
        ],
        out_specs=pl.BlockSpec((1, height, 128), lambda i, *_: (i, 0, 0)),
        scratch_shapes=[
            pltpu.VMEM((4 * cols * PATCH, PATCH), jnp.bfloat16),
            pltpu.VMEM((4 * cols * PATCH, PATCH), jnp.float32),
            pltpu.VMEM((4 * cols * PATCH, PATCH), jnp.float32),
            pltpu.VMEM((cols * PATCH, PATCH), jnp.bfloat16),
            pltpu.VMEM((cols * PATCH, PATCH), jnp.bfloat16),
        ],
    )
    out = pl.pallas_call(
        functools.partial(_flow_kernel, cols=cols, row0=row0),
        grid_spec=grid_spec,
        out_shape=jax.ShapeDtypeStruct((rows, height, 128), jnp.float32),
        compiler_params=pltpu.CompilerParams(
            dimension_semantics=("arbitrary",), vmem_limit_bytes=48 * 1024 * 1024
        ),
    )(skip_flat, skip_next_flat, use_own.reshape(1), own_pad, prev_pad, next_pad, both_t, cos_t, sin_t, inverse_t)
    half = cols // 2
    first = jnp.repeat(jnp.transpose(out[:, :half, 0:2], (2, 0, 1)), 2, axis=2)
    second = jnp.repeat(jnp.transpose(out[:, half:cols, 0:2], (2, 0, 1)), 2, axis=2)
    return first, second


def gather_sections(value, axis):
    count = lax.axis_size(axis)
    spread = jnp.broadcast_to(value[None], (count,) + value.shape)
    return lax.all_to_all(spread, axis, 0, 0, tiled=True)


def earlier(values, steps, axis):
    width = values.shape[axis]
    widths = [(0, 0)] * values.ndim
    widths[axis] = (steps, 0)
    return lax.slice_in_dim(jnp.pad(values, widths), 0, width, axis=axis)


def later(values, steps, axis):
    width = values.shape[axis]
    widths = [(0, 0)] * values.ndim
    widths[axis] = (0, steps)
    return lax.slice_in_dim(jnp.pad(values, widths), steps, steps + width, axis=axis)


def relax(flow_field, weight, distance):
    near = (distance == 1).astype(jnp.float32)
    far = 1.0 - near
    diag = STIFFNESS + weight + later(weight * near, 1, 0) + later(weight * far, 2, 0)
    positions = jnp.zeros_like(flow_field)
    for sweep in range(RELAX):
        partner = near * earlier(positions, 1, 1) + far * earlier(positions, 2, 1)
        error = weight * (positions - partner - flow_field)
        gradient = (
            STIFFNESS * positions + error - later(error * near, 1, 1) - later(error * far, 2, 1)
        )
        positions = positions - RELAXATION * gradient / diag
    return positions


def body(images, skipped, patch_mask):
    index = lax.axis_index("sec")
    own_distance = jnp.where(index >= 2, 1 + skipped, 1)
    if lax.axis_size("sub") == 2 and lax.axis_size("tile") == 2:
        own_pad = extended_pairs(images, RIM)[0]
    else:
        own_pad = extended(images, (("sub", 1), ("tile", 2)), RIM)[0]
    use_own = (index == 0).astype(jnp.int32)
    rows_count = (own_pad.shape[0] - (PATCH - STRIDE)) // STRIDE
    chunks = max(n for n in (1, 2, 4) if rows_count % n == 0)
    per = rows_count // chunks
    cos_t, sin_t = dft_tables(PATCH)
    inverse_t = jnp.concatenate(
        [jnp.concatenate([cos_t, sin_t], axis=1), jnp.concatenate([-sin_t, cos_t], axis=1)], axis=0
    )
    tables = (jnp.concatenate([cos_t, sin_t], axis=0), cos_t, sin_t, inverse_t)
    skip_flat = skipped.reshape(-1)
    firsts, seconds = [], []
    for c in range(chunks):
        start = c * per * STRIDE
        own_c = own_pad[start : start + per * STRIDE + PATCH - STRIDE]
        prev_c = shifted(own_c, "sec", 1)
        next_c = shifted(own_c, "sec", -1)
        if c == 0:
            skip_next = shifted(lax.optimization_barrier((skipped, own_c))[0], "sec", -1)
            skip_next_flat = skip_next.reshape(-1)
        first_c, second_c = pair_flows(
            own_c, prev_c, next_c, skip_flat, skip_next_flat, use_own, c * per, tables
        )
        firsts.append(first_c)
        seconds.append(second_c)
    first = jnp.concatenate(firsts, axis=1)
    second = jnp.concatenate(seconds, axis=1)
    first = jnp.where(skipped[0] == 0, first, 0.0)
    second = jnp.where(skip_next[0] == 1, second, 0.0)
    weight = patch_mask.astype(jnp.float32) * (index >= 1).astype(jnp.float32)
    stacked = jnp.concatenate(
        [first, second, weight, own_distance.astype(jnp.float32)], axis=0
    )
    every = jnp.moveaxis(gather_sections(stacked, "sec"), 0, 1)
    raw_all = every[0:2] + earlier(every[2:4], 1, 1)
    flow_all = raw_all * every[4]
    positions_all = relax(flow_all, every[4], every[5])
    flow_field = lax.dynamic_slice_in_dim(flow_all, index, 1, 1)
    positions = lax.dynamic_slice_in_dim(positions_all, index, 1, 1)
    return (flow_field, positions)


def solution(mesh):
    placed = (
        P(("groups", "sec"), "sub", "tile"),
        P(("groups", "sec"), "sub", "tile"),
        P(("groups", "sec"), "sub", "tile"),
    )
    return jax.shard_map(
        body,
        mesh=mesh,
        in_specs=placed,
        out_specs=(
            P(None, ("groups", "sec"), "sub", "tile"),
            P(None, ("groups", "sec"), "sub", "tile"),
        ),
        check_vma=False,
    )
```
